32 devices in a mesh: groups: 2 (over y), dp: 4 (over z), mp: 4 (over x, core).
Axes of the slice: x: 2, y: 2, z: 4, core: 2. Of those that a mesh axis runs over, the one named last changes fastest.
Arguments:
- latents: bfloat16 [256, 640, 64], P(('groups', 'dp'), 'mp'), parts along dimension 0
- modulation: bfloat16 [256, 2, 640], P(('groups', 'dp'), None, 'mp'), parts along dimension 0, may hold values from -3 to 3
- first_kernel: bfloat16 [640, 9, 640], P('dp', None, 'mp'), may hold values from -0.078125 to 0.078125
- second_kernel: bfloat16 [640, 9, 640], P('dp', None, 'mp'), may hold values from -0.078125 to 0.078125
- encoder_cache: bfloat16 [336, 1280, 128], P(('groups', 'dp'), 'mp'), parts along dimension 0
- query_weight: bfloat16 [640, 640], P('dp'), may hold values from -0.25 to 0.25
- output_weight: bfloat16 [640, 640], P('dp'), may hold values from -0.25 to 0.25
- kept_prompt_list: int32 [256], P('groups'), parts along dimension 0, may hold values from 0 to 167, as said below
- destination: int32 [256], P('groups'), parts along dimension 0, may hold values from 0 to 3, as said below
- lengths: int32 [336], P('groups'), parts along dimension 0, may hold values from 1 to 128, 10752 in all
Outputs:
- level_out: bfloat16 [256, 640, 64], P(('groups', 'dp'), 'mp'), parts along dimension 0
The draws below stay inside these ranges and needn't reach their ends.
There are 2 independent parts, one for each index of `groups`. The reference program is written for one: setup_inputs(seed, part) draws one part's arguments, and reference() takes and returns one part's arrays. A program takes and returns all parts, laid end to end along the dimension named above; an argument that names none is the same for every part. Nothing has to cross between parts.
Inputs may be any that keep to these rules, and one draw needn't show every extreme that they name: `kept_prompt_list`: entries o * 32 to o * 32 + 31 belong to owner o: distinct ids of its prompts o * 42 to o * 42 + 41. `destination`: names the shard of each survivor; every shard receives exactly 32 survivors, one owner sends at most 16 survivors to one shard, and every owner sends exactly 16 to some shard.
All inputs are finite; a program needn't handle non-finite values.
Results may differ from the reference program's by a relative error of at most 0.0055.
Values may be sent and summed in bfloat16 or wider, within the bound.
No kernel may reach another device: no remote copies, remote signals or barrier semaphores. Data moves between devices by JAX's collectives and lax.ppermute only.
A program may use at most 64 MiB of HBM per device.

```python
import math
import jax
import jax.numpy as jnp
import numpy as np
from jax import lax

C = 640
GROUPS = 32
HEAD = 64
SIDE = 8
L = 128
S_DEV = 32
P_DEV = 42
HEADS = 10
SHARDS = 4
SAMPLES = 128
PROMPTS = 168


def draw_latents(key, part):
    sub_keys = jax.random.split(jax.random.fold_in(key, 37), 3)
    full_shape = (SAMPLES, C, SIDE * SIDE)
    cell_scale = jnp.exp(jax.random.uniform(sub_keys[0], (SAMPLES, 1, SIDE * SIDE), minval=-1.15, maxval=1.15))
    channel_scale = jnp.exp(jax.random.uniform(sub_keys[1], (SAMPLES, C, 1), minval=-1.15, maxval=1.15))
    return (jax.random.normal(sub_keys[2], full_shape) * cell_scale * channel_scale).astype(jnp.bfloat16)


def draw_encoder_cache(key, part):
    sub_keys = jax.random.split(jax.random.fold_in(key, 41), 1)
    full_shape = (PROMPTS, 2 * C, L)
    return jax.random.normal(sub_keys[0], full_shape).astype(jnp.bfloat16)


def keep_one_owner(owner_key):
    first_key, second_key = jax.random.split(owner_key)
    middle = 1 + jax.random.permutation(first_key, P_DEV - 2)[:S_DEV - 2]
    chosen = jnp.concatenate([jnp.zeros((1,), jnp.int32), jnp.full((1,), P_DEV - 1, jnp.int32), middle.astype(jnp.int32)])
    return chosen[jax.random.permutation(second_key, S_DEV)]


def draw_kept_prompt_list(key, part):
    owner_keys = jax.random.split(jax.random.fold_in(key, 11), SHARDS)
    local_ids = jax.vmap(keep_one_owner)(owner_keys)
    owners = jnp.arange(SHARDS, dtype=jnp.int32)[:, None] * P_DEV
    return (local_ids + owners).reshape(SAMPLES).astype(jnp.int32)


def shard_order(order_key):
    return jax.random.permutation(order_key, SHARDS)


def slot_order(order_key):
    return jax.random.permutation(order_key, S_DEV)


def draw_destination(key, part):
    sub_keys = jax.random.split(jax.random.fold_in(key, 23), 5)
    base = S_DEV // SHARDS
    half = SHARDS // 2
    owner_ids = jnp.arange(SHARDS, dtype=jnp.int32)
    pairing = jax.random.permutation(sub_keys[0], SHARDS).astype(jnp.int32)
    place = jnp.zeros((SHARDS,), jnp.int32).at[pairing].set(owner_ids)
    pair_of = place // 2
    role = place % 2
    pair_orders = jax.vmap(shard_order)(jax.random.split(sub_keys[1], half)).astype(jnp.int32)
    switch_count = 1 + jax.random.randint(sub_keys[2], (half,), 0, min(3, half))
    moved = 1 + jax.random.randint(sub_keys[3], (half, half), 0, base)
    moved = jnp.where(jnp.arange(half)[None, :] == 0, base, moved)
    orders = pair_orders[pair_of]
    firsts = orders[:, 0::2]
    seconds = orders[:, 1::2]
    sources = jnp.where(role[:, None] == 0, seconds, firsts)
    targets = jnp.where(role[:, None] == 0, firsts, seconds)
    active = jnp.arange(half)[None, :] < switch_count[pair_of][:, None]
    amounts = moved[pair_of]
    hits = (sources[:, :, None] == owner_ids[None, None, :]) & active[:, :, None]
    redirected = jnp.sum(jnp.where(hits, targets[:, :, None], 0), axis=1)
    hit_amount = jnp.sum(jnp.where(hits, amounts[:, :, None], 0), axis=1)
    is_hit = jnp.any(hits, axis=1)
    slots = jnp.arange(S_DEV, dtype=jnp.int32) // base
    copies = jnp.arange(S_DEV, dtype=jnp.int32) % base
    slot_hit = is_hit[:, slots] & (copies[None, :] < hit_amount[:, slots])
    chosen = jnp.where(slot_hit, redirected[:, slots], slots[None, :])
    shuffles = jax.vmap(slot_order)(jax.random.split(sub_keys[4], SHARDS))
    shuffled = jnp.take_along_axis(chosen, shuffles, axis=1)
    return shuffled.reshape(SAMPLES).astype(jnp.int32)


def block_levels(key, dims, cuts, smallest, high):
    factor_of, own = 1.0, jax.random.fold_in(key, 6)
    for axis_at, parts in cuts:
        heights = jnp.exp(jax.random.uniform(jax.random.fold_in(own, axis_at), (parts,), jnp.float32, smallest / len(cuts), high / len(cuts)))
        factor_of = factor_of * jnp.repeat(heights, dims[axis_at] // parts).reshape([-1 if axis == axis_at else 1 for axis in range(len(dims))])
    return factor_of


def split_up(number_of, total, bound, skew):
    portions = [(1 << 20) // math.isqrt(grade ** skew) + 1 for grade in range(2, number_of + 1)]
    surplus, counts = total - bound - (number_of - 1), [1] * (number_of - 1)
    while surplus > 0:
        free = [i for i in range(number_of - 1) if counts[i] < bound]
        pool, budget = sum([portions[i] for i in free]), surplus
        for i in free:
            addition = min(bound - counts[i], max(1, budget * portions[i] // pool), surplus)
            counts[i] = counts[i] + addition
            surplus = surplus - addition
    return np.array([bound] + counts)


def ragged_sizes(rng, amount, total, limit, slope):
    if amount == 2:
        one = jax.random.randint(rng, (), max(1, total - limit), min(limit, total - 1) + 1)
        return jnp.stack([one, total - one])
    sizes = jnp.asarray(split_up(amount, total, limit, slope), jnp.int32)
    twos = (amount - 1) // 2
    donor, taker = sizes[1:1 + 2 * twos:2], sizes[2:2 + 2 * twos:2]
    slack = jnp.minimum(donor - 1, limit - taker)
    moved = jax.random.randint(jax.random.fold_in(rng, 1), (twos,), 0, 1 << 20) % (slack + 1)
    sizes = sizes.at[1:1 + 2 * twos:2].set(donor - moved).at[2:2 + 2 * twos:2].set(taker + moved)
    return sizes[jax.random.permutation(jax.random.fold_in(rng, 2), amount)]


def normal_values(key, extent, scale, limit, cuts=(), kind=jnp.bfloat16):
    values = jax.random.normal(key, extent, jnp.float32) * scale
    if len(cuts) > 0:
        values = block_levels(key, extent, cuts, -0.22, 0.18) * values
    return jnp.clip(values, min=-limit, max=limit).astype(kind)


def setup_inputs(seed: int = 0, part: int = 0) -> dict:
    key_of = jax.random.split(jax.random.key(seed), 11)
    own_keys = jax.random.split(jax.random.fold_in(key_of[10], part), 11)
    return {
        "latents": draw_latents(jax.random.fold_in(jax.random.fold_in(key_of[10], part), 71), part),
        "modulation": normal_values(own_keys[1], (SAMPLES, 2, C), 0.5, 3.0, ((0, 4), (2, 4))),
        "first_kernel": normal_values(key_of[2], (C, 9, C), (9 * C) ** -0.5, 0.078125, ((0, 4), (2, 4))),
        "second_kernel": normal_values(key_of[3], (C, 9, C), (9 * C) ** -0.5, 0.078125, ((0, 4), (2, 4))),
        "encoder_cache": draw_encoder_cache(jax.random.fold_in(jax.random.fold_in(key_of[10], part), 71), part),
        "query_weight": normal_values(key_of[5], (C, C), C ** -0.5, 0.25, ((0, 4),)),
        "output_weight": normal_values(key_of[6], (C, C), C ** -0.5, 0.25, ((0, 4),)),
        "kept_prompt_list": draw_kept_prompt_list(jax.random.fold_in(jax.random.fold_in(key_of[10], part), 71), part),
        "destination": draw_destination(jax.random.fold_in(jax.random.fold_in(key_of[10], part), 71), part),
        "lengths": ragged_sizes(own_keys[9], PROMPTS, PROMPTS * L // 2, L, 1).astype(jnp.int32),
    }


EPSILON = 1e-05
MASKED = -1e+30

def norm_groups(values, group_width):
    field_shape = values.shape
    grouped = values.reshape(field_shape[0], field_shape[1] * field_shape[2], field_shape[3] // group_width, group_width)
    center = grouped - lax.optimization_barrier(jnp.mean(grouped, axis=(1, 3), keepdims=True))
    spread = lax.optimization_barrier(jnp.mean(center * center, axis=(1, 3), keepdims=True))
    return (center * lax.rsqrt(spread + EPSILON)).reshape(field_shape)

def convolve(field, kernel):
    sample_count = field.shape[0]
    padded = jnp.pad(field, ((0, 0), (1, 1), (1, 1), (0, 0)))
    running = jnp.zeros((sample_count * SIDE * SIDE, kernel.shape[2]), jnp.float32)
    for offset in range(9):
        row_shift, col_shift = (offset // 3, offset % 3)
        window = padded[:, row_shift:row_shift + SIDE, col_shift:col_shift + SIDE, :].reshape(sample_count * SIDE * SIDE, C)
        running = running + jnp.dot(window, kernel[:, offset, :], preferred_element_type=jnp.float32)
    return running.reshape(sample_count, SIDE, SIDE, kernel.shape[2])

def reference(latents, modulation, first_kernel, second_kernel, encoder_cache, query_weight, output_weight, kept_prompt_list, destination, lengths):
    group_width = C // GROUPS
    cell_count = SIDE * SIDE
    channel_last = jnp.transpose(latents, (0, 2, 1)).reshape(SAMPLES, SIDE, SIDE, C)
    start_field = channel_last.astype(jnp.float32)
    activated = jax.nn.silu(norm_groups(start_field, group_width)).astype(jnp.bfloat16)
    first_out = convolve(activated, first_kernel)
    scale_term = modulation[:, 0, :].astype(jnp.float32)[:, None, None, :]
    shift_term = modulation[:, 1, :].astype(jnp.float32)[:, None, None, :]
    modulated = jax.nn.silu(norm_groups(first_out, group_width) * (1.0 + scale_term) + shift_term).astype(jnp.bfloat16)
    residual = start_field + convolve(modulated, second_kernel)
    normed_out = norm_groups(residual, group_width).astype(jnp.bfloat16)
    order_index = jnp.argsort(destination, stable=True).astype(jnp.int32)
    prompt_ids = kept_prompt_list[order_index]
    live_lengths = lengths[prompt_ids]
    cache_rows = jnp.transpose(encoder_cache[prompt_ids], (0, 2, 1))
    queries = jnp.dot(normed_out.reshape(SAMPLES * cell_count, C), query_weight, preferred_element_type=jnp.float32)
    queries = queries.astype(jnp.bfloat16).reshape(SAMPLES, cell_count, HEADS, HEAD)
    heads_of_keys = cache_rows[:, :, :C].reshape(SAMPLES, L, HEADS, HEAD)
    value_heads = cache_rows[:, :, C:].reshape(SAMPLES, L, HEADS, HEAD)
    scores = jnp.einsum('sqhd,skhd->shqk', queries.astype(jnp.float32), heads_of_keys.astype(jnp.float32)) * HEAD ** (-0.5)
    visible = jnp.arange(L, dtype=jnp.int32)[None, None, None, :] < live_lengths[:, None, None, None]
    scores = jnp.where(visible, scores, MASKED)
    row_peak = lax.optimization_barrier(jnp.max(scores, axis=3, keepdims=True))
    exponent = jnp.exp(scores - row_peak)
    attention = (exponent / lax.optimization_barrier(jnp.sum(exponent, axis=3, keepdims=True))).astype(jnp.bfloat16)
    context = jnp.einsum('shqk,skhd->sqhd', attention.astype(jnp.float32), value_heads.astype(jnp.float32))
    context = context.astype(jnp.bfloat16).reshape(SAMPLES * cell_count, C)
    attended = jnp.dot(context, output_weight, preferred_element_type=jnp.float32).astype(jnp.bfloat16)
    attended = attended.reshape(SAMPLES, SIDE, SIDE, C)
    final_field = (residual + attended.astype(jnp.float32)).astype(jnp.bfloat16)
    return jnp.transpose(final_field.reshape(SAMPLES, cell_count, C), (0, 2, 1))
```

```python
import jax
import jax.numpy as jnp
from jax import lax
from jax.sharding import PartitionSpec as P

C = 640
GROUPS = 32
HEAD = 64
SIDE = 8


EPSILON = 1e-05
MASKED = -1e30


def norm_groups(values, group_width):
    field_shape = values.shape
    grouped = values.reshape(
        field_shape[0], field_shape[1] // group_width, group_width, field_shape[2]
    )
    center = grouped - jnp.mean(grouped, axis=(2, 3), keepdims=True)
    spread = jnp.mean(center * center, axis=(2, 3), keepdims=True)
    return (center * lax.rsqrt(spread + EPSILON)).reshape(field_shape)


def gather_channels(field):
    return lax.all_gather(field, "mp", axis=1, tiled=True)


def pair_gather_channels(field):
    across = lax.ppermute(field, "mp", [(i, i ^ 2) for i in range(4)])
    beside = lax.ppermute(field, "mp", [(i, i ^ 1) for i in range(4)])
    relayed = lax.ppermute(across, "mp", [(i, i ^ 1) for i in range(4)])
    return jnp.concatenate([field, beside, across, relayed], axis=1)


def shift_parts(shard, count):
    parts = [shard]
    for step in range(1, count):
        parts.append(lax.ppermute(shard, "dp", [(i, (i + step) % count) for i in range(count)]))
    return jnp.stack(parts)


def order_rows(stacked, wanted_blocks):
    my_shard = lax.axis_index("dp")
    count = stacked.shape[0]
    picked = jnp.take(stacked, (my_shard - wanted_blocks) % count, axis=0, mode="clip")
    return picked.reshape((count * stacked.shape[1],) + stacked.shape[2:])


def gather_kernel(weight_shard):
    return lax.all_gather(weight_shard, "dp", axis=0, tiled=True)


def gather_projection(weight_shard):
    return lax.all_gather(weight_shard, "dp", axis=0, tiled=True)


def apply_kernel(full_field, kernel):
    sample_count = full_field.shape[0]
    out_width = kernel.shape[2]
    tap_images = jnp.einsum("scq,cte->steq", full_field, kernel, preferred_element_type=jnp.float32)
    tap_images = tap_images.reshape(sample_count, 9, out_width, SIDE, SIDE)
    padded = jnp.pad(tap_images, ((0, 0), (0, 0), (0, 0), (1, 1), (1, 1)))
    running = padded[:, 0, :, 0:SIDE, 0:SIDE]
    for offset in range(1, 9):
        row_shift, col_shift = (offset // 3, offset % 3)
        running = (
            running
            + padded[:, offset, :, row_shift : row_shift + SIDE, col_shift : col_shift + SIDE]
        )
    return running.reshape(sample_count, out_width, SIDE * SIDE)


def local(
    latents,
    modulation,
    first_kernel,
    second_kernel,
    encoder_cache,
    query_weight,
    output_weight,
    kept_prompt_list,
    destination,
    lengths,
):
    group_width = C // GROUPS
    dp_count = lax.axis_size("dp")
    mp_count = lax.axis_size("mp")
    my_shard = lax.axis_index("dp")
    my_column = lax.axis_index("mp")
    sample_shard_count = latents.shape[0]
    prompt_dev = encoder_cache.shape[0]
    cache_len = encoder_cache.shape[2]
    cache_width = encoder_cache.shape[1]
    cell_count = latents.shape[2]
    slot_limit = 2 * (sample_shard_count // dp_count)
    all_samples = destination.shape[0]
    owner_target = destination.reshape(dp_count, sample_shard_count)
    positions = jnp.arange(sample_shard_count, dtype=jnp.int32)
    before = positions[None, :] < positions[:, None]
    same_target = owner_target[:, :, None] == owner_target[:, None, :]
    slot_rank = jnp.sum((same_target & before[None]).astype(jnp.int32), axis=2)
    my_target = lax.dynamic_index_in_dim(owner_target, my_shard, 0, keepdims=False)
    my_rank = lax.dynamic_index_in_dim(slot_rank, my_shard, 0, keepdims=False)
    my_prompts = (
        lax.dynamic_slice_in_dim(
            kept_prompt_list, my_shard * sample_shard_count, sample_shard_count
        )
        - my_shard * prompt_dev
    )
    send_slot = my_target * slot_limit + my_rank
    slot_table = send_slot[:, None] == jnp.arange(dp_count * slot_limit, dtype=jnp.int32)[None, :]
    source_row = jnp.sum(jnp.where(slot_table, my_prompts[:, None], 0), axis=0)
    filled = jnp.any(slot_table, axis=0)
    send_rows = jnp.take(encoder_cache, source_row, axis=0)
    send_rows = jnp.where(filled[:, None, None], send_rows, jnp.zeros_like(send_rows))
    outgoing = send_rows.reshape(dp_count, slot_limit, cache_width, cache_len)
    incoming = lax.all_to_all(outgoing, "dp", split_axis=0, concat_axis=0, tiled=True)
    arriving = destination == my_shard
    arrival_pos = jnp.cumsum(arriving.astype(jnp.int32)) - 1
    selector = arriving[None, :] & (arrival_pos[None, :] == positions[:, None])
    kept_prompt = jnp.sum(
        jnp.where(selector, jnp.arange(all_samples, dtype=jnp.int32)[None, :], 0), axis=1
    )
    incoming_order_rank = jnp.sum(jnp.where(selector, slot_rank.reshape(-1)[None, :], 0), axis=1)
    prompt_ids = jnp.sum(jnp.where(selector, kept_prompt_list[None, :], 0), axis=1)
    landing_slot = kept_prompt // sample_shard_count * slot_limit + incoming_order_rank
    my_pairs = jnp.take(
        incoming.reshape(dp_count * slot_limit, cache_width, cache_len), landing_slot, axis=0
    )
    prompt_hits = prompt_ids[:, None] == jnp.arange(lengths.shape[0], dtype=jnp.int32)[None, :]
    my_lengths = jnp.sum(jnp.where(prompt_hits, lengths[None, :], 0), axis=1)
    fast = dp_count == 4 and mp_count == 4
    weight_shards = (first_kernel, second_kernel, query_weight, output_weight)
    if fast:
        block_ids = jnp.arange(dp_count, dtype=jnp.int32)
        channel_blocks = jnp.bitwise_xor(block_ids, my_column)
        full_weights = (
            order_rows(shift_parts(first_kernel, dp_count), channel_blocks),
            order_rows(shift_parts(second_kernel, dp_count), channel_blocks),
            order_rows(shift_parts(query_weight, dp_count), block_ids),
            order_rows(shift_parts(output_weight, dp_count), block_ids),
        )
        spread_channels = pair_gather_channels
    else:
        full_weights = (
            gather_kernel(first_kernel),
            gather_kernel(second_kernel),
            gather_projection(query_weight),
            gather_projection(output_weight),
        )
        spread_channels = gather_channels
    start_field = latents.astype(jnp.float32)
    activated = jax.nn.silu(norm_groups(start_field, group_width)).astype(jnp.bfloat16)
    first_in = spread_channels(activated)

    def convolve(full_field, which_weight):
        return apply_kernel(full_field, full_weights[which_weight])

    def project(field_rows, which_weight):
        full_weight = full_weights[which_weight]
        return jnp.einsum(
            "scq,ce->seq", field_rows, full_weight, preferred_element_type=jnp.float32
        )

    first_out = convolve(first_in, 0)
    scale_term = modulation[:, 0, :].astype(jnp.float32)[:, :, None]
    shift_term = modulation[:, 1, :].astype(jnp.float32)[:, :, None]
    modulated = jax.nn.silu(
        norm_groups(first_out, group_width) * (1.0 + scale_term) + shift_term
    ).astype(jnp.bfloat16)
    second_in = spread_channels(modulated)
    residual = start_field + convolve(second_in, 1)
    normed_out = norm_groups(residual, group_width).astype(jnp.bfloat16)
    local_samples = sample_shard_count // mp_count
    query_cells, pair_heads = (
        lax.all_to_all(normed_out, "mp", split_axis=0, concat_axis=1, tiled=True),
        lax.all_to_all(my_pairs, "mp", split_axis=0, concat_axis=1, tiled=True),
    )
    total_width = query_cells.shape[1]
    head_count = total_width // HEAD
    queries = project(query_cells, 2).astype(jnp.bfloat16)
    queries = queries.reshape(local_samples, head_count, HEAD, cell_count)
    heads_of_keys = pair_heads[:, :total_width, :].reshape(
        local_samples, head_count, HEAD, cache_len
    )
    value_heads = pair_heads[:, total_width:, :].reshape(local_samples, head_count, HEAD, cache_len)
    scores = jnp.einsum(
        "shdq,shdk->shqk", queries, heads_of_keys, preferred_element_type=jnp.float32
    ) * HEAD ** (-0.5)
    local_lengths = lax.dynamic_slice_in_dim(my_lengths, my_column * local_samples, local_samples)
    visible = (
        jnp.arange(cache_len, dtype=jnp.int32)[None, None, None, :]
        < local_lengths[:, None, None, None]
    )
    scores = jnp.where(visible, scores, MASKED)
    row_peak = jnp.max(scores, axis=3, keepdims=True)
    exponent = jnp.exp(scores - row_peak)
    attention = (exponent / jnp.sum(exponent, axis=3, keepdims=True)).astype(jnp.bfloat16)
    context = jnp.einsum(
        "shqk,shdk->shdq", attention, value_heads, preferred_element_type=jnp.float32
    ).astype(jnp.bfloat16)
    attended = project(context.reshape(local_samples, total_width, cell_count), 3).astype(
        jnp.bfloat16
    )
    returned = lax.all_to_all(attended, "mp", split_axis=1, concat_axis=0, tiled=True)
    final_field = residual + returned.astype(jnp.float32)
    return final_field.astype(jnp.bfloat16)


def solution(mesh):
    in_specs = (
        P(("groups", "dp"), "mp", None),
        P(("groups", "dp"), None, "mp"),
        P("dp", None, "mp"),
        P("dp", None, "mp"),
        P(("groups", "dp"), "mp", None),
        P("dp", None),
        P("dp", None),
        P("groups"),
        P("groups"),
        P("groups"),
    )
    out_specs = P(("groups", "dp"), "mp", None)
    return jax.shard_map(local, mesh=mesh, in_specs=in_specs, out_specs=out_specs, check_vma=False)
```

```python
import jax
import jax.numpy as jnp
from jax import lax
from jax.sharding import PartitionSpec as P

C = 640
GROUPS = 32
HEAD = 64
SIDE = 8


EPSILON = 1e-05
MASKED = -1e30


def norm_groups(values, group_width):
    field_shape = values.shape
    grouped = values.reshape(
        field_shape[0], field_shape[1] // group_width, group_width, field_shape[2]
    )
    center = grouped - jnp.mean(grouped, axis=(2, 3), keepdims=True)
    spread = jnp.mean(center * center, axis=(2, 3), keepdims=True)
    return (center * lax.rsqrt(spread + EPSILON)).reshape(field_shape)


def gather_channels(field):
    return lax.all_gather(field, "mp", axis=1, tiled=True)


def pair_gather_channels(field):
    across = lax.ppermute(field, "mp", [(i, i ^ 2) for i in range(4)])
    beside = lax.ppermute(field, "mp", [(i, i ^ 1) for i in range(4)])
    relayed = lax.ppermute(across, "mp", [(i, i ^ 1) for i in range(4)])
    return jnp.concatenate([field, beside, across, relayed], axis=1)


def line_gather_flat(flat, count):
    my_shard = lax.axis_index("dp")
    rightward = [(i, i + 1) for i in range(count - 1)]
    leftward = [(i + 1, i) for i in range(count - 1)]
    going_right, going_left = flat, flat
    held = [flat]
    from_left, from_right = [], []
    for _ in range(1, count):
        going_right = lax.ppermute(going_right, "dp", rightward)
        going_left = lax.ppermute(going_left, "dp", leftward)
        from_left.append(going_right)
        from_right.append(going_left)
    stacked = jnp.stack(held + from_left + from_right)
    blocks = jnp.arange(count, dtype=jnp.int32)
    gap = blocks - my_shard
    slot = jnp.where(gap == 0, 0, jnp.where(gap < 0, -gap, count - 1 + gap))
    return jnp.take(stacked, slot, axis=0, mode="clip")


def shift_parts(shard, count):
    parts = [shard]
    for step in range(1, count):
        parts.append(lax.ppermute(shard, "dp", [(i, (i + step) % count) for i in range(count)]))
    return jnp.stack(parts)


def order_rows(stacked, wanted_blocks):
    my_shard = lax.axis_index("dp")
    count = stacked.shape[0]
    picked = jnp.take(stacked, (my_shard - wanted_blocks) % count, axis=0, mode="clip")
    return picked.reshape((count * stacked.shape[1],) + stacked.shape[2:])


def gather_kernel(weight_shard):
    return lax.all_gather(weight_shard, "dp", axis=0, tiled=True)


def gather_projection(weight_shard):
    return lax.all_gather(weight_shard, "dp", axis=0, tiled=True)


def apply_kernel(full_field, kernel):
    sample_count = full_field.shape[0]
    out_width = kernel.shape[2]
    tap_images = jnp.einsum("scq,cte->steq", full_field, kernel, preferred_element_type=jnp.float32)
    tap_images = tap_images.reshape(sample_count, 9, out_width, SIDE, SIDE)
    padded = jnp.pad(tap_images, ((0, 0), (0, 0), (0, 0), (1, 1), (1, 1)))
    running = padded[:, 0, :, 0:SIDE, 0:SIDE]
    for offset in range(1, 9):
        row_shift, col_shift = (offset // 3, offset % 3)
        running = (
            running
            + padded[:, offset, :, row_shift : row_shift + SIDE, col_shift : col_shift + SIDE]
        )
    return running.reshape(sample_count, out_width, SIDE * SIDE)


def local(
    latents,
    modulation,
    first_kernel,
    second_kernel,
    encoder_cache,
    query_weight,
    output_weight,
    kept_prompt_list,
    destination,
    lengths,
):
    group_width = C // GROUPS
    dp_count = lax.axis_size("dp")
    mp_count = lax.axis_size("mp")
    my_shard = lax.axis_index("dp")
    my_column = lax.axis_index("mp")
    sample_shard_count = latents.shape[0]
    prompt_dev = encoder_cache.shape[0]
    cache_len = encoder_cache.shape[2]
    cache_width = encoder_cache.shape[1]
    cell_count = latents.shape[2]
    slot_limit = 2 * (sample_shard_count // dp_count)
    all_samples = destination.shape[0]
    owner_target = destination.reshape(dp_count, sample_shard_count)
    positions = jnp.arange(sample_shard_count, dtype=jnp.int32)
    before = positions[None, :] < positions[:, None]
    same_target = owner_target[:, :, None] == owner_target[:, None, :]
    slot_rank = jnp.sum((same_target & before[None]).astype(jnp.int32), axis=2)
    my_target = lax.dynamic_index_in_dim(owner_target, my_shard, 0, keepdims=False)
    my_rank = lax.dynamic_index_in_dim(slot_rank, my_shard, 0, keepdims=False)
    my_prompts = (
        lax.dynamic_slice_in_dim(
            kept_prompt_list, my_shard * sample_shard_count, sample_shard_count
        )
        - my_shard * prompt_dev
    )
    send_slot = my_target * slot_limit + my_rank
    slot_table = send_slot[:, None] == jnp.arange(dp_count * slot_limit, dtype=jnp.int32)[None, :]
    source_row = jnp.sum(jnp.where(slot_table, my_prompts[:, None], 0), axis=0)
    filled = jnp.any(slot_table, axis=0)
    send_rows = jnp.take(encoder_cache, source_row, axis=0)
    send_rows = jnp.where(filled[:, None, None], send_rows, jnp.zeros_like(send_rows))
    outgoing = send_rows.reshape(dp_count, slot_limit, cache_width, cache_len)
    arriving = destination == my_shard
    arrival_pos = jnp.cumsum(arriving.astype(jnp.int32)) - 1
    selector = arriving[None, :] & (arrival_pos[None, :] == positions[:, None])
    kept_prompt = jnp.sum(
        jnp.where(selector, jnp.arange(all_samples, dtype=jnp.int32)[None, :], 0), axis=1
    )
    incoming_order_rank = jnp.sum(jnp.where(selector, slot_rank.reshape(-1)[None, :], 0), axis=1)
    prompt_ids = jnp.sum(jnp.where(selector, kept_prompt_list[None, :], 0), axis=1)
    landing_slot = kept_prompt // sample_shard_count * slot_limit + incoming_order_rank
    prompt_hits = prompt_ids[:, None] == jnp.arange(lengths.shape[0], dtype=jnp.int32)[None, :]
    my_lengths = jnp.sum(jnp.where(prompt_hits, lengths[None, :], 0), axis=1)
    fast = dp_count == 4 and mp_count == 4
    weight_shards = (first_kernel, second_kernel, query_weight, output_weight)
    if fast:
        block_ids = jnp.arange(dp_count, dtype=jnp.int32)
        channel_blocks = jnp.bitwise_xor(block_ids, my_column)
        rows = first_kernel.shape[0]
        lane = first_kernel.shape[2]
        taps = first_kernel.shape[1]
        packed = jnp.concatenate(
            [
                first_kernel,
                second_kernel,
                query_weight.reshape(rows, -1, lane),
                output_weight.reshape(rows, -1, lane),
            ],
            axis=1,
        )
        gathered = line_gather_flat(packed, dp_count)
        proj_taps = query_weight.shape[1] // lane
        bounds = (
            (0, taps, channel_blocks, None),
            (taps, 2 * taps, channel_blocks, None),
            (2 * taps, 2 * taps + proj_taps, block_ids, query_weight.shape[1]),
            (2 * taps + proj_taps, 2 * taps + 2 * proj_taps, block_ids, output_weight.shape[1]),
        )
        full_weights = []
        for low, high, order, width in bounds:
            picked = jnp.take(gathered[:, :, low:high, :], order, axis=0, mode="clip")
            if width is None:
                full_weights.append(picked.reshape(dp_count * rows, high - low, lane))
            else:
                full_weights.append(picked.reshape(dp_count * rows, width))
        full_weights = tuple(full_weights)
        outgoing = lax.optimization_barrier((outgoing, gathered))[0]
        spread_channels = pair_gather_channels
    else:
        full_weights = (
            gather_kernel(first_kernel),
            gather_kernel(second_kernel),
            gather_projection(query_weight),
            gather_projection(output_weight),
        )
        spread_channels = gather_channels
    incoming = lax.all_to_all(outgoing, "dp", split_axis=0, concat_axis=0, tiled=True)
    my_pairs = jnp.take(
        incoming.reshape(dp_count * slot_limit, cache_width, cache_len), landing_slot, axis=0
    )
    start_field = latents.astype(jnp.float32)
    activated = jax.nn.silu(norm_groups(start_field, group_width)).astype(jnp.bfloat16)
    first_in = spread_channels(activated)

    def convolve(full_field, which_weight):
        return apply_kernel(full_field, full_weights[which_weight])

    def project(field_rows, which_weight):
        full_weight = full_weights[which_weight]
        return jnp.einsum(
            "scq,ce->seq", field_rows, full_weight, preferred_element_type=jnp.float32
        )

    first_out = convolve(first_in, 0)
    scale_term = modulation[:, 0, :].astype(jnp.float32)[:, :, None]
    shift_term = modulation[:, 1, :].astype(jnp.float32)[:, :, None]
    modulated = jax.nn.silu(
        norm_groups(first_out, group_width) * (1.0 + scale_term) + shift_term
    ).astype(jnp.bfloat16)
    second_in = spread_channels(modulated)
    residual = start_field + convolve(second_in, 1)
    normed_out = norm_groups(residual, group_width).astype(jnp.bfloat16)
    local_samples = sample_shard_count // mp_count
    query_cells, pair_heads = (
        lax.all_to_all(normed_out, "mp", split_axis=0, concat_axis=1, tiled=True),
        lax.all_to_all(my_pairs, "mp", split_axis=0, concat_axis=1, tiled=True),
    )
    total_width = query_cells.shape[1]
    head_count = total_width // HEAD
    queries = project(query_cells, 2).astype(jnp.bfloat16)
    queries = queries.reshape(local_samples, head_count, HEAD, cell_count)
    heads_of_keys = pair_heads[:, :total_width, :].reshape(
        local_samples, head_count, HEAD, cache_len
    )
    value_heads = pair_heads[:, total_width:, :].reshape(local_samples, head_count, HEAD, cache_len)
    scores = jnp.einsum(
        "shdq,shdk->shqk", queries, heads_of_keys, preferred_element_type=jnp.float32
    ) * HEAD ** (-0.5)
    local_lengths = lax.dynamic_slice_in_dim(my_lengths, my_column * local_samples, local_samples)
    visible = (
        jnp.arange(cache_len, dtype=jnp.int32)[None, None, None, :]
        < local_lengths[:, None, None, None]
    )
    scores = jnp.where(visible, scores, MASKED)
    row_peak = jnp.max(scores, axis=3, keepdims=True)
    exponent = jnp.exp(scores - row_peak)
    attention = (exponent / jnp.sum(exponent, axis=3, keepdims=True)).astype(jnp.bfloat16)
    context = jnp.einsum(
        "shqk,shdk->shdq", attention, value_heads, preferred_element_type=jnp.float32
    ).astype(jnp.bfloat16)
    attended = project(context.reshape(local_samples, total_width, cell_count), 3).astype(
        jnp.bfloat16
    )
    returned = lax.all_to_all(attended, "mp", split_axis=1, concat_axis=0, tiled=True)
    final_field = residual + returned.astype(jnp.float32)
    return final_field.astype(jnp.bfloat16)


def solution(mesh):
    in_specs = (
        P(("groups", "dp"), "mp", None),
        P(("groups", "dp"), None, "mp"),
        P("dp", None, "mp"),
        P("dp", None, "mp"),
        P(("groups", "dp"), "mp", None),
        P("dp", None),
        P("dp", None),
        P("groups"),
        P("groups"),
        P("groups"),
    )
    out_specs = P(("groups", "dp"), "mp", None)
    return jax.shard_map(local, mesh=mesh, in_specs=in_specs, out_specs=out_specs, check_vma=False)
```

```python
import jax
import jax.numpy as jnp
from jax import lax
from jax.sharding import PartitionSpec as P

C = 640
GROUPS = 32
HEAD = 64
SIDE = 8


EPSILON = 1e-05
MASKED = -1e30


def norm_groups(values, group_width):
    field_shape = values.shape
    grouped = values.reshape(
        field_shape[0], field_shape[1] // group_width, group_width, field_shape[2]
    )
    center = grouped - jnp.mean(grouped, axis=(2, 3), keepdims=True)
    spread = jnp.mean(center * center, axis=(2, 3), keepdims=True)
    return (center * lax.rsqrt(spread + EPSILON)).reshape(field_shape)


def gather_channels(field):
    return lax.all_gather(field, "mp", axis=1, tiled=True)


def pair_gather_channels(field):
    dense = field.reshape(-1, 128)
    across = lax.ppermute(dense, "mp", [(i, i ^ 2) for i in range(4)])
    beside = lax.ppermute(dense, "mp", [(i, i ^ 1) for i in range(4)])
    relayed = lax.ppermute(across, "mp", [(i, i ^ 1) for i in range(4)])
    parts = [part.reshape(field.shape) for part in (beside, across, relayed)]
    return jnp.concatenate([field] + parts, axis=1)


def line_gather_flat(flat, count):
    my_shard = lax.axis_index("dp")
    rightward = [(i, i + 1) for i in range(count - 1)]
    leftward = [(i + 1, i) for i in range(count - 1)]
    going_right, going_left = flat, flat
    held = [flat]
    from_left, from_right = [], []
    for _ in range(1, count):
        going_right = lax.ppermute(going_right, "dp", rightward)
        going_left = lax.ppermute(going_left, "dp", leftward)
        from_left.append(going_right)
        from_right.append(going_left)
    line = jnp.stack(from_left[::-1] + held + from_right)
    return lax.dynamic_slice_in_dim(line, count - 1 - my_shard, count, axis=0)


def shift_parts(shard, count):
    parts = [shard]
    for step in range(1, count):
        parts.append(lax.ppermute(shard, "dp", [(i, (i + step) % count) for i in range(count)]))
    return jnp.stack(parts)


def order_rows(stacked, wanted_blocks):
    my_shard = lax.axis_index("dp")
    count = stacked.shape[0]
    picked = jnp.take(stacked, (my_shard - wanted_blocks) % count, axis=0, mode="clip")
    return picked.reshape((count * stacked.shape[1],) + stacked.shape[2:])


def gather_kernel(weight_shard):
    return lax.all_gather(weight_shard, "dp", axis=0, tiled=True)


def gather_projection(weight_shard):
    return lax.all_gather(weight_shard, "dp", axis=0, tiled=True)


def apply_kernel(full_field, kernel):
    sample_count = full_field.shape[0]
    out_width = kernel.shape[2]
    tap_images = jnp.einsum("scq,cte->stqe", full_field, kernel, preferred_element_type=jnp.float32)
    tap_images = tap_images.reshape(sample_count, 9, SIDE, SIDE, out_width)
    padded = jnp.pad(tap_images, ((0, 0), (0, 0), (1, 1), (1, 1), (0, 0)))
    running = padded[:, 0, 0:SIDE, 0:SIDE, :]
    for offset in range(1, 9):
        row_shift, col_shift = (offset // 3, offset % 3)
        running = (
            running
            + padded[:, offset, row_shift : row_shift + SIDE, col_shift : col_shift + SIDE, :]
        )
    return jnp.transpose(running.reshape(sample_count, SIDE * SIDE, out_width), (0, 2, 1))


def local(
    latents,
    modulation,
    first_kernel,
    second_kernel,
    encoder_cache,
    query_weight,
    output_weight,
    kept_prompt_list,
    destination,
    lengths,
):
    group_width = C // GROUPS
    dp_count = lax.axis_size("dp")
    mp_count = lax.axis_size("mp")
    my_shard = lax.axis_index("dp")
    my_column = lax.axis_index("mp")
    sample_shard_count = latents.shape[0]
    prompt_dev = encoder_cache.shape[0]
    cache_len = encoder_cache.shape[2]
    cache_width = encoder_cache.shape[1]
    cell_count = latents.shape[2]
    slot_limit = 2 * (sample_shard_count // dp_count)
    all_samples = destination.shape[0]
    owner_target = destination.reshape(dp_count, sample_shard_count)
    positions = jnp.arange(sample_shard_count, dtype=jnp.int32)
    before = positions[None, :] < positions[:, None]
    same_target = owner_target[:, :, None] == owner_target[:, None, :]
    slot_rank = jnp.sum((same_target & before[None]).astype(jnp.int32), axis=2)
    my_target = lax.dynamic_index_in_dim(owner_target, my_shard, 0, keepdims=False)
    my_rank = lax.dynamic_index_in_dim(slot_rank, my_shard, 0, keepdims=False)
    my_prompts = (
        lax.dynamic_slice_in_dim(
            kept_prompt_list, my_shard * sample_shard_count, sample_shard_count
        )
        - my_shard * prompt_dev
    )
    send_slot = my_target * slot_limit + my_rank
    slot_table = send_slot[:, None] == jnp.arange(dp_count * slot_limit, dtype=jnp.int32)[None, :]
    source_row = jnp.sum(jnp.where(slot_table, my_prompts[:, None], 0), axis=0)
    filled = jnp.any(slot_table, axis=0)
    send_rows = jnp.take(encoder_cache, source_row, axis=0)
    send_rows = jnp.where(filled[:, None, None], send_rows, jnp.zeros_like(send_rows))
    outgoing = send_rows.reshape(dp_count, slot_limit, cache_width, cache_len)
    arriving = destination == my_shard
    arrival_pos = jnp.cumsum(arriving.astype(jnp.int32)) - 1
    selector = arriving[None, :] & (arrival_pos[None, :] == positions[:, None])
    kept_prompt = jnp.sum(
        jnp.where(selector, jnp.arange(all_samples, dtype=jnp.int32)[None, :], 0), axis=1
    )
    incoming_order_rank = jnp.sum(jnp.where(selector, slot_rank.reshape(-1)[None, :], 0), axis=1)
    prompt_ids = jnp.sum(jnp.where(selector, kept_prompt_list[None, :], 0), axis=1)
    landing_slot = kept_prompt // sample_shard_count * slot_limit + incoming_order_rank
    prompt_hits = prompt_ids[:, None] == jnp.arange(lengths.shape[0], dtype=jnp.int32)[None, :]
    my_lengths = jnp.sum(jnp.where(prompt_hits, lengths[None, :], 0), axis=1)
    fast = dp_count == 4 and mp_count == 4
    weight_shards = (first_kernel, second_kernel, query_weight, output_weight)
    if fast:
        block_ids = jnp.arange(dp_count, dtype=jnp.int32)
        channel_blocks = jnp.bitwise_xor(block_ids, my_column)
        pieces = (first_kernel, second_kernel, query_weight, output_weight)
        dense = [piece.reshape(-1, 128) for piece in pieces]
        natural = line_gather_flat(jnp.concatenate(dense, axis=0), dp_count)
        kernel_rows = dense[0].shape[0] + dense[1].shape[0]
        kernel_part = jnp.take(natural[:, :kernel_rows], channel_blocks, axis=0, mode="clip")
        proj_part = natural[:, kernel_rows:]
        full_weights = []
        cut = 0
        for piece, block, source in zip(pieces, dense, (kernel_part, kernel_part, proj_part, proj_part)):
            if cut == kernel_rows:
                cut = 0
            chunk = source[:, cut : cut + block.shape[0]]
            cut += block.shape[0]
            full_weights.append(chunk.reshape((dp_count * piece.shape[0],) + piece.shape[1:]))
        gathered = (kernel_part, proj_part)
        full_weights = tuple(full_weights)
        outgoing = lax.optimization_barrier((outgoing, gathered))[0]
        spread_channels = pair_gather_channels
    else:
        full_weights = (
            gather_kernel(first_kernel),
            gather_kernel(second_kernel),
            gather_projection(query_weight),
            gather_projection(output_weight),
        )
        spread_channels = gather_channels
    incoming = lax.all_to_all(outgoing, "dp", split_axis=0, concat_axis=0, tiled=True)
    my_pairs = jnp.take(
        incoming.reshape(dp_count * slot_limit, cache_width, cache_len), landing_slot, axis=0
    )
    start_field = latents.astype(jnp.float32)
    activated = jax.nn.silu(norm_groups(start_field, group_width)).astype(jnp.bfloat16)
    first_in = spread_channels(activated)

    def convolve(full_field, which_weight):
        return apply_kernel(full_field, full_weights[which_weight])

    def project(field_rows, which_weight):
        full_weight = full_weights[which_weight]
        return jnp.einsum(
            "scq,ce->seq", field_rows, full_weight, preferred_element_type=jnp.float32
        )

    first_out = convolve(first_in, 0)
    scale_term = modulation[:, 0, :].astype(jnp.float32)[:, :, None]
    shift_term = modulation[:, 1, :].astype(jnp.float32)[:, :, None]
    modulated = jax.nn.silu(
        norm_groups(first_out, group_width) * (1.0 + scale_term) + shift_term
    ).astype(jnp.bfloat16)
    second_in = spread_channels(modulated)
    residual = start_field + convolve(second_in, 1)
    normed_out = norm_groups(residual, group_width).astype(jnp.bfloat16)
    local_samples = sample_shard_count // mp_count
    query_cells, pair_heads = (
        lax.all_to_all(normed_out, "mp", split_axis=0, concat_axis=1, tiled=True),
        lax.all_to_all(my_pairs, "mp", split_axis=0, concat_axis=1, tiled=True),
    )
    total_width = query_cells.shape[1]
    head_count = total_width // HEAD
    queries = project(query_cells, 2).astype(jnp.bfloat16)
    queries = queries.reshape(local_samples, head_count, HEAD, cell_count)
    heads_of_keys = pair_heads[:, :total_width, :].reshape(
        local_samples, head_count, HEAD, cache_len
    )
    value_heads = pair_heads[:, total_width:, :].reshape(local_samples, head_count, HEAD, cache_len)
    scores = jnp.einsum(
        "shdq,shdk->shqk", queries, heads_of_keys, preferred_element_type=jnp.float32
    ) * HEAD ** (-0.5)
    local_lengths = lax.dynamic_slice_in_dim(my_lengths, my_column * local_samples, local_samples)
    visible = (
        jnp.arange(cache_len, dtype=jnp.int32)[None, None, None, :]
        < local_lengths[:, None, None, None]
    )
    scores = jnp.where(visible, scores, MASKED)
    row_peak = jnp.max(scores, axis=3, keepdims=True)
    exponent = jnp.exp(scores - row_peak)
    attention = (exponent / jnp.sum(exponent, axis=3, keepdims=True)).astype(jnp.bfloat16)
    context = jnp.einsum(
        "shqk,shdk->shdq", attention, value_heads, preferred_element_type=jnp.float32
    ).astype(jnp.bfloat16)
    attended = project(context.reshape(local_samples, total_width, cell_count), 3).astype(
        jnp.bfloat16
    )
    returned = lax.all_to_all(attended, "mp", split_axis=1, concat_axis=0, tiled=True)
    final_field = residual + returned.astype(jnp.float32)
    return final_field.astype(jnp.bfloat16)


def solution(mesh):
    in_specs = (
        P(("groups", "dp"), "mp", None),
        P(("groups", "dp"), None, "mp"),
        P("dp", None, "mp"),
        P("dp", None, "mp"),
        P(("groups", "dp"), "mp", None),
        P("dp", None),
        P("dp", None),
        P("groups"),
        P("groups"),
        P("groups"),
    )
    out_specs = P(("groups", "dp"), "mp", None)
    return jax.shard_map(local, mesh=mesh, in_specs=in_specs, out_specs=out_specs, check_vma=False)
```

```python
import jax
import jax.numpy as jnp
from jax import lax
from jax.sharding import PartitionSpec as P

C = 640
GROUPS = 32
HEAD = 64
SIDE = 8


EPSILON = 1e-05
MASKED = -1e30


def norm_groups(values, group_width):
    field_shape = values.shape
    grouped = values.reshape(
        field_shape[0], field_shape[1] // group_width, group_width, field_shape[2]
    )
    center = grouped - jnp.mean(grouped, axis=(2, 3), keepdims=True)
    spread = jnp.mean(center * center, axis=(2, 3), keepdims=True)
    return (center * lax.rsqrt(spread + EPSILON)).reshape(field_shape)


def gather_channels(field):
    return lax.all_gather(field, "mp", axis=1, tiled=True)


def pair_gather_channels(field):
    dense = field.reshape(-1, 128)
    across = lax.ppermute(dense, "mp", [(i, i ^ 2) for i in range(4)])
    beside = lax.ppermute(dense, "mp", [(i, i ^ 1) for i in range(4)])
    relayed = lax.ppermute(across, "mp", [(i, i ^ 1) for i in range(4)])
    parts = [part.reshape(field.shape) for part in (beside, across, relayed)]
    return jnp.concatenate([field] + parts, axis=1)


def line_gather_flat(flat, count):
    my_shard = lax.axis_index("dp")
    rightward = [(i, i + 1) for i in range(count - 1)]
    leftward = [(i + 1, i) for i in range(count - 1)]
    going_right, going_left = flat, flat
    held = [flat]
    from_left, from_right = [], []
    for _ in range(1, count):
        going_right = lax.ppermute(going_right, "dp", rightward)
        going_left = lax.ppermute(going_left, "dp", leftward)
        from_left.append(going_right)
        from_right.append(going_left)
    line = jnp.stack(from_left[::-1] + held + from_right)
    return lax.dynamic_slice_in_dim(line, count - 1 - my_shard, count, axis=0)


def split_line_gather(packed):
    my_shard = lax.axis_index("dp")
    my_group = lax.axis_index("groups")
    halves = packed.reshape(2, packed.shape[0] // 2, packed.shape[1])
    mine = lax.dynamic_index_in_dim(halves, my_group, 0, keepdims=False)
    rightward = [(i, i + 1) for i in range(3)]
    leftward = [(i + 1, i) for i in range(3)]
    swap = [(0, 1), (1, 0)]
    left_1 = lax.ppermute(mine, "dp", rightward)
    right_1 = lax.ppermute(mine, "dp", leftward)
    first_swap = lax.ppermute(jnp.where(my_shard >= 1, left_1, right_1), "groups", swap)
    left_2 = lax.ppermute(left_1, "dp", rightward)
    right_2 = lax.ppermute(right_1, "dp", leftward)
    second_swap = lax.ppermute(jnp.where(my_shard >= 2, left_2, right_2), "groups", swap)
    left_3 = lax.ppermute(left_2, "dp", rightward)
    right_3 = lax.ppermute(right_2, "dp", leftward)
    third_pick = jnp.where(my_shard == 0, right_3, jnp.where(my_shard == 3, left_3, right_1))
    third_swap = lax.ppermute(third_pick, "groups", swap)

    def whole(own_half, other_half):
        lead = jnp.where(my_group == 0, own_half, other_half)
        tail = jnp.where(my_group == 0, other_half, own_half)
        return jnp.concatenate([lead, tail], axis=0)

    line = jnp.stack(
        [
            whole(left_3, third_swap),
            whole(left_2, second_swap),
            whole(left_1, first_swap),
            packed,
            whole(right_1, jnp.where(my_shard == 0, first_swap, third_swap)),
            whole(right_2, second_swap),
            whole(right_3, third_swap),
        ]
    )
    return lax.dynamic_slice_in_dim(line, 3 - my_shard, 4, axis=0)


def shift_parts(shard, count):
    parts = [shard]
    for step in range(1, count):
        parts.append(lax.ppermute(shard, "dp", [(i, (i + step) % count) for i in range(count)]))
    return jnp.stack(parts)


def order_rows(stacked, wanted_blocks):
    my_shard = lax.axis_index("dp")
    count = stacked.shape[0]
    picked = jnp.take(stacked, (my_shard - wanted_blocks) % count, axis=0, mode="clip")
    return picked.reshape((count * stacked.shape[1],) + stacked.shape[2:])


def gather_kernel(weight_shard):
    return lax.all_gather(weight_shard, "dp", axis=0, tiled=True)


def gather_projection(weight_shard):
    return lax.all_gather(weight_shard, "dp", axis=0, tiled=True)


def apply_kernel(full_field, kernel):
    sample_count = full_field.shape[0]
    out_width = kernel.shape[2]
    tap_images = jnp.einsum("scq,cte->stqe", full_field, kernel, preferred_element_type=jnp.float32)
    tap_images = tap_images.reshape(sample_count, 9, SIDE, SIDE, out_width)
    padded = jnp.pad(tap_images, ((0, 0), (0, 0), (1, 1), (1, 1), (0, 0)))
    running = padded[:, 0, 0:SIDE, 0:SIDE, :]
    for offset in range(1, 9):
        row_shift, col_shift = (offset // 3, offset % 3)
        running = (
            running
            + padded[:, offset, row_shift : row_shift + SIDE, col_shift : col_shift + SIDE, :]
        )
    return jnp.transpose(running.reshape(sample_count, SIDE * SIDE, out_width), (0, 2, 1))


def local(
    latents,
    modulation,
    first_kernel,
    second_kernel,
    encoder_cache,
    query_weight,
    output_weight,
    kept_prompt_list,
    destination,
    lengths,
):
    group_width = C // GROUPS
    dp_count = lax.axis_size("dp")
    mp_count = lax.axis_size("mp")
    my_shard = lax.axis_index("dp")
    my_column = lax.axis_index("mp")
    sample_shard_count = latents.shape[0]
    prompt_dev = encoder_cache.shape[0]
    cache_len = encoder_cache.shape[2]
    cache_width = encoder_cache.shape[1]
    cell_count = latents.shape[2]
    slot_limit = 2 * (sample_shard_count // dp_count)
    all_samples = destination.shape[0]
    owner_target = destination.reshape(dp_count, sample_shard_count)
    positions = jnp.arange(sample_shard_count, dtype=jnp.int32)
    before = positions[None, :] < positions[:, None]
    same_target = owner_target[:, :, None] == owner_target[:, None, :]
    slot_rank = jnp.sum((same_target & before[None]).astype(jnp.int32), axis=2)
    my_target = lax.dynamic_index_in_dim(owner_target, my_shard, 0, keepdims=False)
    my_rank = lax.dynamic_index_in_dim(slot_rank, my_shard, 0, keepdims=False)
    my_prompts = (
        lax.dynamic_slice_in_dim(
            kept_prompt_list, my_shard * sample_shard_count, sample_shard_count
        )
        - my_shard * prompt_dev
    )
    send_slot = my_target * slot_limit + my_rank
    slot_table = send_slot[:, None] == jnp.arange(dp_count * slot_limit, dtype=jnp.int32)[None, :]
    source_row = jnp.sum(jnp.where(slot_table, my_prompts[:, None], 0), axis=0)
    filled = jnp.any(slot_table, axis=0)
    send_rows = jnp.take(encoder_cache, source_row, axis=0)
    send_rows = jnp.where(filled[:, None, None], send_rows, jnp.zeros_like(send_rows))
    outgoing = send_rows.reshape(dp_count, slot_limit, cache_width, cache_len)
    arriving = destination == my_shard
    arrival_pos = jnp.cumsum(arriving.astype(jnp.int32)) - 1
    selector = arriving[None, :] & (arrival_pos[None, :] == positions[:, None])
    kept_prompt = jnp.sum(
        jnp.where(selector, jnp.arange(all_samples, dtype=jnp.int32)[None, :], 0), axis=1
    )
    incoming_order_rank = jnp.sum(jnp.where(selector, slot_rank.reshape(-1)[None, :], 0), axis=1)
    prompt_ids = jnp.sum(jnp.where(selector, kept_prompt_list[None, :], 0), axis=1)
    landing_slot = kept_prompt // sample_shard_count * slot_limit + incoming_order_rank
    prompt_hits = prompt_ids[:, None] == jnp.arange(lengths.shape[0], dtype=jnp.int32)[None, :]
    my_lengths = jnp.sum(jnp.where(prompt_hits, lengths[None, :], 0), axis=1)
    fast = dp_count == 4 and mp_count == 4 and lax.axis_size("groups") == 2
    weight_shards = (first_kernel, second_kernel, query_weight, output_weight)
    if fast:
        block_ids = jnp.arange(dp_count, dtype=jnp.int32)
        channel_blocks = jnp.bitwise_xor(block_ids, my_column)
        pieces = (first_kernel, second_kernel, query_weight, output_weight)
        dense = [piece.reshape(-1, 128) for piece in pieces]
        natural = split_line_gather(jnp.concatenate(dense, axis=0))
        kernel_rows = dense[0].shape[0] + dense[1].shape[0]
        kernel_part = jnp.take(natural[:, :kernel_rows], channel_blocks, axis=0, mode="clip")
        proj_part = natural[:, kernel_rows:]
        full_weights = []
        cut = 0
        for piece, block, source in zip(pieces, dense, (kernel_part, kernel_part, proj_part, proj_part)):
            if cut == kernel_rows:
                cut = 0
            chunk = source[:, cut : cut + block.shape[0]]
            cut += block.shape[0]
            full_weights.append(chunk.reshape((dp_count * piece.shape[0],) + piece.shape[1:]))
        gathered = (kernel_part, proj_part)
        full_weights = tuple(full_weights)
        outgoing = lax.optimization_barrier((outgoing, gathered))[0]
        spread_channels = pair_gather_channels
    else:
        full_weights = (
            gather_kernel(first_kernel),
            gather_kernel(second_kernel),
            gather_projection(query_weight),
            gather_projection(output_weight),
        )
        spread_channels = gather_channels
    incoming = lax.all_to_all(outgoing, "dp", split_axis=0, concat_axis=0, tiled=True)
    my_pairs = jnp.take(
        incoming.reshape(dp_count * slot_limit, cache_width, cache_len), landing_slot, axis=0
    )
    start_field = latents.astype(jnp.float32)
    activated = jax.nn.silu(norm_groups(start_field, group_width)).astype(jnp.bfloat16)
    first_in = spread_channels(activated)

    def convolve(full_field, which_weight):
        return apply_kernel(full_field, full_weights[which_weight])

    def project(field_rows, which_weight):
        full_weight = full_weights[which_weight]
        return jnp.einsum(
            "scq,ce->seq", field_rows, full_weight, preferred_element_type=jnp.float32
        )

    first_out = convolve(first_in, 0)
    scale_term = modulation[:, 0, :].astype(jnp.float32)[:, :, None]
    shift_term = modulation[:, 1, :].astype(jnp.float32)[:, :, None]
    modulated = jax.nn.silu(
        norm_groups(first_out, group_width) * (1.0 + scale_term) + shift_term
    ).astype(jnp.bfloat16)
    second_in = spread_channels(modulated)
    residual = start_field + convolve(second_in, 1)
    normed_out = norm_groups(residual, group_width).astype(jnp.bfloat16)
    local_samples = sample_shard_count // mp_count
    query_cells, pair_heads = (
        lax.all_to_all(normed_out, "mp", split_axis=0, concat_axis=1, tiled=True),
        lax.all_to_all(my_pairs, "mp", split_axis=0, concat_axis=1, tiled=True),
    )
    total_width = query_cells.shape[1]
    head_count = total_width // HEAD
    queries = project(query_cells, 2).astype(jnp.bfloat16)
    queries = queries.reshape(local_samples, head_count, HEAD, cell_count)
    heads_of_keys = pair_heads[:, :total_width, :].reshape(
        local_samples, head_count, HEAD, cache_len
    )
    value_heads = pair_heads[:, total_width:, :].reshape(local_samples, head_count, HEAD, cache_len)
    scores = jnp.einsum(
        "shdq,shdk->shqk", queries, heads_of_keys, preferred_element_type=jnp.float32
    ) * HEAD ** (-0.5)
    local_lengths = lax.dynamic_slice_in_dim(my_lengths, my_column * local_samples, local_samples)
    visible = (
        jnp.arange(cache_len, dtype=jnp.int32)[None, None, None, :]
        < local_lengths[:, None, None, None]
    )
    scores = jnp.where(visible, scores, MASKED)
    row_peak = jnp.max(scores, axis=3, keepdims=True)
    exponent = jnp.exp(scores - row_peak)
    attention = (exponent / jnp.sum(exponent, axis=3, keepdims=True)).astype(jnp.bfloat16)
    context = jnp.einsum(
        "shqk,shdk->shdq", attention, value_heads, preferred_element_type=jnp.float32
    ).astype(jnp.bfloat16)
    attended = project(context.reshape(local_samples, total_width, cell_count), 3).astype(
        jnp.bfloat16
    )
    returned = lax.all_to_all(attended, "mp", split_axis=1, concat_axis=0, tiled=True)
    final_field = residual + returned.astype(jnp.float32)
    return final_field.astype(jnp.bfloat16)


def solution(mesh):
    in_specs = (
        P(("groups", "dp"), "mp", None),
        P(("groups", "dp"), None, "mp"),
        P("dp", None, "mp"),
        P("dp", None, "mp"),
        P(("groups", "dp"), "mp", None),
        P("dp", None),
        P("dp", None),
        P("groups"),
        P("groups"),
        P("groups"),
    )
    out_specs = P(("groups", "dp"), "mp", None)
    return jax.shard_map(local, mesh=mesh, in_specs=in_specs, out_specs=out_specs, check_vma=False)
```

```python
import jax
import jax.numpy as jnp
from jax import lax
from jax.sharding import PartitionSpec as P

C = 640
GROUPS = 32
HEAD = 64
SIDE = 8


EPSILON = 1e-05
MASKED = -1e30


def norm_groups(values, group_width):
    field_shape = values.shape
    grouped = values.reshape(
        field_shape[0], field_shape[1] // group_width, group_width, field_shape[2]
    )
    center = grouped - jnp.mean(grouped, axis=(2, 3), keepdims=True)
    spread = jnp.mean(center * center, axis=(2, 3), keepdims=True)
    return (center * lax.rsqrt(spread + EPSILON)).reshape(field_shape)


def gather_channels(field):
    return lax.all_gather(field, "mp", axis=1, tiled=True)


def pair_gather_channels(field):
    dense = field.reshape(-1, 128)
    across = lax.ppermute(dense, "mp", [(i, i ^ 2) for i in range(4)])
    beside = lax.ppermute(dense, "mp", [(i, i ^ 1) for i in range(4)])
    relayed = lax.ppermute(across, "mp", [(i, i ^ 1) for i in range(4)])
    parts = [part.reshape(field.shape) for part in (beside, across, relayed)]
    return jnp.concatenate([field] + parts, axis=1)


def line_gather_flat(flat, count):
    my_shard = lax.axis_index("dp")
    rightward = [(i, i + 1) for i in range(count - 1)]
    leftward = [(i + 1, i) for i in range(count - 1)]
    going_right, going_left = flat, flat
    held = [flat]
    from_left, from_right = [], []
    for _ in range(1, count):
        going_right = lax.ppermute(going_right, "dp", rightward)
        going_left = lax.ppermute(going_left, "dp", leftward)
        from_left.append(going_right)
        from_right.append(going_left)
    line = jnp.stack(from_left[::-1] + held + from_right)
    return lax.dynamic_slice_in_dim(line, count - 1 - my_shard, count, axis=0)


def split_line_gather(packed):
    my_shard = lax.axis_index("dp")
    my_group = lax.axis_index("groups")
    halves = packed.reshape(2, packed.shape[0] // 2, packed.shape[1])
    mine = lax.dynamic_index_in_dim(halves, my_group, 0, keepdims=False)
    rightward = [(i, i + 1) for i in range(3)]
    leftward = [(i + 1, i) for i in range(3)]
    swap = [(0, 1), (1, 0)]
    left_1 = lax.ppermute(mine, "dp", rightward)
    right_1 = lax.ppermute(mine, "dp", leftward)
    first_swap = lax.ppermute(jnp.where(my_shard >= 1, left_1, right_1), "groups", swap)
    left_2 = lax.ppermute(left_1, "dp", rightward)
    right_2 = lax.ppermute(right_1, "dp", leftward)
    second_swap = lax.ppermute(jnp.where(my_shard >= 2, left_2, right_2), "groups", swap)
    left_3 = lax.ppermute(left_2, "dp", rightward)
    right_3 = lax.ppermute(right_2, "dp", leftward)
    third_pick = jnp.where(my_shard == 0, right_3, jnp.where(my_shard == 3, left_3, right_1))
    third_swap = lax.ppermute(third_pick, "groups", swap)

    def whole(own_half, other_half):
        lead = jnp.where(my_group == 0, own_half, other_half)
        tail = jnp.where(my_group == 0, other_half, own_half)
        return jnp.concatenate([lead, tail], axis=0)

    line = jnp.stack(
        [
            whole(left_3, third_swap),
            whole(left_2, second_swap),
            whole(left_1, first_swap),
            packed,
            whole(right_1, jnp.where(my_shard == 0, first_swap, third_swap)),
            whole(right_2, second_swap),
            whole(right_3, third_swap),
        ]
    )
    return lax.dynamic_slice_in_dim(line, 3 - my_shard, 4, axis=0)


def xor_spread_samples(field, group):
    my_column = lax.axis_index("mp")
    parts = [lax.dynamic_slice_in_dim(field, my_column * group, group, axis=0)]
    for step in range(1, 4):
        block = lax.dynamic_slice_in_dim(field, (my_column ^ step) * group, group, axis=0)
        moved = lax.ppermute(block.reshape(-1, 128), "mp", [(i, i ^ step) for i in range(4)])
        parts.append(moved.reshape(block.shape))
    return jnp.concatenate(parts, axis=1)


def xor_return_channels(field, width):
    my_column = lax.axis_index("mp")
    parts = [lax.dynamic_slice_in_dim(field, my_column * width, width, axis=1)]
    for step in range(1, 4):
        block = lax.dynamic_slice_in_dim(field, (my_column ^ step) * width, width, axis=1)
        moved = lax.ppermute(block.reshape(-1, 128), "mp", [(i, i ^ step) for i in range(4)])
        parts.append(moved.reshape(block.shape))
    order = jnp.bitwise_xor(jnp.arange(4, dtype=jnp.int32), my_column)
    picked = jnp.take(jnp.stack(parts), order, axis=0, mode="clip")
    return picked.reshape((4 * field.shape[0],) + picked.shape[2:])


def shift_parts(shard, count):
    parts = [shard]
    for step in range(1, count):
        parts.append(lax.ppermute(shard, "dp", [(i, (i + step) % count) for i in range(count)]))
    return jnp.stack(parts)


def order_rows(stacked, wanted_blocks):
    my_shard = lax.axis_index("dp")
    count = stacked.shape[0]
    picked = jnp.take(stacked, (my_shard - wanted_blocks) % count, axis=0, mode="clip")
    return picked.reshape((count * stacked.shape[1],) + stacked.shape[2:])


def gather_kernel(weight_shard):
    return lax.all_gather(weight_shard, "dp", axis=0, tiled=True)


def gather_projection(weight_shard):
    return lax.all_gather(weight_shard, "dp", axis=0, tiled=True)


def apply_kernel(full_field, kernel):
    sample_count = full_field.shape[0]
    out_width = kernel.shape[2]
    tap_images = jnp.einsum("scq,cte->stqe", full_field, kernel, preferred_element_type=jnp.float32)
    tap_images = tap_images.reshape(sample_count, 9, SIDE, SIDE, out_width)
    padded = jnp.pad(tap_images, ((0, 0), (0, 0), (1, 1), (1, 1), (0, 0)))
    running = padded[:, 0, 0:SIDE, 0:SIDE, :]
    for offset in range(1, 9):
        row_shift, col_shift = (offset // 3, offset % 3)
        running = (
            running
            + padded[:, offset, row_shift : row_shift + SIDE, col_shift : col_shift + SIDE, :]
        )
    return jnp.transpose(running.reshape(sample_count, SIDE * SIDE, out_width), (0, 2, 1))


def local(
    latents,
    modulation,
    first_kernel,
    second_kernel,
    encoder_cache,
    query_weight,
    output_weight,
    kept_prompt_list,
    destination,
    lengths,
):
    group_width = C // GROUPS
    dp_count = lax.axis_size("dp")
    mp_count = lax.axis_size("mp")
    my_shard = lax.axis_index("dp")
    my_column = lax.axis_index("mp")
    sample_shard_count = latents.shape[0]
    prompt_dev = encoder_cache.shape[0]
    cache_len = encoder_cache.shape[2]
    cache_width = encoder_cache.shape[1]
    cell_count = latents.shape[2]
    slot_limit = 2 * (sample_shard_count // dp_count)
    all_samples = destination.shape[0]
    owner_target = destination.reshape(dp_count, sample_shard_count)
    positions = jnp.arange(sample_shard_count, dtype=jnp.int32)
    before = positions[None, :] < positions[:, None]
    same_target = owner_target[:, :, None] == owner_target[:, None, :]
    slot_rank = jnp.sum((same_target & before[None]).astype(jnp.int32), axis=2)
    my_target = lax.dynamic_index_in_dim(owner_target, my_shard, 0, keepdims=False)
    my_rank = lax.dynamic_index_in_dim(slot_rank, my_shard, 0, keepdims=False)
    my_prompts = (
        lax.dynamic_slice_in_dim(
            kept_prompt_list, my_shard * sample_shard_count, sample_shard_count
        )
        - my_shard * prompt_dev
    )
    send_slot = my_target * slot_limit + my_rank
    slot_table = send_slot[:, None] == jnp.arange(dp_count * slot_limit, dtype=jnp.int32)[None, :]
    source_row = jnp.sum(jnp.where(slot_table, my_prompts[:, None], 0), axis=0)
    filled = jnp.any(slot_table, axis=0)
    send_rows = jnp.take(encoder_cache, source_row, axis=0)
    send_rows = jnp.where(filled[:, None, None], send_rows, jnp.zeros_like(send_rows))
    outgoing = send_rows.reshape(dp_count, slot_limit, cache_width, cache_len)
    arriving = destination == my_shard
    arrival_pos = jnp.cumsum(arriving.astype(jnp.int32)) - 1
    selector = arriving[None, :] & (arrival_pos[None, :] == positions[:, None])
    kept_prompt = jnp.sum(
        jnp.where(selector, jnp.arange(all_samples, dtype=jnp.int32)[None, :], 0), axis=1
    )
    incoming_order_rank = jnp.sum(jnp.where(selector, slot_rank.reshape(-1)[None, :], 0), axis=1)
    prompt_ids = jnp.sum(jnp.where(selector, kept_prompt_list[None, :], 0), axis=1)
    landing_slot = kept_prompt // sample_shard_count * slot_limit + incoming_order_rank
    prompt_hits = prompt_ids[:, None] == jnp.arange(lengths.shape[0], dtype=jnp.int32)[None, :]
    my_lengths = jnp.sum(jnp.where(prompt_hits, lengths[None, :], 0), axis=1)
    fast = dp_count == 4 and mp_count == 4 and lax.axis_size("groups") == 2
    weight_shards = (first_kernel, second_kernel, query_weight, output_weight)
    if fast:
        block_ids = jnp.arange(dp_count, dtype=jnp.int32)
        channel_blocks = jnp.bitwise_xor(block_ids, my_column)
        pieces = (first_kernel, second_kernel, query_weight, output_weight)
        dense = [piece.reshape(-1, 128) for piece in pieces]
        natural = split_line_gather(jnp.concatenate(dense, axis=0))
        kernel_rows = dense[0].shape[0] + dense[1].shape[0]
        kernel_part = jnp.take(natural[:, :kernel_rows], channel_blocks, axis=0, mode="clip")
        proj_part = natural[:, kernel_rows:]
        full_weights = []
        cut = 0
        query_part = jnp.take(proj_part, channel_blocks, axis=0, mode="clip")
        for piece, block, source in zip(pieces, dense, (kernel_part, kernel_part, query_part, proj_part)):
            if cut == kernel_rows:
                cut = 0
            chunk = source[:, cut : cut + block.shape[0]]
            cut += block.shape[0]
            full_weights.append(chunk.reshape((dp_count * piece.shape[0],) + piece.shape[1:]))
        gathered = (kernel_part, proj_part)
        full_weights = tuple(full_weights)
        outgoing = lax.optimization_barrier((outgoing, gathered))[0]
        spread_channels = pair_gather_channels
    else:
        full_weights = (
            gather_kernel(first_kernel),
            gather_kernel(second_kernel),
            gather_projection(query_weight),
            gather_projection(output_weight),
        )
        spread_channels = gather_channels
    incoming = lax.all_to_all(outgoing, "dp", split_axis=0, concat_axis=0, tiled=True)
    my_pairs = jnp.take(
        incoming.reshape(dp_count * slot_limit, cache_width, cache_len), landing_slot, axis=0
    )
    start_field = latents.astype(jnp.float32)
    activated = jax.nn.silu(norm_groups(start_field, group_width)).astype(jnp.bfloat16)
    first_in = spread_channels(activated)

    def convolve(full_field, which_weight):
        return apply_kernel(full_field, full_weights[which_weight])

    def project(field_rows, which_weight):
        full_weight = full_weights[which_weight]
        return jnp.einsum(
            "scq,ce->seq", field_rows, full_weight, preferred_element_type=jnp.float32
        )

    first_out = convolve(first_in, 0)
    scale_term = modulation[:, 0, :].astype(jnp.float32)[:, :, None]
    shift_term = modulation[:, 1, :].astype(jnp.float32)[:, :, None]
    modulated = jax.nn.silu(
        norm_groups(first_out, group_width) * (1.0 + scale_term) + shift_term
    ).astype(jnp.bfloat16)
    second_in = spread_channels(modulated)
    residual = start_field + convolve(second_in, 1)
    normed_out = norm_groups(residual, group_width).astype(jnp.bfloat16)
    local_samples = sample_shard_count // mp_count
    query_cells, pair_heads = (
        xor_spread_samples(normed_out, local_samples)
        if fast
        else lax.all_to_all(normed_out, "mp", split_axis=0, concat_axis=1, tiled=True),
        lax.all_to_all(my_pairs, "mp", split_axis=0, concat_axis=1, tiled=True),
    )
    total_width = query_cells.shape[1]
    head_count = total_width // HEAD
    queries = project(query_cells, 2).astype(jnp.bfloat16)
    queries = queries.reshape(local_samples, head_count, HEAD, cell_count)
    heads_of_keys = pair_heads[:, :total_width, :].reshape(
        local_samples, head_count, HEAD, cache_len
    )
    value_heads = pair_heads[:, total_width:, :].reshape(local_samples, head_count, HEAD, cache_len)
    scores = jnp.einsum(
        "shdq,shdk->shqk", queries, heads_of_keys, preferred_element_type=jnp.float32
    ) * HEAD ** (-0.5)
    local_lengths = lax.dynamic_slice_in_dim(my_lengths, my_column * local_samples, local_samples)
    visible = (
        jnp.arange(cache_len, dtype=jnp.int32)[None, None, None, :]
        < local_lengths[:, None, None, None]
    )
    scores = jnp.where(visible, scores, MASKED)
    row_peak = jnp.max(scores, axis=3, keepdims=True)
    exponent = jnp.exp(scores - row_peak)
    attention = (exponent / jnp.sum(exponent, axis=3, keepdims=True)).astype(jnp.bfloat16)
    context = jnp.einsum(
        "shqk,shdk->shdq", attention, value_heads, preferred_element_type=jnp.float32
    ).astype(jnp.bfloat16)
    attended = project(context.reshape(local_samples, total_width, cell_count), 3).astype(
        jnp.bfloat16
    )
    if fast:
        returned = xor_return_channels(attended, attended.shape[1] // mp_count)
    else:
        returned = lax.all_to_all(attended, "mp", split_axis=1, concat_axis=0, tiled=True)
    final_field = residual + returned.astype(jnp.float32)
    return final_field.astype(jnp.bfloat16)


def solution(mesh):
    in_specs = (
        P(("groups", "dp"), "mp", None),
        P(("groups", "dp"), None, "mp"),
        P("dp", None, "mp"),
        P("dp", None, "mp"),
        P(("groups", "dp"), "mp", None),
        P("dp", None),
        P("dp", None),
        P("groups"),
        P("groups"),
        P("groups"),
    )
    out_specs = P(("groups", "dp"), "mp", None)
    return jax.shard_map(local, mesh=mesh, in_specs=in_specs, out_specs=out_specs, check_vma=False)
```

```python
import jax
import jax.numpy as jnp
from jax import lax
from jax.sharding import PartitionSpec as P

C = 640
GROUPS = 32
HEAD = 64
SIDE = 8


EPSILON = 1e-05
MASKED = -1e30


def norm_groups(values, group_width):
    field_shape = values.shape
    grouped = values.reshape(
        field_shape[0], field_shape[1] // group_width, group_width, field_shape[2]
    )
    center = grouped - jnp.mean(grouped, axis=(2, 3), keepdims=True)
    spread = jnp.mean(center * center, axis=(2, 3), keepdims=True)
    return (center * lax.rsqrt(spread + EPSILON)).reshape(field_shape)


def gather_channels(field):
    return lax.all_gather(field, "mp", axis=1, tiled=True)


def pair_gather_channels(field):
    cell_major = jnp.transpose(field, (0, 2, 1))
    dense = cell_major.reshape(-1, 128)
    across = lax.ppermute(dense, "mp", [(i, i ^ 2) for i in range(4)])
    beside = lax.ppermute(dense, "mp", [(i, i ^ 1) for i in range(4)])
    relayed = lax.ppermute(across, "mp", [(i, i ^ 1) for i in range(4)])
    parts = [part.reshape(cell_major.shape) for part in (beside, across, relayed)]
    return jnp.concatenate([cell_major] + parts, axis=2)


def gather_channels_last(field):
    return jnp.transpose(gather_channels(field), (0, 2, 1))


def line_gather_flat(flat, count):
    my_shard = lax.axis_index("dp")
    rightward = [(i, i + 1) for i in range(count - 1)]
    leftward = [(i + 1, i) for i in range(count - 1)]
    going_right, going_left = flat, flat
    held = [flat]
    from_left, from_right = [], []
    for _ in range(1, count):
        going_right = lax.ppermute(going_right, "dp", rightward)
        going_left = lax.ppermute(going_left, "dp", leftward)
        from_left.append(going_right)
        from_right.append(going_left)
    line = jnp.stack(from_left[::-1] + held + from_right)
    return lax.dynamic_slice_in_dim(line, count - 1 - my_shard, count, axis=0)


def split_line_gather(packed):
    my_shard = lax.axis_index("dp")
    my_group = lax.axis_index("groups")
    halves = packed.reshape(2, packed.shape[0] // 2, packed.shape[1])
    mine = lax.dynamic_index_in_dim(halves, my_group, 0, keepdims=False)
    rightward = [(i, i + 1) for i in range(3)]
    leftward = [(i + 1, i) for i in range(3)]
    swap = [(0, 1), (1, 0)]
    left_1 = lax.ppermute(mine, "dp", rightward)
    right_1 = lax.ppermute(mine, "dp", leftward)
    first_swap = lax.ppermute(jnp.where(my_shard >= 1, left_1, right_1), "groups", swap)
    left_2 = lax.ppermute(left_1, "dp", rightward)
    right_2 = lax.ppermute(right_1, "dp", leftward)
    second_swap = lax.ppermute(jnp.where(my_shard >= 2, left_2, right_2), "groups", swap)
    left_3 = lax.ppermute(left_2, "dp", rightward)
    right_3 = lax.ppermute(right_2, "dp", leftward)
    third_pick = jnp.where(my_shard == 0, right_3, jnp.where(my_shard == 3, left_3, right_1))
    third_swap = lax.ppermute(third_pick, "groups", swap)

    def whole(own_half, other_half):
        lead = jnp.where(my_group == 0, own_half, other_half)
        tail = jnp.where(my_group == 0, other_half, own_half)
        return jnp.concatenate([lead, tail], axis=0)

    line = [
        whole(left_3, third_swap),
        whole(left_2, second_swap),
        whole(left_1, first_swap),
        packed,
        whole(right_1, jnp.where(my_shard == 0, first_swap, third_swap)),
        whole(right_2, second_swap),
        whole(right_3, third_swap),
    ]
    natural = []
    for block in range(4):
        picked = line[block]
        for shard in range(1, 4):
            picked = jnp.where(my_shard == 3 - shard, line[block + shard], picked)
        natural.append(picked)
    return jnp.stack(natural)


def xor_spread_samples(field, group):
    my_column = lax.axis_index("mp")
    parts = [lax.dynamic_slice_in_dim(field, my_column * group, group, axis=0)]
    for step in range(1, 4):
        block = lax.dynamic_slice_in_dim(field, (my_column ^ step) * group, group, axis=0)
        moved = lax.ppermute(block.reshape(-1, 128), "mp", [(i, i ^ step) for i in range(4)])
        parts.append(moved.reshape(block.shape))
    return jnp.concatenate(parts, axis=1)


def xor_return_channels(field, width):
    my_column = lax.axis_index("mp")
    parts = [lax.dynamic_slice_in_dim(field, my_column * width, width, axis=1)]
    for step in range(1, 4):
        block = lax.dynamic_slice_in_dim(field, (my_column ^ step) * width, width, axis=1)
        moved = lax.ppermute(block.reshape(-1, 128), "mp", [(i, i ^ step) for i in range(4)])
        parts.append(moved.reshape(block.shape))
    order = jnp.bitwise_xor(jnp.arange(4, dtype=jnp.int32), my_column)
    picked = jnp.take(jnp.stack(parts), order, axis=0, mode="clip")
    return picked.reshape((4 * field.shape[0],) + picked.shape[2:])


def shift_parts(shard, count):
    parts = [shard]
    for step in range(1, count):
        parts.append(lax.ppermute(shard, "dp", [(i, (i + step) % count) for i in range(count)]))
    return jnp.stack(parts)


def order_rows(stacked, wanted_blocks):
    my_shard = lax.axis_index("dp")
    count = stacked.shape[0]
    picked = jnp.take(stacked, (my_shard - wanted_blocks) % count, axis=0, mode="clip")
    return picked.reshape((count * stacked.shape[1],) + stacked.shape[2:])


def gather_kernel(weight_shard):
    return lax.all_gather(weight_shard, "dp", axis=0, tiled=True)


def gather_projection(weight_shard):
    return lax.all_gather(weight_shard, "dp", axis=0, tiled=True)


def apply_kernel(full_field, kernel):
    sample_count = full_field.shape[0]
    out_width = kernel.shape[2]
    tap_images = jnp.einsum("sqc,cte->stqe", full_field, kernel, preferred_element_type=jnp.float32)
    tap_images = tap_images.reshape(sample_count, 9, SIDE, SIDE, out_width)
    padded = jnp.pad(tap_images, ((0, 0), (0, 0), (1, 1), (1, 1), (0, 0)))
    running = padded[:, 0, 0:SIDE, 0:SIDE, :]
    for offset in range(1, 9):
        row_shift, col_shift = (offset // 3, offset % 3)
        running = (
            running
            + padded[:, offset, row_shift : row_shift + SIDE, col_shift : col_shift + SIDE, :]
        )
    return jnp.transpose(running.reshape(sample_count, SIDE * SIDE, out_width), (0, 2, 1))


def local(
    latents,
    modulation,
    first_kernel,
    second_kernel,
    encoder_cache,
    query_weight,
    output_weight,
    kept_prompt_list,
    destination,
    lengths,
):
    group_width = C // GROUPS
    dp_count = lax.axis_size("dp")
    mp_count = lax.axis_size("mp")
    my_shard = lax.axis_index("dp")
    my_column = lax.axis_index("mp")
    sample_shard_count = latents.shape[0]
    prompt_dev = encoder_cache.shape[0]
    cache_len = encoder_cache.shape[2]
    cache_width = encoder_cache.shape[1]
    cell_count = latents.shape[2]
    slot_limit = 2 * (sample_shard_count // dp_count)
    all_samples = destination.shape[0]
    owner_target = destination.reshape(dp_count, sample_shard_count)
    positions = jnp.arange(sample_shard_count, dtype=jnp.int32)
    before = positions[None, :] < positions[:, None]
    same_target = owner_target[:, :, None] == owner_target[:, None, :]
    slot_rank = jnp.sum((same_target & before[None]).astype(jnp.int32), axis=2)
    my_target = lax.dynamic_index_in_dim(owner_target, my_shard, 0, keepdims=False)
    my_rank = lax.dynamic_index_in_dim(slot_rank, my_shard, 0, keepdims=False)
    my_prompts = (
        lax.dynamic_slice_in_dim(
            kept_prompt_list, my_shard * sample_shard_count, sample_shard_count
        )
        - my_shard * prompt_dev
    )
    send_slot = my_target * slot_limit + my_rank
    slot_table = send_slot[:, None] == jnp.arange(dp_count * slot_limit, dtype=jnp.int32)[None, :]
    source_row = jnp.sum(jnp.where(slot_table, my_prompts[:, None], 0), axis=0)
    filled = jnp.any(slot_table, axis=0)
    send_rows = jnp.take(encoder_cache, source_row, axis=0)
    send_rows = jnp.where(filled[:, None, None], send_rows, jnp.zeros_like(send_rows))
    outgoing = send_rows.reshape(dp_count, slot_limit, cache_width, cache_len)
    arriving = destination == my_shard
    arrival_pos = jnp.cumsum(arriving.astype(jnp.int32)) - 1
    selector = arriving[None, :] & (arrival_pos[None, :] == positions[:, None])
    kept_prompt = jnp.sum(
        jnp.where(selector, jnp.arange(all_samples, dtype=jnp.int32)[None, :], 0), axis=1
    )
    incoming_order_rank = jnp.sum(jnp.where(selector, slot_rank.reshape(-1)[None, :], 0), axis=1)
    prompt_ids = jnp.sum(jnp.where(selector, kept_prompt_list[None, :], 0), axis=1)
    landing_slot = kept_prompt // sample_shard_count * slot_limit + incoming_order_rank
    prompt_hits = prompt_ids[:, None] == jnp.arange(lengths.shape[0], dtype=jnp.int32)[None, :]
    my_lengths = jnp.sum(jnp.where(prompt_hits, lengths[None, :], 0), axis=1)
    fast = dp_count == 4 and mp_count == 4 and lax.axis_size("groups") == 2
    weight_shards = (first_kernel, second_kernel, query_weight, output_weight)
    if fast:
        block_ids = jnp.arange(dp_count, dtype=jnp.int32)
        channel_blocks = jnp.bitwise_xor(block_ids, my_column)
        pieces = (first_kernel, second_kernel, query_weight, output_weight)
        dense = [piece.reshape(-1, 128) for piece in pieces]
        natural = split_line_gather(jnp.concatenate(dense, axis=0))
        kernel_rows = dense[0].shape[0] + dense[1].shape[0]
        kernel_part = jnp.take(natural[:, :kernel_rows], channel_blocks, axis=0, mode="clip")
        proj_part = natural[:, kernel_rows:]
        full_weights = []
        cut = 0
        query_part = jnp.take(proj_part, channel_blocks, axis=0, mode="clip")
        for piece, block, source in zip(pieces, dense, (kernel_part, kernel_part, query_part, proj_part)):
            if cut == kernel_rows:
                cut = 0
            chunk = source[:, cut : cut + block.shape[0]]
            cut += block.shape[0]
            full_weights.append(chunk.reshape((dp_count * piece.shape[0],) + piece.shape[1:]))
        gathered = (kernel_part, proj_part)
        full_weights = tuple(full_weights)
        outgoing = lax.optimization_barrier((outgoing, gathered))[0]
        spread_channels = pair_gather_channels
    else:
        full_weights = (
            gather_kernel(first_kernel),
            gather_kernel(second_kernel),
            gather_projection(query_weight),
            gather_projection(output_weight),
        )
        spread_channels = gather_channels_last
    incoming = lax.all_to_all(outgoing, "dp", split_axis=0, concat_axis=0, tiled=True)
    my_pairs = jnp.take(
        incoming.reshape(dp_count * slot_limit, cache_width, cache_len), landing_slot, axis=0
    )
    start_field = latents.astype(jnp.float32)
    activated = jax.nn.silu(norm_groups(start_field, group_width)).astype(jnp.bfloat16)
    first_in = spread_channels(activated)

    def convolve(full_field, which_weight):
        return apply_kernel(full_field, full_weights[which_weight])

    def project(field_rows, which_weight):
        full_weight = full_weights[which_weight]
        return jnp.einsum(
            "scq,ce->seq", field_rows, full_weight, preferred_element_type=jnp.float32
        )

    first_out = convolve(first_in, 0)
    scale_term = modulation[:, 0, :].astype(jnp.float32)[:, :, None]
    shift_term = modulation[:, 1, :].astype(jnp.float32)[:, :, None]
    modulated = jax.nn.silu(
        norm_groups(first_out, group_width) * (1.0 + scale_term) + shift_term
    ).astype(jnp.bfloat16)
    second_in = spread_channels(modulated)
    residual = start_field + convolve(second_in, 1)
    normed_out = norm_groups(residual, group_width).astype(jnp.bfloat16)
    local_samples = sample_shard_count // mp_count
    query_cells, pair_heads = (
        xor_spread_samples(normed_out, local_samples)
        if fast
        else lax.all_to_all(normed_out, "mp", split_axis=0, concat_axis=1, tiled=True),
        lax.all_to_all(my_pairs, "mp", split_axis=0, concat_axis=1, tiled=True),
    )
    total_width = query_cells.shape[1]
    head_count = total_width // HEAD
    queries = project(query_cells, 2).astype(jnp.bfloat16)
    queries = queries.reshape(local_samples, head_count, HEAD, cell_count)
    heads_of_keys = pair_heads[:, :total_width, :].reshape(
        local_samples, head_count, HEAD, cache_len
    )
    value_heads = pair_heads[:, total_width:, :].reshape(local_samples, head_count, HEAD, cache_len)
    scores = jnp.einsum(
        "shdq,shdk->shqk", queries, heads_of_keys, preferred_element_type=jnp.float32
    ) * HEAD ** (-0.5)
    local_lengths = lax.dynamic_slice_in_dim(my_lengths, my_column * local_samples, local_samples)
    visible = (
        jnp.arange(cache_len, dtype=jnp.int32)[None, None, None, :]
        < local_lengths[:, None, None, None]
    )
    scores = jnp.where(visible, scores, MASKED)
    row_peak = jnp.max(scores, axis=3, keepdims=True)
    exponent = jnp.exp(scores - row_peak)
    attention = (exponent / jnp.sum(exponent, axis=3, keepdims=True)).astype(jnp.bfloat16)
    context = jnp.einsum(
        "shqk,shdk->shdq", attention, value_heads, preferred_element_type=jnp.float32
    ).astype(jnp.bfloat16)
    attended = project(context.reshape(local_samples, total_width, cell_count), 3).astype(
        jnp.bfloat16
    )
    if fast:
        returned = xor_return_channels(attended, attended.shape[1] // mp_count)
    else:
        returned = lax.all_to_all(attended, "mp", split_axis=1, concat_axis=0, tiled=True)
    final_field = residual + returned.astype(jnp.float32)
    return final_field.astype(jnp.bfloat16)


def solution(mesh):
    in_specs = (
        P(("groups", "dp"), "mp", None),
        P(("groups", "dp"), None, "mp"),
        P("dp", None, "mp"),
        P("dp", None, "mp"),
        P(("groups", "dp"), "mp", None),
        P("dp", None),
        P("dp", None),
        P("groups"),
        P("groups"),
        P("groups"),
    )
    out_specs = P(("groups", "dp"), "mp", None)
    return jax.shard_map(local, mesh=mesh, in_specs=in_specs, out_specs=out_specs, check_vma=False)
```

```python
import jax
import jax.numpy as jnp
from jax import lax
from jax.sharding import PartitionSpec as P

C = 640
GROUPS = 32
HEAD = 64
SIDE = 8


EPSILON = 1e-05
MASKED = -1e30


def norm_groups(values, group_width):
    field_shape = values.shape
    grouped = values.reshape(
        field_shape[0], field_shape[1] // group_width, group_width, field_shape[2]
    )
    center = grouped - jnp.mean(grouped, axis=(2, 3), keepdims=True)
    spread = jnp.mean(center * center, axis=(2, 3), keepdims=True)
    return (center * lax.rsqrt(spread + EPSILON)).reshape(field_shape)


def gather_channels(field):
    return lax.all_gather(field, "mp", axis=1, tiled=True)


def pair_gather_channels(field):
    dense = field.reshape(-1, 128)
    across = lax.ppermute(dense, "mp", [(i, i ^ 2) for i in range(4)])
    beside = lax.ppermute(dense, "mp", [(i, i ^ 1) for i in range(4)])
    relayed = lax.ppermute(across, "mp", [(i, i ^ 1) for i in range(4)])
    parts = [part.reshape(field.shape) for part in (beside, across, relayed)]
    return jnp.concatenate([field] + parts, axis=1)


def line_gather_flat(flat, count):
    my_shard = lax.axis_index("dp")
    rightward = [(i, i + 1) for i in range(count - 1)]
    leftward = [(i + 1, i) for i in range(count - 1)]
    going_right, going_left = flat, flat
    held = [flat]
    from_left, from_right = [], []
    for _ in range(1, count):
        going_right = lax.ppermute(going_right, "dp", rightward)
        going_left = lax.ppermute(going_left, "dp", leftward)
        from_left.append(going_right)
        from_right.append(going_left)
    line = jnp.stack(from_left[::-1] + held + from_right)
    return lax.dynamic_slice_in_dim(line, count - 1 - my_shard, count, axis=0)


def split_line_gather(packed, gated):
    my_shard = lax.axis_index("dp")
    my_group = lax.axis_index("groups")
    halves = packed.reshape(2, packed.shape[0] // 2, packed.shape[1])
    mine = lax.dynamic_index_in_dim(halves, my_group, 0, keepdims=False)
    mine, gated = lax.optimization_barrier((mine, gated))
    rightward = [(i, i + 1) for i in range(3)]
    leftward = [(i + 1, i) for i in range(3)]
    swap = [(0, 1), (1, 0)]
    left_1 = lax.ppermute(mine, "dp", rightward)
    right_1 = lax.ppermute(mine, "dp", leftward)
    first_swap = lax.ppermute(jnp.where(my_shard >= 1, left_1, right_1), "groups", swap)
    left_2 = lax.ppermute(left_1, "dp", rightward)
    right_2 = lax.ppermute(right_1, "dp", leftward)
    second_swap = lax.ppermute(jnp.where(my_shard >= 2, left_2, right_2), "groups", swap)
    left_3 = lax.ppermute(left_2, "dp", rightward)
    right_3 = lax.ppermute(right_2, "dp", leftward)
    third_pick = jnp.where(my_shard == 0, right_3, jnp.where(my_shard == 3, left_3, right_1))
    third_swap = lax.ppermute(third_pick, "groups", swap)

    def whole(own_half, other_half):
        lead = jnp.where(my_group == 0, own_half, other_half)
        tail = jnp.where(my_group == 0, other_half, own_half)
        return jnp.concatenate([lead, tail], axis=0)

    line = jnp.stack(
        [
            whole(left_3, third_swap),
            whole(left_2, second_swap),
            whole(left_1, first_swap),
            packed,
            whole(right_1, jnp.where(my_shard == 0, first_swap, third_swap)),
            whole(right_2, second_swap),
            whole(right_3, third_swap),
        ]
    )
    return lax.dynamic_slice_in_dim(line, 3 - my_shard, 4, axis=0), gated


def xor_spread_samples(field, group):
    my_column = lax.axis_index("mp")
    parts = [lax.dynamic_slice_in_dim(field, my_column * group, group, axis=0)]
    for step in range(1, 4):
        block = lax.dynamic_slice_in_dim(field, (my_column ^ step) * group, group, axis=0)
        moved = lax.ppermute(block.reshape(-1, 128), "mp", [(i, i ^ step) for i in range(4)])
        parts.append(moved.reshape(block.shape))
    return jnp.concatenate(parts, axis=1)


def xor_return_channels(field, width):
    my_column = lax.axis_index("mp")
    parts = [lax.dynamic_slice_in_dim(field, my_column * width, width, axis=1)]
    for step in range(1, 4):
        block = lax.dynamic_slice_in_dim(field, (my_column ^ step) * width, width, axis=1)
        moved = lax.ppermute(block.reshape(-1, 128), "mp", [(i, i ^ step) for i in range(4)])
        parts.append(moved.reshape(block.shape))
    order = jnp.bitwise_xor(jnp.arange(4, dtype=jnp.int32), my_column)
    picked = jnp.take(jnp.stack(parts), order, axis=0, mode="clip")
    return picked.reshape((4 * field.shape[0],) + picked.shape[2:])


def shift_parts(shard, count):
    parts = [shard]
    for step in range(1, count):
        parts.append(lax.ppermute(shard, "dp", [(i, (i + step) % count) for i in range(count)]))
    return jnp.stack(parts)


def order_rows(stacked, wanted_blocks):
    my_shard = lax.axis_index("dp")
    count = stacked.shape[0]
    picked = jnp.take(stacked, (my_shard - wanted_blocks) % count, axis=0, mode="clip")
    return picked.reshape((count * stacked.shape[1],) + stacked.shape[2:])


def gather_kernel(weight_shard):
    return lax.all_gather(weight_shard, "dp", axis=0, tiled=True)


def gather_projection(weight_shard):
    return lax.all_gather(weight_shard, "dp", axis=0, tiled=True)


def apply_kernel(full_field, kernel):
    sample_count = full_field.shape[0]
    out_width = kernel.shape[2]
    tap_images = jnp.einsum("scq,cte->stqe", full_field, kernel, preferred_element_type=jnp.float32)
    tap_images = tap_images.reshape(sample_count, 9, SIDE, SIDE, out_width)
    padded = jnp.pad(tap_images, ((0, 0), (0, 0), (1, 1), (1, 1), (0, 0)))
    running = padded[:, 0, 0:SIDE, 0:SIDE, :]
    for offset in range(1, 9):
        row_shift, col_shift = (offset // 3, offset % 3)
        running = (
            running
            + padded[:, offset, row_shift : row_shift + SIDE, col_shift : col_shift + SIDE, :]
        )
    return jnp.transpose(running.reshape(sample_count, SIDE * SIDE, out_width), (0, 2, 1))


def local(
    latents,
    modulation,
    first_kernel,
    second_kernel,
    encoder_cache,
    query_weight,
    output_weight,
    kept_prompt_list,
    destination,
    lengths,
):
    group_width = C // GROUPS
    dp_count = lax.axis_size("dp")
    mp_count = lax.axis_size("mp")
    my_shard = lax.axis_index("dp")
    my_column = lax.axis_index("mp")
    sample_shard_count = latents.shape[0]
    prompt_dev = encoder_cache.shape[0]
    cache_len = encoder_cache.shape[2]
    cache_width = encoder_cache.shape[1]
    cell_count = latents.shape[2]
    slot_limit = 2 * (sample_shard_count // dp_count)
    all_samples = destination.shape[0]
    owner_target = destination.reshape(dp_count, sample_shard_count)
    positions = jnp.arange(sample_shard_count, dtype=jnp.int32)
    before = positions[None, :] < positions[:, None]
    same_target = owner_target[:, :, None] == owner_target[:, None, :]
    slot_rank = jnp.sum((same_target & before[None]).astype(jnp.int32), axis=2)
    my_target = lax.dynamic_index_in_dim(owner_target, my_shard, 0, keepdims=False)
    my_rank = lax.dynamic_index_in_dim(slot_rank, my_shard, 0, keepdims=False)
    my_prompts = (
        lax.dynamic_slice_in_dim(
            kept_prompt_list, my_shard * sample_shard_count, sample_shard_count
        )
        - my_shard * prompt_dev
    )
    send_slot = my_target * slot_limit + my_rank
    slot_table = send_slot[:, None] == jnp.arange(dp_count * slot_limit, dtype=jnp.int32)[None, :]
    source_row = jnp.sum(jnp.where(slot_table, my_prompts[:, None], 0), axis=0)
    filled = jnp.any(slot_table, axis=0)
    send_rows = jnp.take(encoder_cache, source_row, axis=0)
    send_rows = jnp.where(filled[:, None, None], send_rows, jnp.zeros_like(send_rows))
    outgoing = send_rows.reshape(dp_count, slot_limit, cache_width, cache_len)
    arriving = destination == my_shard
    arrival_pos = jnp.cumsum(arriving.astype(jnp.int32)) - 1
    selector = arriving[None, :] & (arrival_pos[None, :] == positions[:, None])
    kept_prompt = jnp.sum(
        jnp.where(selector, jnp.arange(all_samples, dtype=jnp.int32)[None, :], 0), axis=1
    )
    incoming_order_rank = jnp.sum(jnp.where(selector, slot_rank.reshape(-1)[None, :], 0), axis=1)
    prompt_ids = jnp.sum(jnp.where(selector, kept_prompt_list[None, :], 0), axis=1)
    landing_slot = kept_prompt // sample_shard_count * slot_limit + incoming_order_rank
    prompt_hits = prompt_ids[:, None] == jnp.arange(lengths.shape[0], dtype=jnp.int32)[None, :]
    my_lengths = jnp.sum(jnp.where(prompt_hits, lengths[None, :], 0), axis=1)
    fast = dp_count == 4 and mp_count == 4 and lax.axis_size("groups") == 2
    weight_shards = (first_kernel, second_kernel, query_weight, output_weight)
    if fast:
        block_ids = jnp.arange(dp_count, dtype=jnp.int32)
        channel_blocks = jnp.bitwise_xor(block_ids, my_column)
        pieces = (first_kernel, second_kernel, query_weight, output_weight)
        dense = [piece.reshape(-1, 128) for piece in pieces]
        natural, latents = split_line_gather(jnp.concatenate(dense, axis=0), latents)
        kernel_rows = dense[0].shape[0] + dense[1].shape[0]
        kernel_part = jnp.take(natural[:, :kernel_rows], channel_blocks, axis=0, mode="clip")
        proj_part = natural[:, kernel_rows:]
        full_weights = []
        cut = 0
        query_part = jnp.take(proj_part, channel_blocks, axis=0, mode="clip")
        for piece, block, source in zip(pieces, dense, (kernel_part, kernel_part, query_part, proj_part)):
            if cut == kernel_rows:
                cut = 0
            chunk = source[:, cut : cut + block.shape[0]]
            cut += block.shape[0]
            full_weights.append(chunk.reshape((dp_count * piece.shape[0],) + piece.shape[1:]))
        gathered = (kernel_part, proj_part)
        full_weights = tuple(full_weights)
        outgoing = lax.optimization_barrier((outgoing, gathered))[0]
        spread_channels = pair_gather_channels
    else:
        full_weights = (
            gather_kernel(first_kernel),
            gather_kernel(second_kernel),
            gather_projection(query_weight),
            gather_projection(output_weight),
        )
        spread_channels = gather_channels
    incoming = lax.all_to_all(outgoing, "dp", split_axis=0, concat_axis=0, tiled=True)
    my_pairs = jnp.take(
        incoming.reshape(dp_count * slot_limit, cache_width, cache_len), landing_slot, axis=0
    )
    start_field = latents.astype(jnp.float32)
    activated = jax.nn.silu(norm_groups(start_field, group_width)).astype(jnp.bfloat16)
    first_in = spread_channels(activated)

    def convolve(full_field, which_weight):
        return apply_kernel(full_field, full_weights[which_weight])

    def project(field_rows, which_weight):
        full_weight = full_weights[which_weight]
        return jnp.einsum(
            "scq,ce->seq", field_rows, full_weight, preferred_element_type=jnp.float32
        )

    first_out = convolve(first_in, 0)
    scale_term = modulation[:, 0, :].astype(jnp.float32)[:, :, None]
    shift_term = modulation[:, 1, :].astype(jnp.float32)[:, :, None]
    modulated = jax.nn.silu(
        norm_groups(first_out, group_width) * (1.0 + scale_term) + shift_term
    ).astype(jnp.bfloat16)
    second_in = spread_channels(modulated)
    residual = start_field + convolve(second_in, 1)
    normed_out = norm_groups(residual, group_width).astype(jnp.bfloat16)
    local_samples = sample_shard_count // mp_count
    query_cells, pair_heads = (
        xor_spread_samples(normed_out, local_samples)
        if fast
        else lax.all_to_all(normed_out, "mp", split_axis=0, concat_axis=1, tiled=True),
        lax.all_to_all(my_pairs, "mp", split_axis=0, concat_axis=1, tiled=True),
    )
    total_width = query_cells.shape[1]
    head_count = total_width // HEAD
    queries = project(query_cells, 2).astype(jnp.bfloat16)
    queries = queries.reshape(local_samples, head_count, HEAD, cell_count)
    heads_of_keys = pair_heads[:, :total_width, :].reshape(
        local_samples, head_count, HEAD, cache_len
    )
    value_heads = pair_heads[:, total_width:, :].reshape(local_samples, head_count, HEAD, cache_len)
    scores = jnp.einsum(
        "shdq,shdk->shqk", queries, heads_of_keys, preferred_element_type=jnp.float32
    ) * HEAD ** (-0.5)
    local_lengths = lax.dynamic_slice_in_dim(my_lengths, my_column * local_samples, local_samples)
    visible = (
        jnp.arange(cache_len, dtype=jnp.int32)[None, None, None, :]
        < local_lengths[:, None, None, None]
    )
    scores = jnp.where(visible, scores, MASKED)
    row_peak = jnp.max(scores, axis=3, keepdims=True)
    exponent = jnp.exp(scores - row_peak)
    attention = (exponent / jnp.sum(exponent, axis=3, keepdims=True)).astype(jnp.bfloat16)
    context = jnp.einsum(
        "shqk,shdk->shdq", attention, value_heads, preferred_element_type=jnp.float32
    ).astype(jnp.bfloat16)
    attended = project(context.reshape(local_samples, total_width, cell_count), 3).astype(
        jnp.bfloat16
    )
    if fast:
        returned = xor_return_channels(attended, attended.shape[1] // mp_count)
    else:
        returned = lax.all_to_all(attended, "mp", split_axis=1, concat_axis=0, tiled=True)
    final_field = residual + returned.astype(jnp.float32)
    return final_field.astype(jnp.bfloat16)


def solution(mesh):
    in_specs = (
        P(("groups", "dp"), "mp", None),
        P(("groups", "dp"), None, "mp"),
        P("dp", None, "mp"),
        P("dp", None, "mp"),
        P(("groups", "dp"), "mp", None),
        P("dp", None),
        P("dp", None),
        P("groups"),
        P("groups"),
        P("groups"),
    )
    out_specs = P(("groups", "dp"), "mp", None)
    return jax.shard_map(local, mesh=mesh, in_specs=in_specs, out_specs=out_specs, check_vma=False)
```

```python
import jax
import jax.numpy as jnp
from jax import lax
from jax.sharding import PartitionSpec as P

C = 640
GROUPS = 32
HEAD = 64
SIDE = 8


EPSILON = 1e-05
MASKED = -1e30


def norm_groups(values, group_width):
    field_shape = values.shape
    grouped = values.reshape(
        field_shape[0], field_shape[1] // group_width, group_width, field_shape[2]
    )
    center = grouped - jnp.mean(grouped, axis=(2, 3), keepdims=True)
    spread = jnp.mean(center * center, axis=(2, 3), keepdims=True)
    return (center * lax.rsqrt(spread + EPSILON)).reshape(field_shape)


def gather_channels(field):
    return lax.all_gather(field, "mp", axis=1, tiled=True)


def pair_gather_channels(field, lane_dense=True):
    dense = field.reshape(-1, 128) if lane_dense else field
    across = lax.ppermute(dense, "mp", [(i, i ^ 2) for i in range(4)])
    beside = lax.ppermute(dense, "mp", [(i, i ^ 1) for i in range(4)])
    relayed = lax.ppermute(across, "mp", [(i, i ^ 1) for i in range(4)])
    parts = [part.reshape(field.shape) for part in (beside, across, relayed)]
    return jnp.concatenate([field] + parts, axis=1)


def line_gather_flat(flat, count):
    my_shard = lax.axis_index("dp")
    rightward = [(i, i + 1) for i in range(count - 1)]
    leftward = [(i + 1, i) for i in range(count - 1)]
    going_right, going_left = flat, flat
    held = [flat]
    from_left, from_right = [], []
    for _ in range(1, count):
        going_right = lax.ppermute(going_right, "dp", rightward)
        going_left = lax.ppermute(going_left, "dp", leftward)
        from_left.append(going_right)
        from_right.append(going_left)
    line = jnp.stack(from_left[::-1] + held + from_right)
    return lax.dynamic_slice_in_dim(line, count - 1 - my_shard, count, axis=0)


def split_line_gather(packed, gated):
    my_shard = lax.axis_index("dp")
    my_group = lax.axis_index("groups")
    halves = packed.reshape(2, packed.shape[0] // 2, packed.shape[1])
    mine = lax.dynamic_index_in_dim(halves, my_group, 0, keepdims=False)
    mine, gated = lax.optimization_barrier((mine, gated))
    rightward = [(i, i + 1) for i in range(3)]
    leftward = [(i + 1, i) for i in range(3)]
    swap = [(0, 1), (1, 0)]
    left_1 = lax.ppermute(mine, "dp", rightward)
    right_1 = lax.ppermute(mine, "dp", leftward)
    first_swap = lax.ppermute(jnp.where(my_shard >= 1, left_1, right_1), "groups", swap)
    left_2 = lax.ppermute(left_1, "dp", rightward)
    right_2 = lax.ppermute(right_1, "dp", leftward)
    second_swap = lax.ppermute(jnp.where(my_shard >= 2, left_2, right_2), "groups", swap)
    left_3 = lax.ppermute(left_2, "dp", rightward)
    right_3 = lax.ppermute(right_2, "dp", leftward)
    third_pick = jnp.where(my_shard == 0, right_3, jnp.where(my_shard == 3, left_3, right_1))
    third_swap = lax.ppermute(third_pick, "groups", swap)

    def whole(own_half, other_half):
        lead = jnp.where(my_group == 0, own_half, other_half)
        tail = jnp.where(my_group == 0, other_half, own_half)
        return jnp.concatenate([lead, tail], axis=0)

    line = jnp.stack(
        [
            whole(left_3, third_swap),
            whole(left_2, second_swap),
            whole(left_1, first_swap),
            packed,
            whole(right_1, jnp.where(my_shard == 0, first_swap, third_swap)),
            whole(right_2, second_swap),
            whole(right_3, third_swap),
        ]
    )
    return lax.dynamic_slice_in_dim(line, 3 - my_shard, 4, axis=0), gated


def xor_spread_samples(field, group):
    my_column = lax.axis_index("mp")
    parts = [lax.dynamic_slice_in_dim(field, my_column * group, group, axis=0)]
    for step in range(1, 4):
        block = lax.dynamic_slice_in_dim(field, (my_column ^ step) * group, group, axis=0)
        moved = lax.ppermute(block.reshape(-1, 128), "mp", [(i, i ^ step) for i in range(4)])
        parts.append(moved.reshape(block.shape))
    return jnp.concatenate(parts, axis=1)


def xor_return_channels(field, width):
    my_column = lax.axis_index("mp")
    parts = [lax.dynamic_slice_in_dim(field, my_column * width, width, axis=1)]
    for step in range(1, 4):
        block = lax.dynamic_slice_in_dim(field, (my_column ^ step) * width, width, axis=1)
        moved = lax.ppermute(block.reshape(-1, 128), "mp", [(i, i ^ step) for i in range(4)])
        parts.append(moved.reshape(block.shape))
    order = jnp.bitwise_xor(jnp.arange(4, dtype=jnp.int32), my_column)
    picked = jnp.take(jnp.stack(parts), order, axis=0, mode="clip")
    return picked.reshape((4 * field.shape[0],) + picked.shape[2:])


def shift_parts(shard, count):
    parts = [shard]
    for step in range(1, count):
        parts.append(lax.ppermute(shard, "dp", [(i, (i + step) % count) for i in range(count)]))
    return jnp.stack(parts)


def order_rows(stacked, wanted_blocks):
    my_shard = lax.axis_index("dp")
    count = stacked.shape[0]
    picked = jnp.take(stacked, (my_shard - wanted_blocks) % count, axis=0, mode="clip")
    return picked.reshape((count * stacked.shape[1],) + stacked.shape[2:])


def gather_kernel(weight_shard):
    return lax.all_gather(weight_shard, "dp", axis=0, tiled=True)


def gather_projection(weight_shard):
    return lax.all_gather(weight_shard, "dp", axis=0, tiled=True)


def apply_kernel(full_field, kernel):
    sample_count = full_field.shape[0]
    out_width = kernel.shape[2]
    tap_images = jnp.einsum("scq,cte->stqe", full_field, kernel, preferred_element_type=jnp.float32)
    tap_images = tap_images.reshape(sample_count, 9, SIDE, SIDE, out_width)
    padded = jnp.pad(tap_images, ((0, 0), (0, 0), (1, 1), (1, 1), (0, 0)))
    running = padded[:, 0, 0:SIDE, 0:SIDE, :]
    for offset in range(1, 9):
        row_shift, col_shift = (offset // 3, offset % 3)
        running = (
            running
            + padded[:, offset, row_shift : row_shift + SIDE, col_shift : col_shift + SIDE, :]
        )
    return jnp.transpose(running.reshape(sample_count, SIDE * SIDE, out_width), (0, 2, 1))


def local(
    latents,
    modulation,
    first_kernel,
    second_kernel,
    encoder_cache,
    query_weight,
    output_weight,
    kept_prompt_list,
    destination,
    lengths,
):
    group_width = C // GROUPS
    dp_count = lax.axis_size("dp")
    mp_count = lax.axis_size("mp")
    my_shard = lax.axis_index("dp")
    my_column = lax.axis_index("mp")
    sample_shard_count = latents.shape[0]
    prompt_dev = encoder_cache.shape[0]
    cache_len = encoder_cache.shape[2]
    cache_width = encoder_cache.shape[1]
    cell_count = latents.shape[2]
    slot_limit = 2 * (sample_shard_count // dp_count)
    all_samples = destination.shape[0]
    owner_target = destination.reshape(dp_count, sample_shard_count)
    positions = jnp.arange(sample_shard_count, dtype=jnp.int32)
    before = positions[None, :] < positions[:, None]
    same_target = owner_target[:, :, None] == owner_target[:, None, :]
    slot_rank = jnp.sum((same_target & before[None]).astype(jnp.int32), axis=2)
    my_target = lax.dynamic_index_in_dim(owner_target, my_shard, 0, keepdims=False)
    my_rank = lax.dynamic_index_in_dim(slot_rank, my_shard, 0, keepdims=False)
    my_prompts = (
        lax.dynamic_slice_in_dim(
            kept_prompt_list, my_shard * sample_shard_count, sample_shard_count
        )
        - my_shard * prompt_dev
    )
    send_slot = my_target * slot_limit + my_rank
    slot_table = send_slot[:, None] == jnp.arange(dp_count * slot_limit, dtype=jnp.int32)[None, :]
    source_row = jnp.sum(jnp.where(slot_table, my_prompts[:, None], 0), axis=0)
    filled = jnp.any(slot_table, axis=0)
    send_rows = jnp.take(encoder_cache, source_row, axis=0)
    send_rows = jnp.where(filled[:, None, None], send_rows, jnp.zeros_like(send_rows))
    outgoing = send_rows.reshape(dp_count, slot_limit, cache_width, cache_len)
    arriving = destination == my_shard
    arrival_pos = jnp.cumsum(arriving.astype(jnp.int32)) - 1
    selector = arriving[None, :] & (arrival_pos[None, :] == positions[:, None])
    kept_prompt = jnp.sum(
        jnp.where(selector, jnp.arange(all_samples, dtype=jnp.int32)[None, :], 0), axis=1
    )
    incoming_order_rank = jnp.sum(jnp.where(selector, slot_rank.reshape(-1)[None, :], 0), axis=1)
    prompt_ids = jnp.sum(jnp.where(selector, kept_prompt_list[None, :], 0), axis=1)
    landing_slot = kept_prompt // sample_shard_count * slot_limit + incoming_order_rank
    prompt_hits = prompt_ids[:, None] == jnp.arange(lengths.shape[0], dtype=jnp.int32)[None, :]
    my_lengths = jnp.sum(jnp.where(prompt_hits, lengths[None, :], 0), axis=1)
    fast = dp_count == 4 and mp_count == 4 and lax.axis_size("groups") == 2
    weight_shards = (first_kernel, second_kernel, query_weight, output_weight)
    if fast:
        block_ids = jnp.arange(dp_count, dtype=jnp.int32)
        channel_blocks = jnp.bitwise_xor(block_ids, my_column)
        pieces = (first_kernel, second_kernel, query_weight, output_weight)
        dense = [piece.reshape(-1, 128) for piece in pieces]
        natural, latents = split_line_gather(jnp.concatenate(dense, axis=0), latents)
        kernel_rows = dense[0].shape[0] + dense[1].shape[0]
        kernel_part = jnp.take(natural[:, :kernel_rows], channel_blocks, axis=0, mode="clip")
        proj_part = natural[:, kernel_rows:]
        full_weights = []
        cut = 0
        query_part = jnp.take(proj_part, channel_blocks, axis=0, mode="clip")
        for piece, block, source in zip(pieces, dense, (kernel_part, kernel_part, query_part, proj_part)):
            if cut == kernel_rows:
                cut = 0
            chunk = source[:, cut : cut + block.shape[0]]
            cut += block.shape[0]
            full_weights.append(chunk.reshape((dp_count * piece.shape[0],) + piece.shape[1:]))
        gathered = (kernel_part, proj_part)
        full_weights = tuple(full_weights)
        outgoing = lax.optimization_barrier((outgoing, gathered))[0]
        spread_channels = pair_gather_channels
    else:
        full_weights = (
            gather_kernel(first_kernel),
            gather_kernel(second_kernel),
            gather_projection(query_weight),
            gather_projection(output_weight),
        )
        spread_channels = gather_channels
    incoming = lax.all_to_all(outgoing, "dp", split_axis=0, concat_axis=0, tiled=True)
    my_pairs = jnp.take(
        incoming.reshape(dp_count * slot_limit, cache_width, cache_len), landing_slot, axis=0
    )
    start_field = latents.astype(jnp.float32)
    activated = jax.nn.silu(norm_groups(start_field, group_width)).astype(jnp.bfloat16)
    first_in = spread_channels(activated)

    def convolve(full_field, which_weight):
        return apply_kernel(full_field, full_weights[which_weight])

    def project(field_rows, which_weight):
        full_weight = full_weights[which_weight]
        return jnp.einsum(
            "scq,ce->seq", field_rows, full_weight, preferred_element_type=jnp.float32
        )

    first_out = convolve(first_in, 0)
    scale_term = modulation[:, 0, :].astype(jnp.float32)[:, :, None]
    shift_term = modulation[:, 1, :].astype(jnp.float32)[:, :, None]
    modulated = jax.nn.silu(
        norm_groups(first_out, group_width) * (1.0 + scale_term) + shift_term
    ).astype(jnp.bfloat16)
    if fast:
        second_in = pair_gather_channels(modulated, lane_dense=False)
    else:
        second_in = spread_channels(modulated)
    residual = start_field + convolve(second_in, 1)
    normed_out = norm_groups(residual, group_width).astype(jnp.bfloat16)
    local_samples = sample_shard_count // mp_count
    query_cells, pair_heads = (
        xor_spread_samples(normed_out, local_samples)
        if fast
        else lax.all_to_all(normed_out, "mp", split_axis=0, concat_axis=1, tiled=True),
        lax.all_to_all(my_pairs, "mp", split_axis=0, concat_axis=1, tiled=True),
    )
    total_width = query_cells.shape[1]
    head_count = total_width // HEAD
    queries = project(query_cells, 2).astype(jnp.bfloat16)
    queries = queries.reshape(local_samples, head_count, HEAD, cell_count)
    heads_of_keys = pair_heads[:, :total_width, :].reshape(
        local_samples, head_count, HEAD, cache_len
    )
    value_heads = pair_heads[:, total_width:, :].reshape(local_samples, head_count, HEAD, cache_len)
    scores = jnp.einsum(
        "shdq,shdk->shqk", queries, heads_of_keys, preferred_element_type=jnp.float32
    ) * HEAD ** (-0.5)
    local_lengths = lax.dynamic_slice_in_dim(my_lengths, my_column * local_samples, local_samples)
    visible = (
        jnp.arange(cache_len, dtype=jnp.int32)[None, None, None, :]
        < local_lengths[:, None, None, None]
    )
    scores = jnp.where(visible, scores, MASKED)
    row_peak = jnp.max(scores, axis=3, keepdims=True)
    exponent = jnp.exp(scores - row_peak)
    attention = (exponent / jnp.sum(exponent, axis=3, keepdims=True)).astype(jnp.bfloat16)
    context = jnp.einsum(
        "shqk,shdk->shdq", attention, value_heads, preferred_element_type=jnp.float32
    ).astype(jnp.bfloat16)
    attended = project(context.reshape(local_samples, total_width, cell_count), 3).astype(
        jnp.bfloat16
    )
    if fast:
        returned = xor_return_channels(attended, attended.shape[1] // mp_count)
    else:
        returned = lax.all_to_all(attended, "mp", split_axis=1, concat_axis=0, tiled=True)
    final_field = residual + returned.astype(jnp.float32)
    return final_field.astype(jnp.bfloat16)


def solution(mesh):
    in_specs = (
        P(("groups", "dp"), "mp", None),
        P(("groups", "dp"), None, "mp"),
        P("dp", None, "mp"),
        P("dp", None, "mp"),
        P(("groups", "dp"), "mp", None),
        P("dp", None),
        P("dp", None),
        P("groups"),
        P("groups"),
        P("groups"),
    )
    out_specs = P(("groups", "dp"), "mp", None)
    return jax.shard_map(local, mesh=mesh, in_specs=in_specs, out_specs=out_specs, check_vma=False)
```

```python
import jax
import jax.numpy as jnp
from jax import lax
from jax.sharding import PartitionSpec as P

C = 640
GROUPS = 32
HEAD = 64
SIDE = 8


EPSILON = 1e-05
MASKED = -1e30


def norm_groups(values, group_width):
    field_shape = values.shape
    grouped = values.reshape(
        field_shape[0], field_shape[1] // group_width, group_width, field_shape[2]
    )
    center = grouped - jnp.mean(grouped, axis=(2, 3), keepdims=True)
    spread = jnp.mean(center * center, axis=(2, 3), keepdims=True)
    return (center * lax.rsqrt(spread + EPSILON)).reshape(field_shape)


def gather_channels(field):
    return lax.all_gather(field, "mp", axis=1, tiled=True)


def pair_gather_channels(field):
    dense = field.reshape(-1, 128)
    across = lax.ppermute(dense, "mp", [(i, i ^ 2) for i in range(4)])
    beside = lax.ppermute(dense, "mp", [(i, i ^ 1) for i in range(4)])
    relayed = lax.ppermute(across, "mp", [(i, i ^ 1) for i in range(4)])
    parts = [part.reshape(field.shape) for part in (beside, across, relayed)]
    return jnp.concatenate([field] + parts, axis=1)


def line_gather_flat(flat, count):
    my_shard = lax.axis_index("dp")
    rightward = [(i, i + 1) for i in range(count - 1)]
    leftward = [(i + 1, i) for i in range(count - 1)]
    going_right, going_left = flat, flat
    held = [flat]
    from_left, from_right = [], []
    for _ in range(1, count):
        going_right = lax.ppermute(going_right, "dp", rightward)
        going_left = lax.ppermute(going_left, "dp", leftward)
        from_left.append(going_right)
        from_right.append(going_left)
    line = jnp.stack(from_left[::-1] + held + from_right)
    return lax.dynamic_slice_in_dim(line, count - 1 - my_shard, count, axis=0)


def split_line_gather(packed, gated):
    my_shard = lax.axis_index("dp")
    my_group = lax.axis_index("groups")
    halves = packed.reshape(2, packed.shape[0] // 2, packed.shape[1])
    mine = lax.dynamic_index_in_dim(halves, my_group, 0, keepdims=False)
    mine, gated = lax.optimization_barrier((mine, gated))
    rightward = [(i, i + 1) for i in range(3)]
    leftward = [(i + 1, i) for i in range(3)]
    swap = [(0, 1), (1, 0)]
    left_1 = lax.ppermute(mine, "dp", rightward)
    right_1 = lax.ppermute(mine, "dp", leftward)
    first_swap = lax.ppermute(jnp.where(my_shard >= 1, left_1, right_1), "groups", swap)
    left_2 = lax.ppermute(left_1, "dp", rightward)
    right_2 = lax.ppermute(right_1, "dp", leftward)
    second_swap = lax.ppermute(jnp.where(my_shard >= 2, left_2, right_2), "groups", swap)
    left_3 = lax.ppermute(left_2, "dp", rightward)
    right_3 = lax.ppermute(right_2, "dp", leftward)
    third_pick = jnp.where(my_shard == 0, right_3, jnp.where(my_shard == 3, left_3, right_1))
    third_swap = lax.ppermute(third_pick, "groups", swap)

    def whole(own_half, other_half):
        lead = jnp.where(my_group == 0, own_half, other_half)
        tail = jnp.where(my_group == 0, other_half, own_half)
        return jnp.concatenate([lead, tail], axis=0)

    line = jnp.stack(
        [
            whole(left_3, third_swap),
            whole(left_2, second_swap),
            whole(left_1, first_swap),
            packed,
            whole(right_1, jnp.where(my_shard == 0, first_swap, third_swap)),
            whole(right_2, second_swap),
            whole(right_3, third_swap),
        ]
    )
    return lax.dynamic_slice_in_dim(line, 3 - my_shard, 4, axis=0), gated, (left_3, right_3)


def xor_spread_samples(field, group):
    my_column = lax.axis_index("mp")
    parts = [lax.dynamic_slice_in_dim(field, my_column * group, group, axis=0)]
    for step in range(1, 4):
        block = lax.dynamic_slice_in_dim(field, (my_column ^ step) * group, group, axis=0)
        moved = lax.ppermute(block.reshape(-1, 128), "mp", [(i, i ^ step) for i in range(4)])
        parts.append(moved.reshape(block.shape))
    return jnp.concatenate(parts, axis=1)


def xor_return_channels(field, width):
    my_column = lax.axis_index("mp")
    parts = [lax.dynamic_slice_in_dim(field, my_column * width, width, axis=1)]
    for step in range(1, 4):
        block = lax.dynamic_slice_in_dim(field, (my_column ^ step) * width, width, axis=1)
        moved = lax.ppermute(block.reshape(-1, 128), "mp", [(i, i ^ step) for i in range(4)])
        parts.append(moved.reshape(block.shape))
    order = jnp.bitwise_xor(jnp.arange(4, dtype=jnp.int32), my_column)
    picked = jnp.take(jnp.stack(parts), order, axis=0, mode="clip")
    return picked.reshape((4 * field.shape[0],) + picked.shape[2:])


def shift_parts(shard, count):
    parts = [shard]
    for step in range(1, count):
        parts.append(lax.ppermute(shard, "dp", [(i, (i + step) % count) for i in range(count)]))
    return jnp.stack(parts)


def order_rows(stacked, wanted_blocks):
    my_shard = lax.axis_index("dp")
    count = stacked.shape[0]
    picked = jnp.take(stacked, (my_shard - wanted_blocks) % count, axis=0, mode="clip")
    return picked.reshape((count * stacked.shape[1],) + stacked.shape[2:])


def gather_kernel(weight_shard):
    return lax.all_gather(weight_shard, "dp", axis=0, tiled=True)


def gather_projection(weight_shard):
    return lax.all_gather(weight_shard, "dp", axis=0, tiled=True)


def apply_kernel(full_field, kernel):
    sample_count = full_field.shape[0]
    out_width = kernel.shape[2]
    tap_images = jnp.einsum("scq,cte->stqe", full_field, kernel, preferred_element_type=jnp.float32)
    tap_images = tap_images.reshape(sample_count, 9, SIDE, SIDE, out_width)
    padded = jnp.pad(tap_images, ((0, 0), (0, 0), (1, 1), (1, 1), (0, 0)))
    running = padded[:, 0, 0:SIDE, 0:SIDE, :]
    for offset in range(1, 9):
        row_shift, col_shift = (offset // 3, offset % 3)
        running = (
            running
            + padded[:, offset, row_shift : row_shift + SIDE, col_shift : col_shift + SIDE, :]
        )
    return jnp.transpose(running.reshape(sample_count, SIDE * SIDE, out_width), (0, 2, 1))


def local(
    latents,
    modulation,
    first_kernel,
    second_kernel,
    encoder_cache,
    query_weight,
    output_weight,
    kept_prompt_list,
    destination,
    lengths,
):
    group_width = C // GROUPS
    dp_count = lax.axis_size("dp")
    mp_count = lax.axis_size("mp")
    my_shard = lax.axis_index("dp")
    my_column = lax.axis_index("mp")
    sample_shard_count = latents.shape[0]
    prompt_dev = encoder_cache.shape[0]
    cache_len = encoder_cache.shape[2]
    cache_width = encoder_cache.shape[1]
    cell_count = latents.shape[2]
    slot_limit = 2 * (sample_shard_count // dp_count)
    all_samples = destination.shape[0]
    owner_target = destination.reshape(dp_count, sample_shard_count)
    positions = jnp.arange(sample_shard_count, dtype=jnp.int32)
    before = positions[None, :] < positions[:, None]
    same_target = owner_target[:, :, None] == owner_target[:, None, :]
    slot_rank = jnp.sum((same_target & before[None]).astype(jnp.int32), axis=2)
    my_target = lax.dynamic_index_in_dim(owner_target, my_shard, 0, keepdims=False)
    my_rank = lax.dynamic_index_in_dim(slot_rank, my_shard, 0, keepdims=False)
    my_prompts = (
        lax.dynamic_slice_in_dim(
            kept_prompt_list, my_shard * sample_shard_count, sample_shard_count
        )
        - my_shard * prompt_dev
    )
    send_slot = my_target * slot_limit + my_rank
    slot_table = send_slot[:, None] == jnp.arange(dp_count * slot_limit, dtype=jnp.int32)[None, :]
    source_row = jnp.sum(jnp.where(slot_table, my_prompts[:, None], 0), axis=0)
    filled = jnp.any(slot_table, axis=0)
    send_rows = jnp.take(encoder_cache, source_row, axis=0)
    send_rows = jnp.where(filled[:, None, None], send_rows, jnp.zeros_like(send_rows))
    outgoing = send_rows.reshape(dp_count, slot_limit, cache_width, cache_len)
    arriving = destination == my_shard
    arrival_pos = jnp.cumsum(arriving.astype(jnp.int32)) - 1
    selector = arriving[None, :] & (arrival_pos[None, :] == positions[:, None])
    kept_prompt = jnp.sum(
        jnp.where(selector, jnp.arange(all_samples, dtype=jnp.int32)[None, :], 0), axis=1
    )
    incoming_order_rank = jnp.sum(jnp.where(selector, slot_rank.reshape(-1)[None, :], 0), axis=1)
    prompt_ids = jnp.sum(jnp.where(selector, kept_prompt_list[None, :], 0), axis=1)
    landing_slot = kept_prompt // sample_shard_count * slot_limit + incoming_order_rank
    prompt_hits = prompt_ids[:, None] == jnp.arange(lengths.shape[0], dtype=jnp.int32)[None, :]
    my_lengths = jnp.sum(jnp.where(prompt_hits, lengths[None, :], 0), axis=1)
    fast = dp_count == 4 and mp_count == 4 and lax.axis_size("groups") == 2
    weight_shards = (first_kernel, second_kernel, query_weight, output_weight)
    if fast:
        block_ids = jnp.arange(dp_count, dtype=jnp.int32)
        channel_blocks = jnp.bitwise_xor(block_ids, my_column)
        pieces = (first_kernel, second_kernel, query_weight, output_weight)
        dense = [piece.reshape(-1, 128) for piece in pieces]
        natural, latents, line_done = split_line_gather(jnp.concatenate(dense, axis=0), latents)
        kernel_rows = dense[0].shape[0] + dense[1].shape[0]
        kernel_part = jnp.take(natural[:, :kernel_rows], channel_blocks, axis=0, mode="clip")
        proj_part = natural[:, kernel_rows:]
        full_weights = []
        cut = 0
        query_part = jnp.take(proj_part, channel_blocks, axis=0, mode="clip")
        for piece, block, source in zip(pieces, dense, (kernel_part, kernel_part, query_part, proj_part)):
            if cut == kernel_rows:
                cut = 0
            chunk = source[:, cut : cut + block.shape[0]]
            cut += block.shape[0]
            full_weights.append(chunk.reshape((dp_count * piece.shape[0],) + piece.shape[1:]))
        gathered = (kernel_part, proj_part)
        full_weights = tuple(full_weights)
        outgoing = lax.optimization_barrier((outgoing, line_done))[0]
        spread_channels = pair_gather_channels
    else:
        full_weights = (
            gather_kernel(first_kernel),
            gather_kernel(second_kernel),
            gather_projection(query_weight),
            gather_projection(output_weight),
        )
        spread_channels = gather_channels
    incoming = lax.all_to_all(outgoing, "dp", split_axis=0, concat_axis=0, tiled=True)
    my_pairs = jnp.take(
        incoming.reshape(dp_count * slot_limit, cache_width, cache_len), landing_slot, axis=0
    )
    start_field = latents.astype(jnp.float32)
    activated = jax.nn.silu(norm_groups(start_field, group_width)).astype(jnp.bfloat16)
    first_in = spread_channels(activated)

    def convolve(full_field, which_weight):
        return apply_kernel(full_field, full_weights[which_weight])

    def project(field_rows, which_weight):
        full_weight = full_weights[which_weight]
        return jnp.einsum(
            "scq,ce->seq", field_rows, full_weight, preferred_element_type=jnp.float32
        )

    first_out = convolve(first_in, 0)
    scale_term = modulation[:, 0, :].astype(jnp.float32)[:, :, None]
    shift_term = modulation[:, 1, :].astype(jnp.float32)[:, :, None]
    modulated = jax.nn.silu(
        norm_groups(first_out, group_width) * (1.0 + scale_term) + shift_term
    ).astype(jnp.bfloat16)
    second_in = spread_channels(modulated)
    residual = start_field + convolve(second_in, 1)
    normed_out = norm_groups(residual, group_width).astype(jnp.bfloat16)
    local_samples = sample_shard_count // mp_count
    query_cells, pair_heads = (
        xor_spread_samples(normed_out, local_samples)
        if fast
        else lax.all_to_all(normed_out, "mp", split_axis=0, concat_axis=1, tiled=True),
        lax.all_to_all(my_pairs, "mp", split_axis=0, concat_axis=1, tiled=True),
    )
    total_width = query_cells.shape[1]
    head_count = total_width // HEAD
    queries = project(query_cells, 2).astype(jnp.bfloat16)
    queries = queries.reshape(local_samples, head_count, HEAD, cell_count)
    heads_of_keys = pair_heads[:, :total_width, :].reshape(
        local_samples, head_count, HEAD, cache_len
    )
    value_heads = pair_heads[:, total_width:, :].reshape(local_samples, head_count, HEAD, cache_len)
    scores = jnp.einsum(
        "shdq,shdk->shqk", queries, heads_of_keys, preferred_element_type=jnp.float32
    ) * HEAD ** (-0.5)
    local_lengths = lax.dynamic_slice_in_dim(my_lengths, my_column * local_samples, local_samples)
    visible = (
        jnp.arange(cache_len, dtype=jnp.int32)[None, None, None, :]
        < local_lengths[:, None, None, None]
    )
    scores = jnp.where(visible, scores, MASKED)
    row_peak = jnp.max(scores, axis=3, keepdims=True)
    exponent = jnp.exp(scores - row_peak)
    attention = (exponent / jnp.sum(exponent, axis=3, keepdims=True)).astype(jnp.bfloat16)
    context = jnp.einsum(
        "shqk,shdk->shdq", attention, value_heads, preferred_element_type=jnp.float32
    ).astype(jnp.bfloat16)
    attended = project(context.reshape(local_samples, total_width, cell_count), 3).astype(
        jnp.bfloat16
    )
    if fast:
        returned = xor_return_channels(attended, attended.shape[1] // mp_count)
    else:
        returned = lax.all_to_all(attended, "mp", split_axis=1, concat_axis=0, tiled=True)
    final_field = residual + returned.astype(jnp.float32)
    return final_field.astype(jnp.bfloat16)


def solution(mesh):
    in_specs = (
        P(("groups", "dp"), "mp", None),
        P(("groups", "dp"), None, "mp"),
        P("dp", None, "mp"),
        P("dp", None, "mp"),
        P(("groups", "dp"), "mp", None),
        P("dp", None),
        P("dp", None),
        P("groups"),
        P("groups"),
        P("groups"),
    )
    out_specs = P(("groups", "dp"), "mp", None)
    return jax.shard_map(local, mesh=mesh, in_specs=in_specs, out_specs=out_specs, check_vma=False)
```

```python
import jax
import jax.numpy as jnp
from jax import lax
from jax.sharding import PartitionSpec as P

C = 640
GROUPS = 32
HEAD = 64
SIDE = 8


EPSILON = 1e-05
MASKED = -1e30


def norm_groups(values, group_width):
    field_shape = values.shape
    grouped = values.reshape(
        field_shape[0], field_shape[1] // group_width, group_width, field_shape[2]
    )
    center = grouped - jnp.mean(grouped, axis=(2, 3), keepdims=True)
    spread = jnp.mean(center * center, axis=(2, 3), keepdims=True)
    return (center * lax.rsqrt(spread + EPSILON)).reshape(field_shape)


def gather_channels(field):
    return lax.all_gather(field, "mp", axis=1, tiled=True)


def pair_gather_channels(field):
    dense = field.reshape(-1, 128)
    across = lax.ppermute(dense, "mp", [(i, i ^ 2) for i in range(4)])
    beside = lax.ppermute(dense, "mp", [(i, i ^ 1) for i in range(4)])
    relayed = lax.ppermute(across, "mp", [(i, i ^ 1) for i in range(4)])
    parts = [part.reshape(field.shape) for part in (beside, across, relayed)]
    return jnp.concatenate([field] + parts, axis=1)


def line_gather_flat(flat, count):
    my_shard = lax.axis_index("dp")
    rightward = [(i, i + 1) for i in range(count - 1)]
    leftward = [(i + 1, i) for i in range(count - 1)]
    going_right, going_left = flat, flat
    held = [flat]
    from_left, from_right = [], []
    for _ in range(1, count):
        going_right = lax.ppermute(going_right, "dp", rightward)
        going_left = lax.ppermute(going_left, "dp", leftward)
        from_left.append(going_right)
        from_right.append(going_left)
    line = jnp.stack(from_left[::-1] + held + from_right)
    return lax.dynamic_slice_in_dim(line, count - 1 - my_shard, count, axis=0)


def split_line_gather(packed, gated):
    my_shard = lax.axis_index("dp")
    my_group = lax.axis_index("groups")
    halves = packed.reshape(2, packed.shape[0] // 2, packed.shape[1])
    mine = lax.dynamic_index_in_dim(halves, my_group, 0, keepdims=False)
    mine, gated = lax.optimization_barrier((mine, gated))
    rightward = [(i, i + 1) for i in range(3)]
    leftward = [(i + 1, i) for i in range(3)]
    swap = [(0, 1), (1, 0)]
    left_1 = lax.ppermute(mine, "dp", rightward)
    right_1 = lax.ppermute(mine, "dp", leftward)
    first_swap = lax.ppermute(jnp.where(my_shard >= 1, left_1, right_1), "groups", swap)
    left_2 = lax.ppermute(left_1, "dp", rightward)
    right_2 = lax.ppermute(right_1, "dp", leftward)
    second_swap = lax.ppermute(jnp.where(my_shard >= 2, left_2, right_2), "groups", swap)
    left_3 = lax.ppermute(left_2, "dp", rightward)
    right_3 = lax.ppermute(right_2, "dp", leftward)
    third_pick = jnp.where(my_shard == 0, right_3, jnp.where(my_shard == 3, left_3, right_1))
    third_swap = lax.ppermute(third_pick, "groups", swap)

    def whole(own_half, other_half):
        lead = jnp.where(my_group == 0, own_half, other_half)
        tail = jnp.where(my_group == 0, other_half, own_half)
        return jnp.concatenate([lead, tail], axis=0)

    line = jnp.stack(
        [
            whole(left_3, third_swap),
            whole(left_2, second_swap),
            whole(left_1, first_swap),
            packed,
            whole(right_1, jnp.where(my_shard == 0, first_swap, third_swap)),
            whole(right_2, second_swap),
            whole(right_3, third_swap),
        ]
    )
    return lax.dynamic_slice_in_dim(line, 3 - my_shard, 4, axis=0), gated, (left_3, right_3)


def xor_spread_samples(field, group):
    my_column = lax.axis_index("mp")
    parts = [lax.dynamic_slice_in_dim(field, my_column * group, group, axis=0)]
    for step in range(1, 4):
        block = lax.dynamic_slice_in_dim(field, (my_column ^ step) * group, group, axis=0)
        moved = lax.ppermute(block.reshape(-1, 128), "mp", [(i, i ^ step) for i in range(4)])
        parts.append(moved.reshape(block.shape))
    return jnp.concatenate(parts, axis=1)


def xor_return_channels(field, width):
    my_column = lax.axis_index("mp")
    parts = [lax.dynamic_slice_in_dim(field, my_column * width, width, axis=1)]
    for step in range(1, 4):
        block = lax.dynamic_slice_in_dim(field, (my_column ^ step) * width, width, axis=1)
        moved = lax.ppermute(block.reshape(-1, 128), "mp", [(i, i ^ step) for i in range(4)])
        parts.append(moved.reshape(block.shape))
    order = jnp.bitwise_xor(jnp.arange(4, dtype=jnp.int32), my_column)
    picked = jnp.take(jnp.stack(parts), order, axis=0, mode="clip")
    return picked.reshape((4 * field.shape[0],) + picked.shape[2:])


def shift_parts(shard, count):
    parts = [shard]
    for step in range(1, count):
        parts.append(lax.ppermute(shard, "dp", [(i, (i + step) % count) for i in range(count)]))
    return jnp.stack(parts)


def order_rows(stacked, wanted_blocks):
    my_shard = lax.axis_index("dp")
    count = stacked.shape[0]
    picked = jnp.take(stacked, (my_shard - wanted_blocks) % count, axis=0, mode="clip")
    return picked.reshape((count * stacked.shape[1],) + stacked.shape[2:])


def gather_kernel(weight_shard):
    return lax.all_gather(weight_shard, "dp", axis=0, tiled=True)


def gather_projection(weight_shard):
    return lax.all_gather(weight_shard, "dp", axis=0, tiled=True)


def apply_kernel(full_field, kernel):
    sample_count = full_field.shape[0]
    out_width = kernel.shape[2]
    tap_images = jnp.einsum("scq,cte->stqe", full_field, kernel, preferred_element_type=jnp.float32)
    tap_images = tap_images.reshape(sample_count, 9, SIDE, SIDE, out_width)
    padded = jnp.pad(tap_images, ((0, 0), (0, 0), (1, 1), (1, 1), (0, 0)))
    running = padded[:, 0, 0:SIDE, 0:SIDE, :]
    for offset in range(1, 9):
        row_shift, col_shift = (offset // 3, offset % 3)
        running = (
            running
            + padded[:, offset, row_shift : row_shift + SIDE, col_shift : col_shift + SIDE, :]
        )
    return jnp.transpose(running.reshape(sample_count, SIDE * SIDE, out_width), (0, 2, 1))


def local(
    latents,
    modulation,
    first_kernel,
    second_kernel,
    encoder_cache,
    query_weight,
    output_weight,
    kept_prompt_list,
    destination,
    lengths,
):
    group_width = C // GROUPS
    dp_count = lax.axis_size("dp")
    mp_count = lax.axis_size("mp")
    my_shard = lax.axis_index("dp")
    my_column = lax.axis_index("mp")
    sample_shard_count = latents.shape[0]
    prompt_dev = encoder_cache.shape[0]
    cache_len = encoder_cache.shape[2]
    cache_width = encoder_cache.shape[1]
    cell_count = latents.shape[2]
    slot_limit = 2 * (sample_shard_count // dp_count)
    all_samples = destination.shape[0]
    owner_target = destination.reshape(dp_count, sample_shard_count)
    positions = jnp.arange(sample_shard_count, dtype=jnp.int32)
    before = positions[None, :] < positions[:, None]
    same_target = owner_target[:, :, None] == owner_target[:, None, :]
    slot_rank = jnp.sum((same_target & before[None]).astype(jnp.int32), axis=2)
    my_target = lax.dynamic_index_in_dim(owner_target, my_shard, 0, keepdims=False)
    my_rank = lax.dynamic_index_in_dim(slot_rank, my_shard, 0, keepdims=False)
    my_prompts = (
        lax.dynamic_slice_in_dim(
            kept_prompt_list, my_shard * sample_shard_count, sample_shard_count
        )
        - my_shard * prompt_dev
    )
    send_slot = my_target * slot_limit + my_rank
    slot_table = send_slot[:, None] == jnp.arange(dp_count * slot_limit, dtype=jnp.int32)[None, :]
    source_row = jnp.sum(jnp.where(slot_table, my_prompts[:, None], 0), axis=0)
    filled = jnp.any(slot_table, axis=0)
    send_rows = jnp.take(encoder_cache, source_row, axis=0)
    send_rows = jnp.where(filled[:, None, None], send_rows, jnp.zeros_like(send_rows))
    outgoing = send_rows.reshape(dp_count, slot_limit, cache_width, cache_len)
    arriving = destination == my_shard
    arrival_pos = jnp.cumsum(arriving.astype(jnp.int32)) - 1
    selector = arriving[None, :] & (arrival_pos[None, :] == positions[:, None])
    kept_prompt = jnp.sum(
        jnp.where(selector, jnp.arange(all_samples, dtype=jnp.int32)[None, :], 0), axis=1
    )
    incoming_order_rank = jnp.sum(jnp.where(selector, slot_rank.reshape(-1)[None, :], 0), axis=1)
    prompt_ids = jnp.sum(jnp.where(selector, kept_prompt_list[None, :], 0), axis=1)
    landing_slot = kept_prompt // sample_shard_count * slot_limit + incoming_order_rank
    prompt_hits = prompt_ids[:, None] == jnp.arange(lengths.shape[0], dtype=jnp.int32)[None, :]
    my_lengths = jnp.sum(jnp.where(prompt_hits, lengths[None, :], 0), axis=1)
    fast = dp_count == 4 and mp_count == 4 and lax.axis_size("groups") == 2
    weight_shards = (first_kernel, second_kernel, query_weight, output_weight)
    if fast:
        block_ids = jnp.arange(dp_count, dtype=jnp.int32)
        channel_blocks = jnp.bitwise_xor(block_ids, my_column)
        pieces = (first_kernel, second_kernel, query_weight, output_weight)
        dense = [piece.reshape(-1, 128) for piece in pieces]
        natural, latents, line_done = split_line_gather(jnp.concatenate(dense, axis=0), latents)
        kernel_rows = dense[0].shape[0] + dense[1].shape[0]
        kernel_part = jnp.take(natural[:, :kernel_rows], channel_blocks, axis=0, mode="clip")
        proj_part = natural[:, kernel_rows:]
        full_weights = []
        cut = 0
        query_part = jnp.take(proj_part, channel_blocks, axis=0, mode="clip")
        for piece, block, source in zip(pieces, dense, (kernel_part, kernel_part, query_part, proj_part)):
            if cut == kernel_rows:
                cut = 0
            chunk = source[:, cut : cut + block.shape[0]]
            cut += block.shape[0]
            full_weights.append(chunk.reshape((dp_count * piece.shape[0],) + piece.shape[1:]))
        gathered = (kernel_part, proj_part)
        full_weights = tuple(full_weights)
        outgoing = lax.optimization_barrier((outgoing, line_done))[0]
        spread_channels = pair_gather_channels
    else:
        full_weights = (
            gather_kernel(first_kernel),
            gather_kernel(second_kernel),
            gather_projection(query_weight),
            gather_projection(output_weight),
        )
        spread_channels = gather_channels
    incoming = lax.all_to_all(outgoing, "dp", split_axis=0, concat_axis=0, tiled=True)
    my_pairs = jnp.take(
        incoming.reshape(dp_count * slot_limit, cache_width, cache_len), landing_slot, axis=0
    )
    start_field = latents.astype(jnp.float32)
    activated = jax.nn.silu(norm_groups(start_field, group_width)).astype(jnp.bfloat16)
    first_in = spread_channels(activated)

    def convolve(full_field, which_weight):
        return apply_kernel(full_field, full_weights[which_weight])

    def project(field_rows, which_weight):
        full_weight = full_weights[which_weight]
        return jnp.einsum(
            "scq,ce->seq", field_rows, full_weight, preferred_element_type=jnp.float32
        )

    first_out = convolve(first_in, 0)
    scale_term = modulation[:, 0, :].astype(jnp.float32)[:, :, None]
    shift_term = modulation[:, 1, :].astype(jnp.float32)[:, :, None]
    modulated = jax.nn.silu(
        norm_groups(first_out, group_width) * (1.0 + scale_term) + shift_term
    ).astype(jnp.bfloat16)
    second_in = spread_channels(modulated)
    residual = start_field + convolve(second_in, 1)
    normed_out = norm_groups(residual, group_width).astype(jnp.bfloat16)
    local_samples = sample_shard_count // mp_count
    if fast:
        query_cells = xor_spread_samples(normed_out, local_samples)
        my_pairs = lax.optimization_barrier((my_pairs, query_cells))[0]
    else:
        query_cells = lax.all_to_all(normed_out, "mp", split_axis=0, concat_axis=1, tiled=True)
    pair_heads = lax.all_to_all(my_pairs, "mp", split_axis=0, concat_axis=1, tiled=True)
    total_width = query_cells.shape[1]
    head_count = total_width // HEAD
    queries = project(query_cells, 2).astype(jnp.bfloat16)
    queries = queries.reshape(local_samples, head_count, HEAD, cell_count)
    heads_of_keys = pair_heads[:, :total_width, :].reshape(
        local_samples, head_count, HEAD, cache_len
    )
    value_heads = pair_heads[:, total_width:, :].reshape(local_samples, head_count, HEAD, cache_len)
    scores = jnp.einsum(
        "shdq,shdk->shqk", queries, heads_of_keys, preferred_element_type=jnp.float32
    ) * HEAD ** (-0.5)
    local_lengths = lax.dynamic_slice_in_dim(my_lengths, my_column * local_samples, local_samples)
    visible = (
        jnp.arange(cache_len, dtype=jnp.int32)[None, None, None, :]
        < local_lengths[:, None, None, None]
    )
    scores = jnp.where(visible, scores, MASKED)
    row_peak = jnp.max(scores, axis=3, keepdims=True)
    exponent = jnp.exp(scores - row_peak)
    attention = (exponent / jnp.sum(exponent, axis=3, keepdims=True)).astype(jnp.bfloat16)
    context = jnp.einsum(
        "shqk,shdk->shdq", attention, value_heads, preferred_element_type=jnp.float32
    ).astype(jnp.bfloat16)
    attended = project(context.reshape(local_samples, total_width, cell_count), 3).astype(
        jnp.bfloat16
    )
    if fast:
        returned = xor_return_channels(attended, attended.shape[1] // mp_count)
    else:
        returned = lax.all_to_all(attended, "mp", split_axis=1, concat_axis=0, tiled=True)
    final_field = residual + returned.astype(jnp.float32)
    return final_field.astype(jnp.bfloat16)


def solution(mesh):
    in_specs = (
        P(("groups", "dp"), "mp", None),
        P(("groups", "dp"), None, "mp"),
        P("dp", None, "mp"),
        P("dp", None, "mp"),
        P(("groups", "dp"), "mp", None),
        P("dp", None),
        P("dp", None),
        P("groups"),
        P("groups"),
        P("groups"),
    )
    out_specs = P(("groups", "dp"), "mp", None)
    return jax.shard_map(local, mesh=mesh, in_specs=in_specs, out_specs=out_specs, check_vma=False)
```

```python
import jax
import jax.numpy as jnp
from jax import lax
from jax.sharding import PartitionSpec as P

C = 640
GROUPS = 32
HEAD = 64
SIDE = 8


EPSILON = 1e-05
MASKED = -1e30


def norm_groups(values, group_width):
    field_shape = values.shape
    grouped = values.reshape(
        field_shape[0], field_shape[1] // group_width, group_width, field_shape[2]
    )
    center = grouped - jnp.mean(grouped, axis=(2, 3), keepdims=True)
    spread = jnp.mean(center * center, axis=(2, 3), keepdims=True)
    return (center * lax.rsqrt(spread + EPSILON)).reshape(field_shape)


def gather_channels(field):
    return lax.all_gather(field, "mp", axis=1, tiled=True)


def pair_gather_channels(field):
    dense = field.reshape(-1, 128)
    across = lax.ppermute(dense, "mp", [(i, i ^ 2) for i in range(4)])
    beside = lax.ppermute(dense, "mp", [(i, i ^ 1) for i in range(4)])
    relayed = lax.ppermute(across, "mp", [(i, i ^ 1) for i in range(4)])
    parts = [part.reshape(field.shape) for part in (beside, across, relayed)]
    return jnp.concatenate([field] + parts, axis=1)


def line_gather_flat(flat, count):
    my_shard = lax.axis_index("dp")
    rightward = [(i, i + 1) for i in range(count - 1)]
    leftward = [(i + 1, i) for i in range(count - 1)]
    going_right, going_left = flat, flat
    held = [flat]
    from_left, from_right = [], []
    for _ in range(1, count):
        going_right = lax.ppermute(going_right, "dp", rightward)
        going_left = lax.ppermute(going_left, "dp", leftward)
        from_left.append(going_right)
        from_right.append(going_left)
    line = jnp.stack(from_left[::-1] + held + from_right)
    return lax.dynamic_slice_in_dim(line, count - 1 - my_shard, count, axis=0)


def split_line_gather(packed, gated):
    my_shard = lax.axis_index("dp")
    my_group = lax.axis_index("groups")
    halves = packed.reshape(2, packed.shape[0] // 2, packed.shape[1])
    mine = lax.dynamic_index_in_dim(halves, my_group, 0, keepdims=False)
    mine, gated = lax.optimization_barrier((mine, gated))
    rightward = [(i, i + 1) for i in range(3)]
    leftward = [(i + 1, i) for i in range(3)]
    swap = [(0, 1), (1, 0)]
    left_1 = lax.ppermute(mine, "dp", rightward)
    right_1 = lax.ppermute(mine, "dp", leftward)
    first_swap = lax.ppermute(jnp.where(my_shard >= 1, left_1, right_1), "groups", swap)
    left_2 = lax.ppermute(left_1, "dp", rightward)
    right_2 = lax.ppermute(right_1, "dp", leftward)
    second_swap = lax.ppermute(jnp.where(my_shard >= 2, left_2, right_2), "groups", swap)
    left_3 = lax.ppermute(left_2, "dp", rightward)
    right_3 = lax.ppermute(right_2, "dp", leftward)
    third_pick = jnp.where(my_shard == 0, right_3, jnp.where(my_shard == 3, left_3, right_1))
    third_swap = lax.ppermute(third_pick, "groups", swap)

    def whole(own_half, other_half):
        lead = jnp.where(my_group == 0, own_half, other_half)
        tail = jnp.where(my_group == 0, other_half, own_half)
        return jnp.concatenate([lead, tail], axis=0)

    line = jnp.stack(
        [
            whole(left_3, third_swap),
            whole(left_2, second_swap),
            whole(left_1, first_swap),
            packed,
            whole(right_1, jnp.where(my_shard == 0, first_swap, third_swap)),
            whole(right_2, second_swap),
            whole(right_3, third_swap),
        ]
    )
    return lax.dynamic_slice_in_dim(line, 3 - my_shard, 4, axis=0), gated, (left_3, right_3)


def pair_gather_channel_minor(field):
    cell_major = jnp.transpose(field, (0, 2, 1))
    dense = cell_major.reshape(-1, 128)
    across = lax.ppermute(dense, "mp", [(i, i ^ 2) for i in range(4)])
    beside = lax.ppermute(dense, "mp", [(i, i ^ 1) for i in range(4)])
    relayed = lax.ppermute(across, "mp", [(i, i ^ 1) for i in range(4)])
    parts = [jnp.transpose(part.reshape(cell_major.shape), (0, 2, 1)) for part in (beside, across, relayed)]
    return jnp.concatenate([field] + parts, axis=1)


def xor_spread_samples(field, group):
    my_column = lax.axis_index("mp")
    parts = [lax.dynamic_slice_in_dim(field, my_column * group, group, axis=0)]
    for step in range(1, 4):
        block = lax.dynamic_slice_in_dim(field, (my_column ^ step) * group, group, axis=0)
        moved = lax.ppermute(block.reshape(-1, 128), "mp", [(i, i ^ step) for i in range(4)])
        parts.append(moved.reshape(block.shape))
    return jnp.concatenate(parts, axis=1)


def xor_return_channels(field, width):
    my_column = lax.axis_index("mp")
    parts = [lax.dynamic_slice_in_dim(field, my_column * width, width, axis=1)]
    for step in range(1, 4):
        block = lax.dynamic_slice_in_dim(field, (my_column ^ step) * width, width, axis=1)
        moved = lax.ppermute(block.reshape(-1, 128), "mp", [(i, i ^ step) for i in range(4)])
        parts.append(moved.reshape(block.shape))
    order = jnp.bitwise_xor(jnp.arange(4, dtype=jnp.int32), my_column)
    picked = jnp.take(jnp.stack(parts), order, axis=0, mode="clip")
    return picked.reshape((4 * field.shape[0],) + picked.shape[2:])


def shift_parts(shard, count):
    parts = [shard]
    for step in range(1, count):
        parts.append(lax.ppermute(shard, "dp", [(i, (i + step) % count) for i in range(count)]))
    return jnp.stack(parts)


def order_rows(stacked, wanted_blocks):
    my_shard = lax.axis_index("dp")
    count = stacked.shape[0]
    picked = jnp.take(stacked, (my_shard - wanted_blocks) % count, axis=0, mode="clip")
    return picked.reshape((count * stacked.shape[1],) + stacked.shape[2:])


def gather_kernel(weight_shard):
    return lax.all_gather(weight_shard, "dp", axis=0, tiled=True)


def gather_projection(weight_shard):
    return lax.all_gather(weight_shard, "dp", axis=0, tiled=True)


def apply_kernel(full_field, kernel):
    sample_count = full_field.shape[0]
    out_width = kernel.shape[2]
    tap_images = jnp.einsum("scq,cte->stqe", full_field, kernel, preferred_element_type=jnp.float32)
    tap_images = tap_images.reshape(sample_count, 9, SIDE, SIDE, out_width)
    padded = jnp.pad(tap_images, ((0, 0), (0, 0), (1, 1), (1, 1), (0, 0)))
    running = padded[:, 0, 0:SIDE, 0:SIDE, :]
    for offset in range(1, 9):
        row_shift, col_shift = (offset // 3, offset % 3)
        running = (
            running
            + padded[:, offset, row_shift : row_shift + SIDE, col_shift : col_shift + SIDE, :]
        )
    return jnp.transpose(running.reshape(sample_count, SIDE * SIDE, out_width), (0, 2, 1))


def local(
    latents,
    modulation,
    first_kernel,
    second_kernel,
    encoder_cache,
    query_weight,
    output_weight,
    kept_prompt_list,
    destination,
    lengths,
):
    group_width = C // GROUPS
    dp_count = lax.axis_size("dp")
    mp_count = lax.axis_size("mp")
    my_shard = lax.axis_index("dp")
    my_column = lax.axis_index("mp")
    sample_shard_count = latents.shape[0]
    prompt_dev = encoder_cache.shape[0]
    cache_len = encoder_cache.shape[2]
    cache_width = encoder_cache.shape[1]
    cell_count = latents.shape[2]
    slot_limit = 2 * (sample_shard_count // dp_count)
    all_samples = destination.shape[0]
    owner_target = destination.reshape(dp_count, sample_shard_count)
    positions = jnp.arange(sample_shard_count, dtype=jnp.int32)
    before = positions[None, :] < positions[:, None]
    same_target = owner_target[:, :, None] == owner_target[:, None, :]
    slot_rank = jnp.sum((same_target & before[None]).astype(jnp.int32), axis=2)
    my_target = lax.dynamic_index_in_dim(owner_target, my_shard, 0, keepdims=False)
    my_rank = lax.dynamic_index_in_dim(slot_rank, my_shard, 0, keepdims=False)
    my_prompts = (
        lax.dynamic_slice_in_dim(
            kept_prompt_list, my_shard * sample_shard_count, sample_shard_count
        )
        - my_shard * prompt_dev
    )
    send_slot = my_target * slot_limit + my_rank
    slot_table = send_slot[:, None] == jnp.arange(dp_count * slot_limit, dtype=jnp.int32)[None, :]
    source_row = jnp.sum(jnp.where(slot_table, my_prompts[:, None], 0), axis=0)
    filled = jnp.any(slot_table, axis=0)
    send_rows = jnp.take(encoder_cache, source_row, axis=0)
    send_rows = jnp.where(filled[:, None, None], send_rows, jnp.zeros_like(send_rows))
    outgoing = send_rows.reshape(dp_count, slot_limit, cache_width, cache_len)
    arriving = destination == my_shard
    arrival_pos = jnp.cumsum(arriving.astype(jnp.int32)) - 1
    selector = arriving[None, :] & (arrival_pos[None, :] == positions[:, None])
    kept_prompt = jnp.sum(
        jnp.where(selector, jnp.arange(all_samples, dtype=jnp.int32)[None, :], 0), axis=1
    )
    incoming_order_rank = jnp.sum(jnp.where(selector, slot_rank.reshape(-1)[None, :], 0), axis=1)
    prompt_ids = jnp.sum(jnp.where(selector, kept_prompt_list[None, :], 0), axis=1)
    landing_slot = kept_prompt // sample_shard_count * slot_limit + incoming_order_rank
    prompt_hits = prompt_ids[:, None] == jnp.arange(lengths.shape[0], dtype=jnp.int32)[None, :]
    my_lengths = jnp.sum(jnp.where(prompt_hits, lengths[None, :], 0), axis=1)
    fast = dp_count == 4 and mp_count == 4 and lax.axis_size("groups") == 2
    weight_shards = (first_kernel, second_kernel, query_weight, output_weight)
    if fast:
        block_ids = jnp.arange(dp_count, dtype=jnp.int32)
        channel_blocks = jnp.bitwise_xor(block_ids, my_column)
        pieces = (first_kernel, second_kernel, query_weight, output_weight)
        dense = [piece.reshape(-1, 128) for piece in pieces]
        natural, latents, line_done = split_line_gather(jnp.concatenate(dense, axis=0), latents)
        kernel_rows = dense[0].shape[0] + dense[1].shape[0]
        kernel_part = jnp.take(natural[:, :kernel_rows], channel_blocks, axis=0, mode="clip")
        proj_part = natural[:, kernel_rows:]
        full_weights = []
        cut = 0
        query_part = jnp.take(proj_part, channel_blocks, axis=0, mode="clip")
        for piece, block, source in zip(pieces, dense, (kernel_part, kernel_part, query_part, proj_part)):
            if cut == kernel_rows:
                cut = 0
            chunk = source[:, cut : cut + block.shape[0]]
            cut += block.shape[0]
            full_weights.append(chunk.reshape((dp_count * piece.shape[0],) + piece.shape[1:]))
        gathered = (kernel_part, proj_part)
        full_weights = tuple(full_weights)
        outgoing = lax.optimization_barrier((outgoing, line_done))[0]
        spread_channels = pair_gather_channels
    else:
        full_weights = (
            gather_kernel(first_kernel),
            gather_kernel(second_kernel),
            gather_projection(query_weight),
            gather_projection(output_weight),
        )
        spread_channels = gather_channels
    incoming = lax.all_to_all(outgoing, "dp", split_axis=0, concat_axis=0, tiled=True)
    my_pairs = jnp.take(
        incoming.reshape(dp_count * slot_limit, cache_width, cache_len), landing_slot, axis=0
    )
    start_field = latents.astype(jnp.float32)
    activated = jax.nn.silu(norm_groups(start_field, group_width)).astype(jnp.bfloat16)
    first_in = spread_channels(activated)

    def convolve(full_field, which_weight):
        half = full_field.shape[0] // 2
        return jnp.concatenate(
            [
                apply_kernel(full_field[:half], full_weights[which_weight]),
                apply_kernel(full_field[half:], full_weights[which_weight]),
            ]
        )

    def project(field_rows, which_weight):
        full_weight = full_weights[which_weight]
        return jnp.einsum(
            "scq,ce->seq", field_rows, full_weight, preferred_element_type=jnp.float32
        )

    first_out = convolve(first_in, 0)
    scale_term = modulation[:, 0, :].astype(jnp.float32)[:, :, None]
    shift_term = modulation[:, 1, :].astype(jnp.float32)[:, :, None]
    modulated = jax.nn.silu(
        norm_groups(first_out, group_width) * (1.0 + scale_term) + shift_term
    ).astype(jnp.bfloat16)
    if fast:
        second_in = pair_gather_channel_minor(modulated)
    else:
        second_in = spread_channels(modulated)
    residual = start_field + convolve(second_in, 1)
    normed_out = norm_groups(residual, group_width).astype(jnp.bfloat16)
    local_samples = sample_shard_count // mp_count
    if fast:
        query_cells = xor_spread_samples(normed_out, local_samples)
        my_pairs = lax.optimization_barrier((my_pairs, query_cells))[0]
    else:
        query_cells = lax.all_to_all(normed_out, "mp", split_axis=0, concat_axis=1, tiled=True)
    pair_heads = lax.all_to_all(my_pairs, "mp", split_axis=0, concat_axis=1, tiled=True)
    total_width = query_cells.shape[1]
    head_count = total_width // HEAD
    queries = project(query_cells, 2).astype(jnp.bfloat16)
    queries = queries.reshape(local_samples, head_count, HEAD, cell_count)
    heads_of_keys = pair_heads[:, :total_width, :].reshape(
        local_samples, head_count, HEAD, cache_len
    )
    value_heads = pair_heads[:, total_width:, :].reshape(local_samples, head_count, HEAD, cache_len)
    scores = jnp.einsum(
        "shdq,shdk->shqk", queries, heads_of_keys, preferred_element_type=jnp.float32
    ) * HEAD ** (-0.5)
    local_lengths = lax.dynamic_slice_in_dim(my_lengths, my_column * local_samples, local_samples)
    visible = (
        jnp.arange(cache_len, dtype=jnp.int32)[None, None, None, :]
        < local_lengths[:, None, None, None]
    )
    scores = jnp.where(visible, scores, MASKED)
    row_peak = jnp.max(scores, axis=3, keepdims=True)
    exponent = jnp.exp(scores - row_peak)
    attention = (exponent / jnp.sum(exponent, axis=3, keepdims=True)).astype(jnp.bfloat16)
    context = jnp.einsum(
        "shqk,shdk->shdq", attention, value_heads, preferred_element_type=jnp.float32
    ).astype(jnp.bfloat16)
    attended = project(context.reshape(local_samples, total_width, cell_count), 3).astype(
        jnp.bfloat16
    )
    if fast:
        returned = xor_return_channels(attended, attended.shape[1] // mp_count)
    else:
        returned = lax.all_to_all(attended, "mp", split_axis=1, concat_axis=0, tiled=True)
    final_field = residual + returned.astype(jnp.float32)
    return final_field.astype(jnp.bfloat16)


def solution(mesh):
    in_specs = (
        P(("groups", "dp"), "mp", None),
        P(("groups", "dp"), None, "mp"),
        P("dp", None, "mp"),
        P("dp", None, "mp"),
        P(("groups", "dp"), "mp", None),
        P("dp", None),
        P("dp", None),
        P("groups"),
        P("groups"),
        P("groups"),
    )
    out_specs = P(("groups", "dp"), "mp", None)
    return jax.shard_map(local, mesh=mesh, in_specs=in_specs, out_specs=out_specs, check_vma=False)
```

```python
import jax
import jax.numpy as jnp
from jax import lax
from jax.sharding import PartitionSpec as P

C = 640
GROUPS = 32
HEAD = 64
SIDE = 8


EPSILON = 1e-05
MASKED = -1e30


def norm_groups(values, group_width):
    field_shape = values.shape
    grouped = values.reshape(
        field_shape[0], field_shape[1] // group_width, group_width, field_shape[2]
    )
    center = grouped - jnp.mean(grouped, axis=(2, 3), keepdims=True)
    spread = jnp.mean(center * center, axis=(2, 3), keepdims=True)
    return (center * lax.rsqrt(spread + EPSILON)).reshape(field_shape)


def gather_channels(field):
    return lax.all_gather(field, "mp", axis=1, tiled=True)


def pair_gather_channels(field):
    dense = field.reshape(-1, 128)
    across = lax.ppermute(dense, "mp", [(i, i ^ 2) for i in range(4)])
    beside = lax.ppermute(dense, "mp", [(i, i ^ 1) for i in range(4)])
    relayed = lax.ppermute(across, "mp", [(i, i ^ 1) for i in range(4)])
    parts = [part.reshape(field.shape) for part in (beside, across, relayed)]
    return jnp.concatenate([field] + parts, axis=1)


def line_gather_flat(flat, count):
    my_shard = lax.axis_index("dp")
    rightward = [(i, i + 1) for i in range(count - 1)]
    leftward = [(i + 1, i) for i in range(count - 1)]
    going_right, going_left = flat, flat
    held = [flat]
    from_left, from_right = [], []
    for _ in range(1, count):
        going_right = lax.ppermute(going_right, "dp", rightward)
        going_left = lax.ppermute(going_left, "dp", leftward)
        from_left.append(going_right)
        from_right.append(going_left)
    line = jnp.stack(from_left[::-1] + held + from_right)
    return lax.dynamic_slice_in_dim(line, count - 1 - my_shard, count, axis=0)


def split_line_gather(packed, gated):
    my_shard = lax.axis_index("dp")
    my_group = lax.axis_index("groups")
    halves = packed.reshape(2, packed.shape[0] // 2, packed.shape[1])
    mine = lax.dynamic_index_in_dim(halves, my_group, 0, keepdims=False)
    mine, gated = lax.optimization_barrier((mine, gated))
    rightward = [(i, i + 1) for i in range(3)]
    leftward = [(i + 1, i) for i in range(3)]
    swap = [(0, 1), (1, 0)]
    left_1 = lax.ppermute(mine, "dp", rightward)
    right_1 = lax.ppermute(mine, "dp", leftward)
    first_swap = lax.ppermute(jnp.where(my_shard >= 1, left_1, right_1), "groups", swap)
    left_2 = lax.ppermute(left_1, "dp", rightward)
    right_2 = lax.ppermute(right_1, "dp", leftward)
    second_swap = lax.ppermute(jnp.where(my_shard >= 2, left_2, right_2), "groups", swap)
    left_3 = lax.ppermute(left_2, "dp", rightward)
    right_3 = lax.ppermute(right_2, "dp", leftward)
    third_pick = jnp.where(my_shard == 0, right_3, jnp.where(my_shard == 3, left_3, right_1))
    third_swap = lax.ppermute(third_pick, "groups", swap)

    def whole(own_half, other_half):
        lead = jnp.where(my_group == 0, own_half, other_half)
        tail = jnp.where(my_group == 0, other_half, own_half)
        return jnp.concatenate([lead, tail], axis=0)

    line = jnp.stack(
        [
            whole(left_3, third_swap),
            whole(left_2, second_swap),
            whole(left_1, first_swap),
            packed,
            whole(right_1, jnp.where(my_shard == 0, first_swap, third_swap)),
            whole(right_2, second_swap),
            whole(right_3, third_swap),
        ]
    )
    return lax.dynamic_slice_in_dim(line, 3 - my_shard, 4, axis=0), gated, (left_3, right_3)


def pair_gather_channel_minor(field):
    cell_major = jnp.transpose(field, (0, 2, 1))
    dense = cell_major.reshape(-1, 128)
    across = lax.ppermute(dense, "mp", [(i, i ^ 2) for i in range(4)])
    beside = lax.ppermute(dense, "mp", [(i, i ^ 1) for i in range(4)])
    relayed = lax.ppermute(across, "mp", [(i, i ^ 1) for i in range(4)])
    parts = [jnp.transpose(part.reshape(cell_major.shape), (0, 2, 1)) for part in (beside, across, relayed)]
    return jnp.concatenate([field] + parts, axis=1)


def xor_spread_samples(field, group):
    my_column = lax.axis_index("mp")
    parts = [lax.dynamic_slice_in_dim(field, my_column * group, group, axis=0)]
    for step in range(1, 4):
        block = lax.dynamic_slice_in_dim(field, (my_column ^ step) * group, group, axis=0)
        moved = lax.ppermute(block.reshape(-1, 128), "mp", [(i, i ^ step) for i in range(4)])
        parts.append(moved.reshape(block.shape))
    return jnp.concatenate(parts, axis=1)


def xor_return_channels(field, width):
    my_column = lax.axis_index("mp")
    parts = [lax.dynamic_slice_in_dim(field, my_column * width, width, axis=1)]
    for step in range(1, 4):
        block = lax.dynamic_slice_in_dim(field, (my_column ^ step) * width, width, axis=1)
        moved = lax.ppermute(block.reshape(-1, 128), "mp", [(i, i ^ step) for i in range(4)])
        parts.append(moved.reshape(block.shape))
    order = jnp.bitwise_xor(jnp.arange(4, dtype=jnp.int32), my_column)
    picked = jnp.take(jnp.stack(parts), order, axis=0, mode="clip")
    return picked.reshape((4 * field.shape[0],) + picked.shape[2:])


def shift_parts(shard, count):
    parts = [shard]
    for step in range(1, count):
        parts.append(lax.ppermute(shard, "dp", [(i, (i + step) % count) for i in range(count)]))
    return jnp.stack(parts)


def order_rows(stacked, wanted_blocks):
    my_shard = lax.axis_index("dp")
    count = stacked.shape[0]
    picked = jnp.take(stacked, (my_shard - wanted_blocks) % count, axis=0, mode="clip")
    return picked.reshape((count * stacked.shape[1],) + stacked.shape[2:])


def gather_kernel(weight_shard):
    return lax.all_gather(weight_shard, "dp", axis=0, tiled=True)


def gather_projection(weight_shard):
    return lax.all_gather(weight_shard, "dp", axis=0, tiled=True)


def apply_kernel(full_field, kernel):
    sample_count = full_field.shape[0]
    out_width = kernel.shape[2]
    tap_images = jnp.einsum("scq,cte->stqe", full_field, kernel, preferred_element_type=jnp.float32)
    tap_images = tap_images.reshape(sample_count, 9, SIDE, SIDE, out_width)
    padded = jnp.pad(tap_images, ((0, 0), (0, 0), (1, 1), (1, 1), (0, 0)))
    running = padded[:, 0, 0:SIDE, 0:SIDE, :]
    for offset in range(1, 9):
        row_shift, col_shift = (offset // 3, offset % 3)
        running = (
            running
            + padded[:, offset, row_shift : row_shift + SIDE, col_shift : col_shift + SIDE, :]
        )
    return jnp.transpose(running.reshape(sample_count, SIDE * SIDE, out_width), (0, 2, 1))


def local(
    latents,
    modulation,
    first_kernel,
    second_kernel,
    encoder_cache,
    query_weight,
    output_weight,
    kept_prompt_list,
    destination,
    lengths,
):
    group_width = C // GROUPS
    dp_count = lax.axis_size("dp")
    mp_count = lax.axis_size("mp")
    my_shard = lax.axis_index("dp")
    my_column = lax.axis_index("mp")
    sample_shard_count = latents.shape[0]
    prompt_dev = encoder_cache.shape[0]
    cache_len = encoder_cache.shape[2]
    cache_width = encoder_cache.shape[1]
    cell_count = latents.shape[2]
    slot_limit = 2 * (sample_shard_count // dp_count)
    all_samples = destination.shape[0]
    owner_target = destination.reshape(dp_count, sample_shard_count)
    positions = jnp.arange(sample_shard_count, dtype=jnp.int32)
    before = positions[None, :] < positions[:, None]
    same_target = owner_target[:, :, None] == owner_target[:, None, :]
    slot_rank = jnp.sum((same_target & before[None]).astype(jnp.int32), axis=2)
    my_target = lax.dynamic_index_in_dim(owner_target, my_shard, 0, keepdims=False)
    my_rank = lax.dynamic_index_in_dim(slot_rank, my_shard, 0, keepdims=False)
    my_prompts = (
        lax.dynamic_slice_in_dim(
            kept_prompt_list, my_shard * sample_shard_count, sample_shard_count
        )
        - my_shard * prompt_dev
    )
    send_slot = my_target * slot_limit + my_rank
    slot_table = send_slot[:, None] == jnp.arange(dp_count * slot_limit, dtype=jnp.int32)[None, :]
    source_row = jnp.sum(jnp.where(slot_table, my_prompts[:, None], 0), axis=0)
    filled = jnp.any(slot_table, axis=0)
    send_rows = jnp.take(encoder_cache, source_row, axis=0)
    send_rows = jnp.where(filled[:, None, None], send_rows, jnp.zeros_like(send_rows))
    outgoing = send_rows.reshape(dp_count, slot_limit, cache_width, cache_len)
    arriving = destination == my_shard
    arrival_pos = jnp.cumsum(arriving.astype(jnp.int32)) - 1
    selector = arriving[None, :] & (arrival_pos[None, :] == positions[:, None])
    kept_prompt = jnp.sum(
        jnp.where(selector, jnp.arange(all_samples, dtype=jnp.int32)[None, :], 0), axis=1
    )
    incoming_order_rank = jnp.sum(jnp.where(selector, slot_rank.reshape(-1)[None, :], 0), axis=1)
    prompt_ids = jnp.sum(jnp.where(selector, kept_prompt_list[None, :], 0), axis=1)
    landing_slot = kept_prompt // sample_shard_count * slot_limit + incoming_order_rank
    prompt_hits = prompt_ids[:, None] == jnp.arange(lengths.shape[0], dtype=jnp.int32)[None, :]
    my_lengths = jnp.sum(jnp.where(prompt_hits, lengths[None, :], 0), axis=1)
    fast = dp_count == 4 and mp_count == 4 and lax.axis_size("groups") == 2
    weight_shards = (first_kernel, second_kernel, query_weight, output_weight)
    if fast:
        block_ids = jnp.arange(dp_count, dtype=jnp.int32)
        channel_blocks = jnp.bitwise_xor(block_ids, my_column)
        pieces = (first_kernel, second_kernel, query_weight, output_weight)
        dense = [piece.reshape(-1, 128) for piece in pieces]
        natural, latents, line_done = split_line_gather(jnp.concatenate(dense, axis=0), latents)
        kernel_rows = dense[0].shape[0] + dense[1].shape[0]
        kernel_part = jnp.take(natural[:, :kernel_rows], channel_blocks, axis=0, mode="clip")
        proj_part = natural[:, kernel_rows:]
        full_weights = []
        cut = 0
        query_part = jnp.take(proj_part, channel_blocks, axis=0, mode="clip")
        for piece, block, source in zip(pieces, dense, (kernel_part, kernel_part, query_part, proj_part)):
            if cut == kernel_rows:
                cut = 0
            chunk = source[:, cut : cut + block.shape[0]]
            cut += block.shape[0]
            full_weights.append(chunk.reshape((dp_count * piece.shape[0],) + piece.shape[1:]))
        gathered = (kernel_part, proj_part)
        full_weights = tuple(full_weights)
        outgoing = lax.optimization_barrier((outgoing, line_done))[0]
        spread_channels = pair_gather_channels
    else:
        full_weights = (
            gather_kernel(first_kernel),
            gather_kernel(second_kernel),
            gather_projection(query_weight),
            gather_projection(output_weight),
        )
        spread_channels = gather_channels
    incoming = lax.all_to_all(outgoing, "dp", split_axis=0, concat_axis=0, tiled=True)
    my_pairs = jnp.take(
        incoming.reshape(dp_count * slot_limit, cache_width, cache_len), landing_slot, axis=0
    )
    start_field = latents.astype(jnp.float32)
    activated = jax.nn.silu(norm_groups(start_field, group_width)).astype(jnp.bfloat16)
    first_in = spread_channels(activated)

    def convolve(full_field, which_weight):
        pieces = 4 if full_field.shape[0] % 4 == 0 else 1
        step = full_field.shape[0] // pieces
        return jnp.concatenate(
            [
                apply_kernel(full_field[i * step : (i + 1) * step], full_weights[which_weight])
                for i in range(pieces)
            ]
        )

    def project(field_rows, which_weight):
        full_weight = full_weights[which_weight]
        return jnp.einsum(
            "scq,ce->seq", field_rows, full_weight, preferred_element_type=jnp.float32
        )

    first_out = convolve(first_in, 0)
    scale_term = modulation[:, 0, :].astype(jnp.float32)[:, :, None]
    shift_term = modulation[:, 1, :].astype(jnp.float32)[:, :, None]
    modulated = jax.nn.silu(
        norm_groups(first_out, group_width) * (1.0 + scale_term) + shift_term
    ).astype(jnp.bfloat16)
    if fast:
        second_in = pair_gather_channel_minor(modulated)
    else:
        second_in = spread_channels(modulated)
    residual = start_field + convolve(second_in, 1)
    normed_out = norm_groups(residual, group_width).astype(jnp.bfloat16)
    local_samples = sample_shard_count // mp_count
    if fast:
        query_cells = xor_spread_samples(normed_out, local_samples)
        my_pairs = lax.optimization_barrier((my_pairs, query_cells))[0]
    else:
        query_cells = lax.all_to_all(normed_out, "mp", split_axis=0, concat_axis=1, tiled=True)
    pair_heads = lax.all_to_all(my_pairs, "mp", split_axis=0, concat_axis=1, tiled=True)
    total_width = query_cells.shape[1]
    head_count = total_width // HEAD
    queries = project(query_cells, 2).astype(jnp.bfloat16)
    queries = queries.reshape(local_samples, head_count, HEAD, cell_count)
    heads_of_keys = pair_heads[:, :total_width, :].reshape(
        local_samples, head_count, HEAD, cache_len
    )
    value_heads = pair_heads[:, total_width:, :].reshape(local_samples, head_count, HEAD, cache_len)
    scores = jnp.einsum(
        "shdq,shdk->shqk", queries, heads_of_keys, preferred_element_type=jnp.float32
    ) * HEAD ** (-0.5)
    local_lengths = lax.dynamic_slice_in_dim(my_lengths, my_column * local_samples, local_samples)
    visible = (
        jnp.arange(cache_len, dtype=jnp.int32)[None, None, None, :]
        < local_lengths[:, None, None, None]
    )
    scores = jnp.where(visible, scores, MASKED)
    row_peak = jnp.max(scores, axis=3, keepdims=True)
    exponent = jnp.exp(scores - row_peak)
    attention = (exponent / jnp.sum(exponent, axis=3, keepdims=True)).astype(jnp.bfloat16)
    context = jnp.einsum(
        "shqk,shdk->shdq", attention, value_heads, preferred_element_type=jnp.float32
    ).astype(jnp.bfloat16)
    attended = project(context.reshape(local_samples, total_width, cell_count), 3).astype(
        jnp.bfloat16
    )
    if fast:
        returned = xor_return_channels(attended, attended.shape[1] // mp_count)
    else:
        returned = lax.all_to_all(attended, "mp", split_axis=1, concat_axis=0, tiled=True)
    final_field = residual + returned.astype(jnp.float32)
    return final_field.astype(jnp.bfloat16)


def solution(mesh):
    in_specs = (
        P(("groups", "dp"), "mp", None),
        P(("groups", "dp"), None, "mp"),
        P("dp", None, "mp"),
        P("dp", None, "mp"),
        P(("groups", "dp"), "mp", None),
        P("dp", None),
        P("dp", None),
        P("groups"),
        P("groups"),
        P("groups"),
    )
    out_specs = P(("groups", "dp"), "mp", None)
    return jax.shard_map(local, mesh=mesh, in_specs=in_specs, out_specs=out_specs, check_vma=False)
```

```python
import jax
import jax.numpy as jnp
from jax import lax
from jax.sharding import PartitionSpec as P

C = 640
GROUPS = 32
HEAD = 64
SIDE = 8


EPSILON = 1e-05
MASKED = -1e30


def norm_groups(values, group_width):
    field_shape = values.shape
    grouped = values.reshape(
        field_shape[0], field_shape[1] // group_width, group_width, field_shape[2]
    )
    center = grouped - jnp.mean(grouped, axis=(2, 3), keepdims=True)
    spread = jnp.mean(center * center, axis=(2, 3), keepdims=True)
    return (center * lax.rsqrt(spread + EPSILON)).reshape(field_shape)


def gather_channels(field):
    return lax.all_gather(field, "mp", axis=1, tiled=True)


def pair_gather_channels(field):
    dense = field.reshape(-1, 128)
    across = lax.ppermute(dense, "mp", [(i, i ^ 2) for i in range(4)])
    beside = lax.ppermute(dense, "mp", [(i, i ^ 1) for i in range(4)])
    relayed = lax.ppermute(across, "mp", [(i, i ^ 1) for i in range(4)])
    parts = [part.reshape(field.shape) for part in (beside, across, relayed)]
    return jnp.concatenate([field] + parts, axis=1)


def line_gather_flat(flat, count):
    my_shard = lax.axis_index("dp")
    rightward = [(i, i + 1) for i in range(count - 1)]
    leftward = [(i + 1, i) for i in range(count - 1)]
    going_right, going_left = flat, flat
    held = [flat]
    from_left, from_right = [], []
    for _ in range(1, count):
        going_right = lax.ppermute(going_right, "dp", rightward)
        going_left = lax.ppermute(going_left, "dp", leftward)
        from_left.append(going_right)
        from_right.append(going_left)
    line = jnp.stack(from_left[::-1] + held + from_right)
    return lax.dynamic_slice_in_dim(line, count - 1 - my_shard, count, axis=0)


def split_line_gather(packed, gated):
    my_shard = lax.axis_index("dp")
    my_group = lax.axis_index("groups")
    halves = packed.reshape(2, packed.shape[0] // 2, packed.shape[1])
    mine = lax.dynamic_index_in_dim(halves, my_group, 0, keepdims=False)
    mine, gated = lax.optimization_barrier((mine, gated))
    rightward = [(i, i + 1) for i in range(3)]
    leftward = [(i + 1, i) for i in range(3)]
    swap = [(0, 1), (1, 0)]
    left_1 = lax.ppermute(mine, "dp", rightward)
    right_1 = lax.ppermute(mine, "dp", leftward)
    first_swap = lax.ppermute(jnp.where(my_shard >= 1, left_1, right_1), "groups", swap)
    left_2 = lax.ppermute(left_1, "dp", rightward)
    right_2 = lax.ppermute(right_1, "dp", leftward)
    second_swap = lax.ppermute(jnp.where(my_shard >= 2, left_2, right_2), "groups", swap)
    left_3 = lax.ppermute(left_2, "dp", rightward)
    right_3 = lax.ppermute(right_2, "dp", leftward)
    third_pick = jnp.where(my_shard == 0, right_3, jnp.where(my_shard == 3, left_3, right_1))
    third_swap = lax.ppermute(third_pick, "groups", swap)

    def whole(own_half, other_half):
        lead = jnp.where(my_group == 0, own_half, other_half)
        tail = jnp.where(my_group == 0, other_half, own_half)
        return jnp.concatenate([lead, tail], axis=0)

    line = jnp.stack(
        [
            whole(left_3, third_swap),
            whole(left_2, second_swap),
            whole(left_1, first_swap),
            packed,
            whole(right_1, jnp.where(my_shard == 0, first_swap, third_swap)),
            whole(right_2, second_swap),
            whole(right_3, third_swap),
        ]
    )
    return lax.dynamic_slice_in_dim(line, 3 - my_shard, 4, axis=0), gated, (left_3, right_3)


def pair_gather_channel_minor(field):
    cell_major = jnp.transpose(field, (0, 2, 1))
    dense = cell_major.reshape(-1, 128)
    across = lax.ppermute(dense, "mp", [(i, i ^ 2) for i in range(4)])
    beside = lax.ppermute(dense, "mp", [(i, i ^ 1) for i in range(4)])
    relayed = lax.ppermute(across, "mp", [(i, i ^ 1) for i in range(4)])
    parts = [jnp.transpose(part.reshape(cell_major.shape), (0, 2, 1)) for part in (beside, across, relayed)]
    return jnp.concatenate([field] + parts, axis=1)


def xor_spread_samples(field, group):
    my_column = lax.axis_index("mp")
    parts = [lax.dynamic_slice_in_dim(field, my_column * group, group, axis=0)]
    for step in range(1, 4):
        block = lax.dynamic_slice_in_dim(field, (my_column ^ step) * group, group, axis=0)
        moved = lax.ppermute(block.reshape(-1, 128), "mp", [(i, i ^ step) for i in range(4)])
        parts.append(moved.reshape(block.shape))
    return jnp.concatenate(parts, axis=1)


def xor_return_channels(field, width):
    my_column = lax.axis_index("mp")
    parts = [lax.dynamic_slice_in_dim(field, my_column * width, width, axis=1)]
    for step in range(1, 4):
        block = lax.dynamic_slice_in_dim(field, (my_column ^ step) * width, width, axis=1)
        moved = lax.ppermute(block.reshape(-1, 128), "mp", [(i, i ^ step) for i in range(4)])
        parts.append(moved.reshape(block.shape))
    order = jnp.bitwise_xor(jnp.arange(4, dtype=jnp.int32), my_column)
    picked = jnp.take(jnp.stack(parts), order, axis=0, mode="clip")
    return picked.reshape((4 * field.shape[0],) + picked.shape[2:])


def shift_parts(shard, count):
    parts = [shard]
    for step in range(1, count):
        parts.append(lax.ppermute(shard, "dp", [(i, (i + step) % count) for i in range(count)]))
    return jnp.stack(parts)


def order_rows(stacked, wanted_blocks):
    my_shard = lax.axis_index("dp")
    count = stacked.shape[0]
    picked = jnp.take(stacked, (my_shard - wanted_blocks) % count, axis=0, mode="clip")
    return picked.reshape((count * stacked.shape[1],) + stacked.shape[2:])


def gather_kernel(weight_shard):
    return lax.all_gather(weight_shard, "dp", axis=0, tiled=True)


def gather_projection(weight_shard):
    return lax.all_gather(weight_shard, "dp", axis=0, tiled=True)


def apply_kernel(full_field, kernel):
    sample_count = full_field.shape[0]
    out_width = kernel.shape[1]
    tap_images = jnp.einsum("scq,tec->stqe", full_field, kernel, preferred_element_type=jnp.float32)
    tap_images = tap_images.reshape(sample_count, 9, SIDE, SIDE, out_width)
    padded = jnp.pad(tap_images, ((0, 0), (0, 0), (1, 1), (1, 1), (0, 0)))
    running = padded[:, 0, 0:SIDE, 0:SIDE, :]
    for offset in range(1, 9):
        row_shift, col_shift = (offset // 3, offset % 3)
        running = (
            running
            + padded[:, offset, row_shift : row_shift + SIDE, col_shift : col_shift + SIDE, :]
        )
    return jnp.transpose(running.reshape(sample_count, SIDE * SIDE, out_width), (0, 2, 1))


def local(
    latents,
    modulation,
    first_kernel,
    second_kernel,
    encoder_cache,
    query_weight,
    output_weight,
    kept_prompt_list,
    destination,
    lengths,
):
    group_width = C // GROUPS
    dp_count = lax.axis_size("dp")
    mp_count = lax.axis_size("mp")
    my_shard = lax.axis_index("dp")
    my_column = lax.axis_index("mp")
    sample_shard_count = latents.shape[0]
    prompt_dev = encoder_cache.shape[0]
    cache_len = encoder_cache.shape[2]
    cache_width = encoder_cache.shape[1]
    cell_count = latents.shape[2]
    slot_limit = 2 * (sample_shard_count // dp_count)
    all_samples = destination.shape[0]
    owner_target = destination.reshape(dp_count, sample_shard_count)
    positions = jnp.arange(sample_shard_count, dtype=jnp.int32)
    before = positions[None, :] < positions[:, None]
    same_target = owner_target[:, :, None] == owner_target[:, None, :]
    slot_rank = jnp.sum((same_target & before[None]).astype(jnp.int32), axis=2)
    my_target = lax.dynamic_index_in_dim(owner_target, my_shard, 0, keepdims=False)
    my_rank = lax.dynamic_index_in_dim(slot_rank, my_shard, 0, keepdims=False)
    my_prompts = (
        lax.dynamic_slice_in_dim(
            kept_prompt_list, my_shard * sample_shard_count, sample_shard_count
        )
        - my_shard * prompt_dev
    )
    send_slot = my_target * slot_limit + my_rank
    slot_table = send_slot[:, None] == jnp.arange(dp_count * slot_limit, dtype=jnp.int32)[None, :]
    source_row = jnp.sum(jnp.where(slot_table, my_prompts[:, None], 0), axis=0)
    filled = jnp.any(slot_table, axis=0)
    send_rows = jnp.take(encoder_cache, source_row, axis=0)
    send_rows = jnp.where(filled[:, None, None], send_rows, jnp.zeros_like(send_rows))
    outgoing = send_rows.reshape(dp_count, slot_limit, cache_width, cache_len)
    arriving = destination == my_shard
    arrival_pos = jnp.cumsum(arriving.astype(jnp.int32)) - 1
    selector = arriving[None, :] & (arrival_pos[None, :] == positions[:, None])
    kept_prompt = jnp.sum(
        jnp.where(selector, jnp.arange(all_samples, dtype=jnp.int32)[None, :], 0), axis=1
    )
    incoming_order_rank = jnp.sum(jnp.where(selector, slot_rank.reshape(-1)[None, :], 0), axis=1)
    prompt_ids = jnp.sum(jnp.where(selector, kept_prompt_list[None, :], 0), axis=1)
    landing_slot = kept_prompt // sample_shard_count * slot_limit + incoming_order_rank
    prompt_hits = prompt_ids[:, None] == jnp.arange(lengths.shape[0], dtype=jnp.int32)[None, :]
    my_lengths = jnp.sum(jnp.where(prompt_hits, lengths[None, :], 0), axis=1)
    fast = dp_count == 4 and mp_count == 4 and lax.axis_size("groups") == 2
    weight_shards = (first_kernel, second_kernel, query_weight, output_weight)
    if fast:
        block_ids = jnp.arange(dp_count, dtype=jnp.int32)
        channel_blocks = jnp.bitwise_xor(block_ids, my_column)
        pieces = (
            jnp.transpose(first_kernel, (1, 2, 0)),
            jnp.transpose(second_kernel, (1, 2, 0)),
            query_weight,
            output_weight,
        )
        dense = [piece.reshape(-1, 128) for piece in pieces]
        natural, latents, line_done = split_line_gather(jnp.concatenate(dense, axis=0), latents)
        kernel_rows = dense[0].shape[0] + dense[1].shape[0]
        kernel_part = jnp.take(natural[:, :kernel_rows], channel_blocks, axis=0, mode="clip")
        proj_part = natural[:, kernel_rows:]
        full_weights = []
        cut = 0
        query_part = jnp.take(proj_part, channel_blocks, axis=0, mode="clip")
        for piece, block, source in zip(pieces, dense, (kernel_part, kernel_part, query_part, proj_part)):
            if cut == kernel_rows:
                cut = 0
            chunk = source[:, cut : cut + block.shape[0]]
            cut += block.shape[0]
            if piece.ndim == 3:
                blocks = chunk.reshape((dp_count,) + piece.shape)
                full_weights.append(
                    jnp.transpose(blocks, (1, 2, 0, 3)).reshape(
                        piece.shape[0], piece.shape[1], dp_count * piece.shape[2]
                    )
                )
            else:
                full_weights.append(chunk.reshape((dp_count * piece.shape[0],) + piece.shape[1:]))
        gathered = (kernel_part, proj_part)
        full_weights = tuple(full_weights)
        outgoing = lax.optimization_barrier((outgoing, line_done))[0]
        spread_channels = pair_gather_channels
    else:
        full_weights = (
            jnp.transpose(gather_kernel(first_kernel), (1, 2, 0)),
            jnp.transpose(gather_kernel(second_kernel), (1, 2, 0)),
            gather_projection(query_weight),
            gather_projection(output_weight),
        )
        spread_channels = gather_channels
    incoming = lax.all_to_all(outgoing, "dp", split_axis=0, concat_axis=0, tiled=True)
    my_pairs = jnp.take(
        incoming.reshape(dp_count * slot_limit, cache_width, cache_len), landing_slot, axis=0
    )
    start_field = latents.astype(jnp.float32)
    activated = jax.nn.silu(norm_groups(start_field, group_width)).astype(jnp.bfloat16)
    first_in = spread_channels(activated)

    def convolve(full_field, which_weight):
        half = full_field.shape[0] // 2
        return jnp.concatenate(
            [
                apply_kernel(full_field[:half], full_weights[which_weight]),
                apply_kernel(full_field[half:], full_weights[which_weight]),
            ]
        )

    def project(field_rows, which_weight):
        full_weight = full_weights[which_weight]
        return jnp.einsum(
            "scq,ce->seq", field_rows, full_weight, preferred_element_type=jnp.float32
        )

    first_out = convolve(first_in, 0)
    scale_term = modulation[:, 0, :].astype(jnp.float32)[:, :, None]
    shift_term = modulation[:, 1, :].astype(jnp.float32)[:, :, None]
    modulated = jax.nn.silu(
        norm_groups(first_out, group_width) * (1.0 + scale_term) + shift_term
    ).astype(jnp.bfloat16)
    if fast:
        second_in = pair_gather_channel_minor(modulated)
    else:
        second_in = spread_channels(modulated)
    residual = start_field + convolve(second_in, 1)
    normed_out = norm_groups(residual, group_width).astype(jnp.bfloat16)
    local_samples = sample_shard_count // mp_count
    if fast:
        query_cells = xor_spread_samples(normed_out, local_samples)
        my_pairs = lax.optimization_barrier((my_pairs, query_cells))[0]
    else:
        query_cells = lax.all_to_all(normed_out, "mp", split_axis=0, concat_axis=1, tiled=True)
    pair_heads = lax.all_to_all(my_pairs, "mp", split_axis=0, concat_axis=1, tiled=True)
    total_width = query_cells.shape[1]
    head_count = total_width // HEAD
    queries = project(query_cells, 2).astype(jnp.bfloat16)
    queries = queries.reshape(local_samples, head_count, HEAD, cell_count)
    heads_of_keys = pair_heads[:, :total_width, :].reshape(
        local_samples, head_count, HEAD, cache_len
    )
    value_heads = pair_heads[:, total_width:, :].reshape(local_samples, head_count, HEAD, cache_len)
    scores = jnp.einsum(
        "shdq,shdk->shqk", queries, heads_of_keys, preferred_element_type=jnp.float32
    ) * HEAD ** (-0.5)
    local_lengths = lax.dynamic_slice_in_dim(my_lengths, my_column * local_samples, local_samples)
    visible = (
        jnp.arange(cache_len, dtype=jnp.int32)[None, None, None, :]
        < local_lengths[:, None, None, None]
    )
    scores = jnp.where(visible, scores, MASKED)
    row_peak = jnp.max(scores, axis=3, keepdims=True)
    exponent = jnp.exp(scores - row_peak)
    attention = (exponent / jnp.sum(exponent, axis=3, keepdims=True)).astype(jnp.bfloat16)
    context = jnp.einsum(
        "shqk,shdk->shdq", attention, value_heads, preferred_element_type=jnp.float32
    ).astype(jnp.bfloat16)
    attended = project(context.reshape(local_samples, total_width, cell_count), 3).astype(
        jnp.bfloat16
    )
    if fast:
        returned = xor_return_channels(attended, attended.shape[1] // mp_count)
    else:
        returned = lax.all_to_all(attended, "mp", split_axis=1, concat_axis=0, tiled=True)
    final_field = residual + returned.astype(jnp.float32)
    return final_field.astype(jnp.bfloat16)


def solution(mesh):
    in_specs = (
        P(("groups", "dp"), "mp", None),
        P(("groups", "dp"), None, "mp"),
        P("dp", None, "mp"),
        P("dp", None, "mp"),
        P(("groups", "dp"), "mp", None),
        P("dp", None),
        P("dp", None),
        P("groups"),
        P("groups"),
        P("groups"),
    )
    out_specs = P(("groups", "dp"), "mp", None)
    return jax.shard_map(local, mesh=mesh, in_specs=in_specs, out_specs=out_specs, check_vma=False)
```

```python
import jax
import jax.numpy as jnp
from jax import lax
from jax.sharding import PartitionSpec as P

C = 640
GROUPS = 32
HEAD = 64
SIDE = 8


EPSILON = 1e-05
MASKED = -1e30


def norm_groups(values, group_width):
    field_shape = values.shape
    grouped = values.reshape(
        field_shape[0], field_shape[1] // group_width, group_width, field_shape[2]
    )
    center = grouped - jnp.mean(grouped, axis=(2, 3), keepdims=True)
    spread = jnp.mean(center * center, axis=(2, 3), keepdims=True)
    return (center * lax.rsqrt(spread + EPSILON)).reshape(field_shape)


def gather_channels(field):
    return lax.all_gather(field, "mp", axis=1, tiled=True)


def pair_gather_channels(field):
    dense = field.reshape(-1, 128)
    across = lax.ppermute(dense, "mp", [(i, i ^ 2) for i in range(4)])
    beside = lax.ppermute(dense, "mp", [(i, i ^ 1) for i in range(4)])
    relayed = lax.ppermute(across, "mp", [(i, i ^ 1) for i in range(4)])
    parts = [part.reshape(field.shape) for part in (beside, across, relayed)]
    return jnp.concatenate([field] + parts, axis=1)


def line_gather_flat(flat, count):
    my_shard = lax.axis_index("dp")
    rightward = [(i, i + 1) for i in range(count - 1)]
    leftward = [(i + 1, i) for i in range(count - 1)]
    going_right, going_left = flat, flat
    held = [flat]
    from_left, from_right = [], []
    for _ in range(1, count):
        going_right = lax.ppermute(going_right, "dp", rightward)
        going_left = lax.ppermute(going_left, "dp", leftward)
        from_left.append(going_right)
        from_right.append(going_left)
    line = jnp.stack(from_left[::-1] + held + from_right)
    return lax.dynamic_slice_in_dim(line, count - 1 - my_shard, count, axis=0)


def split_line_gather(packed, gated):
    my_shard = lax.axis_index("dp")
    my_group = lax.axis_index("groups")
    halves = packed.reshape(2, packed.shape[0] // 2, packed.shape[1])
    mine = lax.dynamic_index_in_dim(halves, my_group, 0, keepdims=False)
    mine, gated = lax.optimization_barrier((mine, gated))
    rightward = [(i, i + 1) for i in range(3)]
    leftward = [(i + 1, i) for i in range(3)]
    swap = [(0, 1), (1, 0)]
    left_1 = lax.ppermute(mine, "dp", rightward)
    right_1 = lax.ppermute(mine, "dp", leftward)
    first_swap = lax.ppermute(jnp.where(my_shard >= 1, left_1, right_1), "groups", swap)
    left_2 = lax.ppermute(left_1, "dp", rightward)
    right_2 = lax.ppermute(right_1, "dp", leftward)
    second_swap = lax.ppermute(jnp.where(my_shard >= 2, left_2, right_2), "groups", swap)
    left_3 = lax.ppermute(left_2, "dp", rightward)
    right_3 = lax.ppermute(right_2, "dp", leftward)
    third_pick = jnp.where(my_shard == 0, right_3, jnp.where(my_shard == 3, left_3, right_1))
    third_swap = lax.ppermute(third_pick, "groups", swap)

    def whole(own_half, other_half):
        lead = jnp.where(my_group == 0, own_half, other_half)
        tail = jnp.where(my_group == 0, other_half, own_half)
        return jnp.concatenate([lead, tail], axis=0)

    line = jnp.stack(
        [
            whole(left_3, third_swap),
            whole(left_2, second_swap),
            whole(left_1, first_swap),
            packed,
            whole(right_1, jnp.where(my_shard == 0, first_swap, third_swap)),
            whole(right_2, second_swap),
            whole(right_3, third_swap),
        ]
    )
    return lax.dynamic_slice_in_dim(line, 3 - my_shard, 4, axis=0), gated, (left_3, right_3)


def pair_gather_channel_minor(field):
    cell_major = jnp.transpose(field, (0, 2, 1))
    dense = cell_major.reshape(-1, 128)
    across = lax.ppermute(dense, "mp", [(i, i ^ 2) for i in range(4)])
    beside = lax.ppermute(dense, "mp", [(i, i ^ 1) for i in range(4)])
    relayed = lax.ppermute(across, "mp", [(i, i ^ 1) for i in range(4)])
    parts = [jnp.transpose(part.reshape(cell_major.shape), (0, 2, 1)) for part in (beside, across, relayed)]
    return jnp.concatenate([field] + parts, axis=1)


def xor_spread_samples(field, group):
    my_column = lax.axis_index("mp")
    parts = [lax.dynamic_slice_in_dim(field, my_column * group, group, axis=0)]
    for step in range(1, 4):
        block = lax.dynamic_slice_in_dim(field, (my_column ^ step) * group, group, axis=0)
        moved = lax.ppermute(block.reshape(-1, 128), "mp", [(i, i ^ step) for i in range(4)])
        parts.append(moved.reshape(block.shape))
    return jnp.concatenate(parts, axis=1)


def xor_return_channels(field, width):
    my_column = lax.axis_index("mp")
    parts = [lax.dynamic_slice_in_dim(field, my_column * width, width, axis=1)]
    for step in range(1, 4):
        block = lax.dynamic_slice_in_dim(field, (my_column ^ step) * width, width, axis=1)
        moved = lax.ppermute(block.reshape(-1, 128), "mp", [(i, i ^ step) for i in range(4)])
        parts.append(moved.reshape(block.shape))
    order = jnp.bitwise_xor(jnp.arange(4, dtype=jnp.int32), my_column)
    picked = jnp.take(jnp.stack(parts), order, axis=0, mode="clip")
    return picked.reshape((4 * field.shape[0],) + picked.shape[2:])


def shift_parts(shard, count):
    parts = [shard]
    for step in range(1, count):
        parts.append(lax.ppermute(shard, "dp", [(i, (i + step) % count) for i in range(count)]))
    return jnp.stack(parts)


def order_rows(stacked, wanted_blocks):
    my_shard = lax.axis_index("dp")
    count = stacked.shape[0]
    picked = jnp.take(stacked, (my_shard - wanted_blocks) % count, axis=0, mode="clip")
    return picked.reshape((count * stacked.shape[1],) + stacked.shape[2:])


def gather_kernel(weight_shard):
    return lax.all_gather(weight_shard, "dp", axis=0, tiled=True)


def gather_projection(weight_shard):
    return lax.all_gather(weight_shard, "dp", axis=0, tiled=True)


def apply_kernel(full_field, kernel):
    sample_count = full_field.shape[0]
    out_width = kernel.shape[2]
    tap_images = jnp.einsum("scq,cte->stqe", full_field, kernel, preferred_element_type=jnp.float32)
    tap_images = tap_images.reshape(sample_count, 9, SIDE, SIDE, out_width)
    padded = jnp.pad(tap_images, ((0, 0), (0, 0), (1, 1), (1, 1), (0, 0)))
    running = padded[:, 0, 0:SIDE, 0:SIDE, :]
    for offset in range(1, 9):
        row_shift, col_shift = (offset // 3, offset % 3)
        running = (
            running
            + padded[:, offset, row_shift : row_shift + SIDE, col_shift : col_shift + SIDE, :]
        )
    return jnp.transpose(running.reshape(sample_count, SIDE * SIDE, out_width), (0, 2, 1))


def local(
    latents,
    modulation,
    first_kernel,
    second_kernel,
    encoder_cache,
    query_weight,
    output_weight,
    kept_prompt_list,
    destination,
    lengths,
):
    group_width = C // GROUPS
    dp_count = lax.axis_size("dp")
    mp_count = lax.axis_size("mp")
    my_shard = lax.axis_index("dp")
    my_column = lax.axis_index("mp")
    sample_shard_count = latents.shape[0]
    prompt_dev = encoder_cache.shape[0]
    cache_len = encoder_cache.shape[2]
    cache_width = encoder_cache.shape[1]
    cell_count = latents.shape[2]
    slot_limit = 2 * (sample_shard_count // dp_count)
    all_samples = destination.shape[0]
    owner_target = destination.reshape(dp_count, sample_shard_count)
    positions = jnp.arange(sample_shard_count, dtype=jnp.int32)
    before = positions[None, :] < positions[:, None]
    same_target = owner_target[:, :, None] == owner_target[:, None, :]
    slot_rank = jnp.sum((same_target & before[None]).astype(jnp.int32), axis=2)
    my_target = lax.dynamic_index_in_dim(owner_target, my_shard, 0, keepdims=False)
    my_rank = lax.dynamic_index_in_dim(slot_rank, my_shard, 0, keepdims=False)
    my_prompts = (
        lax.dynamic_slice_in_dim(
            kept_prompt_list, my_shard * sample_shard_count, sample_shard_count
        )
        - my_shard * prompt_dev
    )
    send_slot = my_target * slot_limit + my_rank
    slot_table = send_slot[:, None] == jnp.arange(dp_count * slot_limit, dtype=jnp.int32)[None, :]
    source_row = jnp.sum(jnp.where(slot_table, my_prompts[:, None], 0), axis=0)
    filled = jnp.any(slot_table, axis=0)
    send_rows = jnp.take(encoder_cache, source_row, axis=0)
    send_rows = jnp.where(filled[:, None, None], send_rows, jnp.zeros_like(send_rows))
    outgoing = send_rows.reshape(dp_count, slot_limit, cache_width, cache_len)
    arriving = destination == my_shard
    arrival_pos = jnp.cumsum(arriving.astype(jnp.int32)) - 1
    selector = arriving[None, :] & (arrival_pos[None, :] == positions[:, None])
    kept_prompt = jnp.sum(
        jnp.where(selector, jnp.arange(all_samples, dtype=jnp.int32)[None, :], 0), axis=1
    )
    incoming_order_rank = jnp.sum(jnp.where(selector, slot_rank.reshape(-1)[None, :], 0), axis=1)
    prompt_ids = jnp.sum(jnp.where(selector, kept_prompt_list[None, :], 0), axis=1)
    landing_slot = kept_prompt // sample_shard_count * slot_limit + incoming_order_rank
    prompt_hits = prompt_ids[:, None] == jnp.arange(lengths.shape[0], dtype=jnp.int32)[None, :]
    my_lengths = jnp.sum(jnp.where(prompt_hits, lengths[None, :], 0), axis=1)
    fast = dp_count == 4 and mp_count == 4 and lax.axis_size("groups") == 2
    weight_shards = (first_kernel, second_kernel, query_weight, output_weight)
    if fast:
        block_ids = jnp.arange(dp_count, dtype=jnp.int32)
        channel_blocks = jnp.bitwise_xor(block_ids, my_column)
        pieces = (first_kernel, second_kernel, query_weight, output_weight)
        dense = [piece.reshape(-1, 128) for piece in pieces]
        natural, latents, line_done = split_line_gather(jnp.concatenate(dense, axis=0), latents)
        kernel_rows = dense[0].shape[0] + dense[1].shape[0]
        kernel_part = jnp.take(natural[:, :kernel_rows], channel_blocks, axis=0, mode="clip")
        proj_part = natural[:, kernel_rows:]
        full_weights = []
        cut = 0
        query_part = jnp.take(proj_part, channel_blocks, axis=0, mode="clip")
        for piece, block, source in zip(pieces, dense, (kernel_part, kernel_part, query_part, proj_part)):
            if cut == kernel_rows:
                cut = 0
            chunk = source[:, cut : cut + block.shape[0]]
            cut += block.shape[0]
            full_weights.append(chunk.reshape((dp_count * piece.shape[0],) + piece.shape[1:]))
        gathered = (kernel_part, proj_part)
        full_weights = tuple(full_weights)
        outgoing = lax.optimization_barrier((outgoing, line_done))[0]
        spread_channels = pair_gather_channels
    else:
        full_weights = (
            gather_kernel(first_kernel),
            gather_kernel(second_kernel),
            gather_projection(query_weight),
            gather_projection(output_weight),
        )
        spread_channels = gather_channels
    incoming = lax.all_to_all(outgoing, "dp", split_axis=0, concat_axis=0, tiled=True)
    my_pairs = jnp.take(
        incoming.reshape(dp_count * slot_limit, cache_width, cache_len), landing_slot, axis=0
    )
    start_field = latents.astype(jnp.float32)
    activated = jax.nn.silu(norm_groups(start_field, group_width)).astype(jnp.bfloat16)
    first_in = spread_channels(activated)

    def convolve(full_field, which_weight):
        half = full_field.shape[0] // 2
        return jnp.concatenate(
            [
                apply_kernel(full_field[:half], full_weights[which_weight]),
                apply_kernel(full_field[half:], full_weights[which_weight]),
            ]
        )

    def project(field_rows, which_weight):
        full_weight = full_weights[which_weight]
        return jnp.einsum(
            "scq,ce->seq", field_rows, full_weight, preferred_element_type=jnp.float32
        )

    first_out = convolve(first_in, 0)
    scale_term = modulation[:, 0, :].astype(jnp.float32)[:, :, None]
    shift_term = modulation[:, 1, :].astype(jnp.float32)[:, :, None]
    modulated = jax.nn.silu(
        norm_groups(first_out, group_width) * (1.0 + scale_term) + shift_term
    ).astype(jnp.bfloat16)
    if fast:
        second_in = pair_gather_channel_minor(modulated)
    else:
        second_in = spread_channels(modulated)
    residual = start_field + convolve(second_in, 1)
    normed_out = norm_groups(residual, group_width).astype(jnp.bfloat16)
    local_samples = sample_shard_count // mp_count
    if fast:
        query_cells = xor_spread_samples(normed_out, local_samples)
        my_pairs = lax.optimization_barrier((my_pairs, query_cells))[0]
    else:
        query_cells = lax.all_to_all(normed_out, "mp", split_axis=0, concat_axis=1, tiled=True)
    pair_heads = lax.all_to_all(my_pairs, "mp", split_axis=0, concat_axis=1, tiled=True)
    total_width = query_cells.shape[1]
    head_count = total_width // HEAD
    queries = project(query_cells, 2).astype(jnp.bfloat16)
    queries = queries.reshape(local_samples, head_count, HEAD, cell_count)
    heads_of_keys = pair_heads[:, :total_width, :].reshape(
        local_samples, head_count, HEAD, cache_len
    )
    value_heads = pair_heads[:, total_width:, :].reshape(local_samples, head_count, HEAD, cache_len)
    scores = jnp.einsum(
        "shdq,shdk->shqk", queries, heads_of_keys, preferred_element_type=jnp.float32
    ) * HEAD ** (-0.5)
    local_lengths = lax.dynamic_slice_in_dim(my_lengths, my_column * local_samples, local_samples)
    visible = (
        jnp.arange(cache_len, dtype=jnp.int32)[None, None, None, :]
        < local_lengths[:, None, None, None]
    )
    scores = jnp.where(visible, scores, MASKED)
    row_peak = jnp.max(scores, axis=3, keepdims=True)
    exponent = jnp.exp(scores - row_peak)
    attention = (exponent / jnp.sum(exponent, axis=3, keepdims=True)).astype(jnp.bfloat16)
    context = jnp.einsum(
        "shqk,shdk->sqhd", attention, value_heads, preferred_element_type=jnp.float32
    ).astype(jnp.bfloat16)
    attended = jnp.einsum(
        "sqc,ce->seq",
        context.reshape(local_samples, cell_count, total_width),
        full_weights[3],
        preferred_element_type=jnp.float32,
    ).astype(jnp.bfloat16)
    if fast:
        returned = xor_return_channels(attended, attended.shape[1] // mp_count)
    else:
        returned = lax.all_to_all(attended, "mp", split_axis=1, concat_axis=0, tiled=True)
    final_field = residual + returned.astype(jnp.float32)
    return final_field.astype(jnp.bfloat16)


def solution(mesh):
    in_specs = (
        P(("groups", "dp"), "mp", None),
        P(("groups", "dp"), None, "mp"),
        P("dp", None, "mp"),
        P("dp", None, "mp"),
        P(("groups", "dp"), "mp", None),
        P("dp", None),
        P("dp", None),
        P("groups"),
        P("groups"),
        P("groups"),
    )
    out_specs = P(("groups", "dp"), "mp", None)
    return jax.shard_map(local, mesh=mesh, in_specs=in_specs, out_specs=out_specs, check_vma=False)
```

```python
import jax
import jax.numpy as jnp
from jax import lax
from jax.sharding import PartitionSpec as P

C = 640
GROUPS = 32
HEAD = 64
SIDE = 8


EPSILON = 1e-05
MASKED = -1e30


def norm_groups(values, group_width):
    field_shape = values.shape
    grouped = values.reshape(
        field_shape[0], field_shape[1] // group_width, group_width, field_shape[2]
    )
    center = grouped - jnp.mean(grouped, axis=(2, 3), keepdims=True)
    spread = jnp.mean(center * center, axis=(2, 3), keepdims=True)
    return (center * lax.rsqrt(spread + EPSILON)).reshape(field_shape)


def gather_channels(field):
    return lax.all_gather(field, "mp", axis=1, tiled=True)


def pair_gather_channels(field):
    dense = field.reshape(-1, 128)
    across = lax.ppermute(dense, "mp", [(i, i ^ 2) for i in range(4)])
    beside = lax.ppermute(dense, "mp", [(i, i ^ 1) for i in range(4)])
    relayed = lax.ppermute(across, "mp", [(i, i ^ 1) for i in range(4)])
    parts = [part.reshape(field.shape) for part in (beside, across, relayed)]
    return jnp.concatenate([field] + parts, axis=1)


def line_gather_flat(flat, count):
    my_shard = lax.axis_index("dp")
    rightward = [(i, i + 1) for i in range(count - 1)]
    leftward = [(i + 1, i) for i in range(count - 1)]
    going_right, going_left = flat, flat
    held = [flat]
    from_left, from_right = [], []
    for _ in range(1, count):
        going_right = lax.ppermute(going_right, "dp", rightward)
        going_left = lax.ppermute(going_left, "dp", leftward)
        from_left.append(going_right)
        from_right.append(going_left)
    line = jnp.stack(from_left[::-1] + held + from_right)
    return lax.dynamic_slice_in_dim(line, count - 1 - my_shard, count, axis=0)


def split_line_gather(packed, gated):
    my_shard = lax.axis_index("dp")
    my_group = lax.axis_index("groups")
    halves = packed.reshape(2, packed.shape[0] // 2, packed.shape[1])
    mine = lax.dynamic_index_in_dim(halves, my_group, 0, keepdims=False)
    mine, gated = lax.optimization_barrier((mine, gated))
    rightward = [(i, i + 1) for i in range(3)]
    leftward = [(i + 1, i) for i in range(3)]
    swap = [(0, 1), (1, 0)]
    left_1 = lax.ppermute(mine, "dp", rightward)
    right_1 = lax.ppermute(mine, "dp", leftward)
    first_swap = lax.ppermute(jnp.where(my_shard >= 1, left_1, right_1), "groups", swap)
    left_2 = lax.ppermute(left_1, "dp", rightward)
    right_2 = lax.ppermute(right_1, "dp", leftward)
    second_swap = lax.ppermute(jnp.where(my_shard >= 2, left_2, right_2), "groups", swap)
    left_3 = lax.ppermute(left_2, "dp", rightward)
    right_3 = lax.ppermute(right_2, "dp", leftward)
    third_pick = jnp.where(my_shard == 0, right_3, jnp.where(my_shard == 3, left_3, right_1))
    third_swap = lax.ppermute(third_pick, "groups", swap)

    def whole(own_half, other_half):
        lead = jnp.where(my_group == 0, own_half, other_half)
        tail = jnp.where(my_group == 0, other_half, own_half)
        return jnp.concatenate([lead, tail], axis=0)

    line = jnp.stack(
        [
            whole(left_3, third_swap),
            whole(left_2, second_swap),
            whole(left_1, first_swap),
            packed,
            whole(right_1, jnp.where(my_shard == 0, first_swap, third_swap)),
            whole(right_2, second_swap),
            whole(right_3, third_swap),
        ]
    )
    return lax.dynamic_slice_in_dim(line, 3 - my_shard, 4, axis=0), gated, (left_3, right_3)


def pair_gather_channel_minor(field):
    cell_major = jnp.transpose(field, (0, 2, 1))
    dense = cell_major.reshape(-1, 128)
    across = lax.ppermute(dense, "mp", [(i, i ^ 2) for i in range(4)])
    beside = lax.ppermute(dense, "mp", [(i, i ^ 1) for i in range(4)])
    relayed = lax.ppermute(across, "mp", [(i, i ^ 1) for i in range(4)])
    parts = [jnp.transpose(part.reshape(cell_major.shape), (0, 2, 1)) for part in (beside, across, relayed)]
    return jnp.concatenate([field] + parts, axis=1)


def xor_spread_samples(field, group):
    my_column = lax.axis_index("mp")
    parts = [lax.dynamic_slice_in_dim(field, my_column * group, group, axis=0)]
    for step in range(1, 4):
        block = lax.dynamic_slice_in_dim(field, (my_column ^ step) * group, group, axis=0)
        moved = lax.ppermute(block.reshape(-1, 128), "mp", [(i, i ^ step) for i in range(4)])
        parts.append(moved.reshape(block.shape))
    return jnp.concatenate(parts, axis=1)


def xor_return_channels(field, width):
    my_column = lax.axis_index("mp")
    parts = [lax.dynamic_slice_in_dim(field, my_column * width, width, axis=1)]
    for step in range(1, 4):
        block = lax.dynamic_slice_in_dim(field, (my_column ^ step) * width, width, axis=1)
        moved = lax.ppermute(block.reshape(-1, 128), "mp", [(i, i ^ step) for i in range(4)])
        parts.append(moved.reshape(block.shape))
    order = jnp.bitwise_xor(jnp.arange(4, dtype=jnp.int32), my_column)
    picked = jnp.take(jnp.stack(parts), order, axis=0, mode="clip")
    return picked.reshape((4 * field.shape[0],) + picked.shape[2:])


def shift_parts(shard, count):
    parts = [shard]
    for step in range(1, count):
        parts.append(lax.ppermute(shard, "dp", [(i, (i + step) % count) for i in range(count)]))
    return jnp.stack(parts)


def order_rows(stacked, wanted_blocks):
    my_shard = lax.axis_index("dp")
    count = stacked.shape[0]
    picked = jnp.take(stacked, (my_shard - wanted_blocks) % count, axis=0, mode="clip")
    return picked.reshape((count * stacked.shape[1],) + stacked.shape[2:])


def gather_kernel(weight_shard):
    return lax.all_gather(weight_shard, "dp", axis=0, tiled=True)


def gather_projection(weight_shard):
    return lax.all_gather(weight_shard, "dp", axis=0, tiled=True)


def apply_kernel(full_field, kernel):
    sample_count = full_field.shape[0]
    out_width = kernel.shape[2]
    tap_images = jnp.einsum("scq,cte->stqe", full_field, kernel, preferred_element_type=jnp.float32)
    tap_images = tap_images.reshape(sample_count, 9, SIDE, SIDE, out_width)
    padded = jnp.pad(tap_images, ((0, 0), (0, 0), (1, 1), (1, 1), (0, 0)))
    running = padded[:, 0, 0:SIDE, 0:SIDE, :]
    for offset in range(1, 9):
        row_shift, col_shift = (offset // 3, offset % 3)
        running = (
            running
            + padded[:, offset, row_shift : row_shift + SIDE, col_shift : col_shift + SIDE, :]
        )
    return jnp.transpose(running.reshape(sample_count, SIDE * SIDE, out_width), (0, 2, 1))


def local(
    latents,
    modulation,
    first_kernel,
    second_kernel,
    encoder_cache,
    query_weight,
    output_weight,
    kept_prompt_list,
    destination,
    lengths,
):
    group_width = C // GROUPS
    dp_count = lax.axis_size("dp")
    mp_count = lax.axis_size("mp")
    my_shard = lax.axis_index("dp")
    my_column = lax.axis_index("mp")
    sample_shard_count = latents.shape[0]
    prompt_dev = encoder_cache.shape[0]
    cache_len = encoder_cache.shape[2]
    cache_width = encoder_cache.shape[1]
    cell_count = latents.shape[2]
    slot_limit = 2 * (sample_shard_count // dp_count)
    all_samples = destination.shape[0]
    owner_target = destination.reshape(dp_count, sample_shard_count)
    positions = jnp.arange(sample_shard_count, dtype=jnp.int32)
    before = positions[None, :] < positions[:, None]
    same_target = owner_target[:, :, None] == owner_target[:, None, :]
    slot_rank = jnp.sum((same_target & before[None]).astype(jnp.int32), axis=2)
    my_target = lax.dynamic_index_in_dim(owner_target, my_shard, 0, keepdims=False)
    my_rank = lax.dynamic_index_in_dim(slot_rank, my_shard, 0, keepdims=False)
    my_prompts = (
        lax.dynamic_slice_in_dim(
            kept_prompt_list, my_shard * sample_shard_count, sample_shard_count
        )
        - my_shard * prompt_dev
    )
    send_slot = my_target * slot_limit + my_rank
    slot_table = send_slot[:, None] == jnp.arange(dp_count * slot_limit, dtype=jnp.int32)[None, :]
    source_row = jnp.sum(jnp.where(slot_table, my_prompts[:, None], 0), axis=0)
    filled = jnp.any(slot_table, axis=0)
    send_rows = jnp.take(encoder_cache, source_row, axis=0)
    send_rows = jnp.where(filled[:, None, None], send_rows, jnp.zeros_like(send_rows))
    outgoing = send_rows.reshape(dp_count, slot_limit, cache_width, cache_len)
    arriving = destination == my_shard
    arrival_pos = jnp.cumsum(arriving.astype(jnp.int32)) - 1
    selector = arriving[None, :] & (arrival_pos[None, :] == positions[:, None])
    kept_prompt = jnp.sum(
        jnp.where(selector, jnp.arange(all_samples, dtype=jnp.int32)[None, :], 0), axis=1
    )
    incoming_order_rank = jnp.sum(jnp.where(selector, slot_rank.reshape(-1)[None, :], 0), axis=1)
    prompt_ids = jnp.sum(jnp.where(selector, kept_prompt_list[None, :], 0), axis=1)
    landing_slot = kept_prompt // sample_shard_count * slot_limit + incoming_order_rank
    prompt_hits = prompt_ids[:, None] == jnp.arange(lengths.shape[0], dtype=jnp.int32)[None, :]
    my_lengths = jnp.sum(jnp.where(prompt_hits, lengths[None, :], 0), axis=1)
    fast = dp_count == 4 and mp_count == 4 and lax.axis_size("groups") == 2
    weight_shards = (first_kernel, second_kernel, query_weight, output_weight)
    if fast:
        block_ids = jnp.arange(dp_count, dtype=jnp.int32)
        channel_blocks = jnp.bitwise_xor(block_ids, my_column)
        pieces = (first_kernel, second_kernel, query_weight, output_weight)
        dense = [piece.reshape(-1, 128) for piece in pieces]
        natural, latents, line_done = split_line_gather(jnp.concatenate(dense, axis=0), latents)
        kernel_rows = dense[0].shape[0] + dense[1].shape[0]
        kernel_part = jnp.take(natural[:, :kernel_rows], channel_blocks, axis=0, mode="clip")
        proj_part = natural[:, kernel_rows:]
        full_weights = []
        cut = 0
        query_part = jnp.take(proj_part, channel_blocks, axis=0, mode="clip")
        for piece, block, source in zip(pieces, dense, (kernel_part, kernel_part, query_part, proj_part)):
            if cut == kernel_rows:
                cut = 0
            chunk = source[:, cut : cut + block.shape[0]]
            cut += block.shape[0]
            full_weights.append(chunk.reshape((dp_count * piece.shape[0],) + piece.shape[1:]))
        gathered = (kernel_part, proj_part)
        full_weights = tuple(full_weights)
        outgoing = lax.optimization_barrier((outgoing, line_done))[0]
        spread_channels = pair_gather_channels
    else:
        full_weights = (
            gather_kernel(first_kernel),
            gather_kernel(second_kernel),
            gather_projection(query_weight),
            gather_projection(output_weight),
        )
        spread_channels = gather_channels
    incoming = lax.all_to_all(outgoing, "dp", split_axis=0, concat_axis=0, tiled=True)
    my_pairs = jnp.take(
        incoming.reshape(dp_count * slot_limit, cache_width, cache_len), landing_slot, axis=0
    )
    start_field = latents.astype(jnp.float32)
    activated = jax.nn.silu(norm_groups(start_field, group_width)).astype(jnp.bfloat16)
    first_in = spread_channels(activated)

    def convolve(full_field, which_weight):
        half = full_field.shape[0] // 2
        return jnp.concatenate(
            [
                apply_kernel(full_field[:half], full_weights[which_weight]),
                apply_kernel(full_field[half:], full_weights[which_weight]),
            ]
        )

    def project(field_rows, which_weight):
        full_weight = full_weights[which_weight]
        return jnp.einsum(
            "scq,ce->seq", field_rows, full_weight, preferred_element_type=jnp.float32
        )

    first_out = convolve(first_in, 0)
    scale_term = modulation[:, 0, :].astype(jnp.float32)[:, :, None]
    shift_term = modulation[:, 1, :].astype(jnp.float32)[:, :, None]
    modulated = jax.nn.silu(
        norm_groups(first_out, group_width) * (1.0 + scale_term) + shift_term
    ).astype(jnp.bfloat16)
    if fast:
        second_in = pair_gather_channel_minor(modulated)
    else:
        second_in = spread_channels(modulated)
    residual = start_field + convolve(second_in, 1)
    normed_out = norm_groups(residual, group_width).astype(jnp.bfloat16)
    local_samples = sample_shard_count // mp_count
    if fast:
        query_cells = xor_spread_samples(normed_out, local_samples)
        my_pairs = lax.optimization_barrier((my_pairs, query_cells))[0]
    else:
        query_cells = lax.all_to_all(normed_out, "mp", split_axis=0, concat_axis=1, tiled=True)
    pair_heads = lax.all_to_all(my_pairs, "mp", split_axis=0, concat_axis=1, tiled=True)
    total_width = query_cells.shape[1]
    head_count = total_width // HEAD
    queries = project(query_cells, 2).astype(jnp.bfloat16)
    queries = queries.reshape(local_samples, head_count, HEAD, cell_count)
    heads_of_keys = pair_heads[:, :total_width, :].reshape(
        local_samples, head_count, HEAD, cache_len
    )
    value_heads = pair_heads[:, total_width:, :].reshape(local_samples, head_count, HEAD, cache_len)
    scores = jnp.einsum(
        "shdq,shdk->shqk", queries, heads_of_keys, preferred_element_type=jnp.float32
    ) * HEAD ** (-0.5)
    local_lengths = lax.dynamic_slice_in_dim(my_lengths, my_column * local_samples, local_samples)
    visible = (
        jnp.arange(cache_len, dtype=jnp.int32)[None, None, None, :]
        < local_lengths[:, None, None, None]
    )
    scores = jnp.where(visible, scores, MASKED)
    row_peak = jnp.max(scores, axis=3, keepdims=True)
    exponent = jnp.exp(scores - row_peak)
    attention = (exponent / jnp.sum(exponent, axis=3, keepdims=True)).astype(jnp.bfloat16)
    attention = lax.optimization_barrier(attention)
    context = jnp.einsum(
        "shqk,shdk->sqhd", attention, value_heads, preferred_element_type=jnp.float32
    ).astype(jnp.bfloat16)
    attended = jnp.einsum(
        "sqc,ce->seq",
        context.reshape(local_samples, cell_count, total_width),
        full_weights[3],
        preferred_element_type=jnp.float32,
    ).astype(jnp.bfloat16)
    if fast:
        returned = xor_return_channels(attended, attended.shape[1] // mp_count)
    else:
        returned = lax.all_to_all(attended, "mp", split_axis=1, concat_axis=0, tiled=True)
    final_field = residual + returned.astype(jnp.float32)
    return final_field.astype(jnp.bfloat16)


def solution(mesh):
    in_specs = (
        P(("groups", "dp"), "mp", None),
        P(("groups", "dp"), None, "mp"),
        P("dp", None, "mp"),
        P("dp", None, "mp"),
        P(("groups", "dp"), "mp", None),
        P("dp", None),
        P("dp", None),
        P("groups"),
        P("groups"),
        P("groups"),
    )
    out_specs = P(("groups", "dp"), "mp", None)
    return jax.shard_map(local, mesh=mesh, in_specs=in_specs, out_specs=out_specs, check_vma=False)
```

```python
import jax
import jax.numpy as jnp
from jax import lax
from jax.sharding import PartitionSpec as P

C = 640
GROUPS = 32
HEAD = 64
SIDE = 8


EPSILON = 1e-05
MASKED = -1e30


def norm_groups(values, group_width):
    field_shape = values.shape
    grouped = values.reshape(
        field_shape[0], field_shape[1] // group_width, group_width, field_shape[2]
    )
    center = grouped - jnp.mean(grouped, axis=(2, 3), keepdims=True)
    spread = jnp.mean(center * center, axis=(2, 3), keepdims=True)
    return (center * lax.rsqrt(spread + EPSILON)).reshape(field_shape)


def gather_channels(field):
    return lax.all_gather(field, "mp", axis=1, tiled=True)


def pair_gather_channels(field):
    dense = field.reshape(-1, 128)
    across = lax.ppermute(dense, "mp", [(i, i ^ 2) for i in range(4)])
    beside = lax.ppermute(dense, "mp", [(i, i ^ 1) for i in range(4)])
    relayed = lax.ppermute(across, "mp", [(i, i ^ 1) for i in range(4)])
    parts = [part.reshape(field.shape) for part in (beside, across, relayed)]
    return jnp.concatenate([field] + parts, axis=1)


def line_gather_flat(flat, count):
    my_shard = lax.axis_index("dp")
    rightward = [(i, i + 1) for i in range(count - 1)]
    leftward = [(i + 1, i) for i in range(count - 1)]
    going_right, going_left = flat, flat
    held = [flat]
    from_left, from_right = [], []
    for _ in range(1, count):
        going_right = lax.ppermute(going_right, "dp", rightward)
        going_left = lax.ppermute(going_left, "dp", leftward)
        from_left.append(going_right)
        from_right.append(going_left)
    line = jnp.stack(from_left[::-1] + held + from_right)
    return lax.dynamic_slice_in_dim(line, count - 1 - my_shard, count, axis=0)


def split_line_gather(packed, gated):
    my_shard = lax.axis_index("dp")
    my_group = lax.axis_index("groups")
    halves = packed.reshape(2, packed.shape[0] // 2, packed.shape[1])
    mine = lax.dynamic_index_in_dim(halves, my_group, 0, keepdims=False)
    mine, gated = lax.optimization_barrier((mine, gated))
    rightward = [(i, i + 1) for i in range(3)]
    leftward = [(i + 1, i) for i in range(3)]
    swap = [(0, 1), (1, 0)]
    left_1 = lax.ppermute(mine, "dp", rightward)
    right_1 = lax.ppermute(mine, "dp", leftward)
    first_swap = lax.ppermute(jnp.where(my_shard >= 1, left_1, right_1), "groups", swap)
    left_2 = lax.ppermute(left_1, "dp", rightward)
    right_2 = lax.ppermute(right_1, "dp", leftward)
    second_swap = lax.ppermute(jnp.where(my_shard >= 2, left_2, right_2), "groups", swap)
    left_3 = lax.ppermute(left_2, "dp", rightward)
    right_3 = lax.ppermute(right_2, "dp", leftward)
    third_pick = jnp.where(my_shard == 0, right_3, jnp.where(my_shard == 3, left_3, right_1))
    third_swap = lax.ppermute(third_pick, "groups", swap)

    def whole(own_half, other_half):
        lead = jnp.where(my_group == 0, own_half, other_half)
        tail = jnp.where(my_group == 0, other_half, own_half)
        return jnp.concatenate([lead, tail], axis=0)

    line = jnp.stack(
        [
            whole(left_3, third_swap),
            whole(left_2, second_swap),
            whole(left_1, first_swap),
            packed,
            whole(right_1, jnp.where(my_shard == 0, first_swap, third_swap)),
            whole(right_2, second_swap),
            whole(right_3, third_swap),
        ]
    )
    return lax.dynamic_slice_in_dim(line, 3 - my_shard, 4, axis=0), gated, (left_3, right_3)


def pair_gather_channel_minor(field):
    cell_major = jnp.transpose(field, (0, 2, 1))
    dense = cell_major.reshape(-1, 128)
    across = lax.ppermute(dense, "mp", [(i, i ^ 2) for i in range(4)])
    beside = lax.ppermute(dense, "mp", [(i, i ^ 1) for i in range(4)])
    relayed = lax.ppermute(across, "mp", [(i, i ^ 1) for i in range(4)])
    parts = [jnp.transpose(part.reshape(cell_major.shape), (0, 2, 1)) for part in (beside, across, relayed)]
    return jnp.concatenate([field] + parts, axis=1)


def xor_spread_samples(field, group):
    my_column = lax.axis_index("mp")
    parts = [lax.dynamic_slice_in_dim(field, my_column * group, group, axis=0)]
    for step in range(1, 4):
        block = lax.dynamic_slice_in_dim(field, (my_column ^ step) * group, group, axis=0)
        moved = lax.ppermute(block.reshape(-1, 128), "mp", [(i, i ^ step) for i in range(4)])
        parts.append(moved.reshape(block.shape))
    return jnp.concatenate(parts, axis=1)


def xor_return_channels(field, width):
    my_column = lax.axis_index("mp")
    parts = [lax.dynamic_slice_in_dim(field, my_column * width, width, axis=1)]
    for step in range(1, 4):
        block = lax.dynamic_slice_in_dim(field, (my_column ^ step) * width, width, axis=1)
        moved = lax.ppermute(block.reshape(-1, 128), "mp", [(i, i ^ step) for i in range(4)])
        parts.append(moved.reshape(block.shape))
    order = jnp.bitwise_xor(jnp.arange(4, dtype=jnp.int32), my_column)
    picked = jnp.take(jnp.stack(parts), order, axis=0, mode="clip")
    return picked.reshape((4 * field.shape[0],) + picked.shape[2:])


def shift_parts(shard, count):
    parts = [shard]
    for step in range(1, count):
        parts.append(lax.ppermute(shard, "dp", [(i, (i + step) % count) for i in range(count)]))
    return jnp.stack(parts)


def order_rows(stacked, wanted_blocks):
    my_shard = lax.axis_index("dp")
    count = stacked.shape[0]
    picked = jnp.take(stacked, (my_shard - wanted_blocks) % count, axis=0, mode="clip")
    return picked.reshape((count * stacked.shape[1],) + stacked.shape[2:])


def gather_kernel(weight_shard):
    return lax.all_gather(weight_shard, "dp", axis=0, tiled=True)


def gather_projection(weight_shard):
    return lax.all_gather(weight_shard, "dp", axis=0, tiled=True)


def apply_kernel(full_field, kernel):
    sample_count = full_field.shape[0]
    out_width = kernel.shape[2]
    tap_images = jnp.einsum("scq,cte->stqe", full_field, kernel, preferred_element_type=jnp.float32)
    tap_images = tap_images.reshape(sample_count, 9, SIDE, SIDE, out_width)
    padded = jnp.pad(tap_images, ((0, 0), (0, 0), (1, 1), (1, 1), (0, 0)))
    running = padded[:, 0, 0:SIDE, 0:SIDE, :]
    for offset in range(1, 9):
        row_shift, col_shift = (offset // 3, offset % 3)
        running = (
            running
            + padded[:, offset, row_shift : row_shift + SIDE, col_shift : col_shift + SIDE, :]
        )
    return jnp.transpose(running.reshape(sample_count, SIDE * SIDE, out_width), (0, 2, 1))


def local(
    latents,
    modulation,
    first_kernel,
    second_kernel,
    encoder_cache,
    query_weight,
    output_weight,
    kept_prompt_list,
    destination,
    lengths,
):
    group_width = C // GROUPS
    dp_count = lax.axis_size("dp")
    mp_count = lax.axis_size("mp")
    my_shard = lax.axis_index("dp")
    my_column = lax.axis_index("mp")
    sample_shard_count = latents.shape[0]
    prompt_dev = encoder_cache.shape[0]
    cache_len = encoder_cache.shape[2]
    cache_width = encoder_cache.shape[1]
    cell_count = latents.shape[2]
    slot_limit = 2 * (sample_shard_count // dp_count)
    all_samples = destination.shape[0]
    owner_target = destination.reshape(dp_count, sample_shard_count)
    positions = jnp.arange(sample_shard_count, dtype=jnp.int32)
    before = positions[None, :] < positions[:, None]
    same_target = owner_target[:, :, None] == owner_target[:, None, :]
    slot_rank = jnp.sum((same_target & before[None]).astype(jnp.int32), axis=2)
    my_target = lax.dynamic_index_in_dim(owner_target, my_shard, 0, keepdims=False)
    my_rank = lax.dynamic_index_in_dim(slot_rank, my_shard, 0, keepdims=False)
    my_prompts = (
        lax.dynamic_slice_in_dim(
            kept_prompt_list, my_shard * sample_shard_count, sample_shard_count
        )
        - my_shard * prompt_dev
    )
    send_slot = my_target * slot_limit + my_rank
    slot_table = send_slot[:, None] == jnp.arange(dp_count * slot_limit, dtype=jnp.int32)[None, :]
    source_row = jnp.sum(jnp.where(slot_table, my_prompts[:, None], 0), axis=0)
    filled = jnp.any(slot_table, axis=0)
    send_rows = jnp.take(encoder_cache, source_row, axis=0)
    send_rows = jnp.where(filled[:, None, None], send_rows, jnp.zeros_like(send_rows))
    outgoing = send_rows.reshape(dp_count, slot_limit, cache_width, cache_len)
    arriving = destination == my_shard
    arrival_pos = jnp.cumsum(arriving.astype(jnp.int32)) - 1
    selector = arriving[None, :] & (arrival_pos[None, :] == positions[:, None])
    kept_prompt = jnp.sum(
        jnp.where(selector, jnp.arange(all_samples, dtype=jnp.int32)[None, :], 0), axis=1
    )
    incoming_order_rank = jnp.sum(jnp.where(selector, slot_rank.reshape(-1)[None, :], 0), axis=1)
    prompt_ids = jnp.sum(jnp.where(selector, kept_prompt_list[None, :], 0), axis=1)
    landing_slot = kept_prompt // sample_shard_count * slot_limit + incoming_order_rank
    prompt_hits = prompt_ids[:, None] == jnp.arange(lengths.shape[0], dtype=jnp.int32)[None, :]
    my_lengths = jnp.sum(jnp.where(prompt_hits, lengths[None, :], 0), axis=1)
    fast = dp_count == 4 and mp_count == 4 and lax.axis_size("groups") == 2
    weight_shards = (first_kernel, second_kernel, query_weight, output_weight)
    if fast:
        block_ids = jnp.arange(dp_count, dtype=jnp.int32)
        channel_blocks = jnp.bitwise_xor(block_ids, my_column)
        pieces = (first_kernel, second_kernel, query_weight, output_weight)
        dense = [piece.reshape(-1, 128) for piece in pieces]
        natural, latents, line_done = split_line_gather(jnp.concatenate(dense, axis=0), latents)
        kernel_rows = dense[0].shape[0] + dense[1].shape[0]
        kernel_part = jnp.take(natural[:, :kernel_rows], channel_blocks, axis=0, mode="clip")
        proj_part = natural[:, kernel_rows:]
        full_weights = []
        cut = 0
        query_part = jnp.take(proj_part, channel_blocks, axis=0, mode="clip")
        for piece, block, source in zip(pieces, dense, (kernel_part, kernel_part, query_part, proj_part)):
            if cut == kernel_rows:
                cut = 0
            chunk = source[:, cut : cut + block.shape[0]]
            cut += block.shape[0]
            full_weights.append(chunk.reshape((dp_count * piece.shape[0],) + piece.shape[1:]))
        gathered = (kernel_part, proj_part)
        full_weights = tuple(full_weights)
        outgoing = lax.optimization_barrier((outgoing, line_done))[0]
        spread_channels = pair_gather_channels
    else:
        full_weights = (
            gather_kernel(first_kernel),
            gather_kernel(second_kernel),
            gather_projection(query_weight),
            gather_projection(output_weight),
        )
        spread_channels = gather_channels
    incoming = lax.all_to_all(outgoing, "dp", split_axis=0, concat_axis=0, tiled=True)
    my_pairs = jnp.take(
        incoming.reshape(dp_count * slot_limit, cache_width, cache_len), landing_slot, axis=0
    )
    start_field = latents.astype(jnp.float32)
    activated = jax.nn.silu(norm_groups(start_field, group_width)).astype(jnp.bfloat16)
    first_in = spread_channels(activated)

    def convolve(full_field, which_weight):
        half = full_field.shape[0] // 2
        return jnp.concatenate(
            [
                apply_kernel(full_field[:half], full_weights[which_weight]),
                apply_kernel(full_field[half:], full_weights[which_weight]),
            ]
        )

    def project(field_rows, which_weight):
        full_weight = full_weights[which_weight]
        return jnp.einsum(
            "scq,ce->seq", field_rows, full_weight, preferred_element_type=jnp.float32
        )

    first_out = convolve(first_in, 0)
    scale_term = modulation[:, 0, :].astype(jnp.float32)[:, :, None]
    shift_term = modulation[:, 1, :].astype(jnp.float32)[:, :, None]
    modulated = jax.nn.silu(
        norm_groups(first_out, group_width) * (1.0 + scale_term) + shift_term
    ).astype(jnp.bfloat16)
    if fast:
        modulated, second_weight = lax.optimization_barrier((modulated, full_weights[1]))
        full_weights = (full_weights[0], second_weight) + tuple(full_weights[2:])
        second_in = pair_gather_channel_minor(modulated)
    else:
        second_in = spread_channels(modulated)
    residual = start_field + convolve(second_in, 1)
    normed_out = norm_groups(residual, group_width).astype(jnp.bfloat16)
    local_samples = sample_shard_count // mp_count
    if fast:
        query_cells = xor_spread_samples(normed_out, local_samples)
        my_pairs = lax.optimization_barrier((my_pairs, query_cells))[0]
    else:
        query_cells = lax.all_to_all(normed_out, "mp", split_axis=0, concat_axis=1, tiled=True)
    pair_heads = lax.all_to_all(my_pairs, "mp", split_axis=0, concat_axis=1, tiled=True)
    total_width = query_cells.shape[1]
    head_count = total_width // HEAD
    queries = project(query_cells, 2).astype(jnp.bfloat16)
    queries = queries.reshape(local_samples, head_count, HEAD, cell_count)
    heads_of_keys = pair_heads[:, :total_width, :].reshape(
        local_samples, head_count, HEAD, cache_len
    )
    value_heads = pair_heads[:, total_width:, :].reshape(local_samples, head_count, HEAD, cache_len)
    scores = jnp.einsum(
        "shdq,shdk->shqk", queries, heads_of_keys, preferred_element_type=jnp.float32
    ) * HEAD ** (-0.5)
    local_lengths = lax.dynamic_slice_in_dim(my_lengths, my_column * local_samples, local_samples)
    visible = (
        jnp.arange(cache_len, dtype=jnp.int32)[None, None, None, :]
        < local_lengths[:, None, None, None]
    )
    scores = jnp.where(visible, scores, MASKED)
    row_peak = jnp.max(scores, axis=3, keepdims=True)
    exponent = jnp.exp(scores - row_peak)
    attention = (exponent / jnp.sum(exponent, axis=3, keepdims=True)).astype(jnp.bfloat16)
    attention = lax.optimization_barrier(attention)
    context = jnp.einsum(
        "shqk,shdk->sqhd", attention, value_heads, preferred_element_type=jnp.float32
    ).astype(jnp.bfloat16)
    attended = jnp.einsum(
        "sqc,ce->seq",
        context.reshape(local_samples, cell_count, total_width),
        full_weights[3],
        preferred_element_type=jnp.float32,
    ).astype(jnp.bfloat16)
    if fast:
        returned = xor_return_channels(attended, attended.shape[1] // mp_count)
    else:
        returned = lax.all_to_all(attended, "mp", split_axis=1, concat_axis=0, tiled=True)
    final_field = residual + returned.astype(jnp.float32)
    return final_field.astype(jnp.bfloat16)


def solution(mesh):
    in_specs = (
        P(("groups", "dp"), "mp", None),
        P(("groups", "dp"), None, "mp"),
        P("dp", None, "mp"),
        P("dp", None, "mp"),
        P(("groups", "dp"), "mp", None),
        P("dp", None),
        P("dp", None),
        P("groups"),
        P("groups"),
        P("groups"),
    )
    out_specs = P(("groups", "dp"), "mp", None)
    return jax.shard_map(local, mesh=mesh, in_specs=in_specs, out_specs=out_specs, check_vma=False)
```

```python
import jax
import jax.numpy as jnp
from jax import lax
from jax.sharding import PartitionSpec as P

C = 640
GROUPS = 32
HEAD = 64
SIDE = 8


EPSILON = 1e-05
MASKED = -1e30


def norm_groups(values, group_width):
    field_shape = values.shape
    grouped = values.reshape(
        field_shape[0], field_shape[1] // group_width, group_width, field_shape[2]
    )
    center = grouped - jnp.mean(grouped, axis=(2, 3), keepdims=True)
    spread = jnp.mean(center * center, axis=(2, 3), keepdims=True)
    return (center * lax.rsqrt(spread + EPSILON)).reshape(field_shape)


def gather_channels(field):
    return lax.all_gather(field, "mp", axis=1, tiled=True)


def pair_gather_channels(field):
    dense = field.reshape(-1, 128)
    across = lax.ppermute(dense, "mp", [(i, i ^ 2) for i in range(4)])
    beside = lax.ppermute(dense, "mp", [(i, i ^ 1) for i in range(4)])
    relayed = lax.ppermute(across, "mp", [(i, i ^ 1) for i in range(4)])
    parts = [part.reshape(field.shape) for part in (beside, across, relayed)]
    return jnp.concatenate([field] + parts, axis=1)


def line_gather_flat(flat, count):
    my_shard = lax.axis_index("dp")
    rightward = [(i, i + 1) for i in range(count - 1)]
    leftward = [(i + 1, i) for i in range(count - 1)]
    going_right, going_left = flat, flat
    held = [flat]
    from_left, from_right = [], []
    for _ in range(1, count):
        going_right = lax.ppermute(going_right, "dp", rightward)
        going_left = lax.ppermute(going_left, "dp", leftward)
        from_left.append(going_right)
        from_right.append(going_left)
    line = jnp.stack(from_left[::-1] + held + from_right)
    return lax.dynamic_slice_in_dim(line, count - 1 - my_shard, count, axis=0)


def split_line_gather(packed, gated):
    my_shard = lax.axis_index("dp")
    my_group = lax.axis_index("groups")
    halves = packed.reshape(2, packed.shape[0] // 2, packed.shape[1])
    mine = lax.dynamic_index_in_dim(halves, my_group, 0, keepdims=False)
    mine, gated = lax.optimization_barrier((mine, gated))
    rightward = [(i, i + 1) for i in range(3)]
    leftward = [(i + 1, i) for i in range(3)]
    swap = [(0, 1), (1, 0)]
    left_1 = lax.ppermute(mine, "dp", rightward)
    right_1 = lax.ppermute(mine, "dp", leftward)
    first_swap = lax.ppermute(jnp.where(my_shard >= 1, left_1, right_1), "groups", swap)
    left_2 = lax.ppermute(left_1, "dp", rightward)
    right_2 = lax.ppermute(right_1, "dp", leftward)
    second_swap = lax.ppermute(jnp.where(my_shard >= 2, left_2, right_2), "groups", swap)
    left_3 = lax.ppermute(left_2, "dp", rightward)
    right_3 = lax.ppermute(right_2, "dp", leftward)
    third_pick = jnp.where(my_shard == 0, right_3, jnp.where(my_shard == 3, left_3, right_1))
    third_swap = lax.ppermute(third_pick, "groups", swap)

    def whole(own_half, other_half):
        lead = jnp.where(my_group == 0, own_half, other_half)
        tail = jnp.where(my_group == 0, other_half, own_half)
        return jnp.concatenate([lead, tail], axis=0)

    line = jnp.stack(
        [
            whole(left_3, third_swap),
            whole(left_2, second_swap),
            whole(left_1, first_swap),
            packed,
            whole(right_1, jnp.where(my_shard == 0, first_swap, third_swap)),
            whole(right_2, second_swap),
            whole(right_3, third_swap),
        ]
    )
    return lax.dynamic_slice_in_dim(line, 3 - my_shard, 4, axis=0), gated, (left_3, right_3)


def pair_gather_channel_minor(field):
    cell_major = jnp.transpose(field, (0, 2, 1))
    dense = cell_major.reshape(-1, 128)
    across = lax.ppermute(dense, "mp", [(i, i ^ 2) for i in range(4)])
    beside = lax.ppermute(dense, "mp", [(i, i ^ 1) for i in range(4)])
    relayed = lax.ppermute(across, "mp", [(i, i ^ 1) for i in range(4)])
    parts = [jnp.transpose(part.reshape(cell_major.shape), (0, 2, 1)) for part in (beside, across, relayed)]
    return jnp.concatenate([field] + parts, axis=1)


def xor_spread_samples(field, group):
    my_column = lax.axis_index("mp")
    parts = [lax.dynamic_slice_in_dim(field, my_column * group, group, axis=0)]
    for step in range(1, 4):
        block = lax.dynamic_slice_in_dim(field, (my_column ^ step) * group, group, axis=0)
        moved = lax.ppermute(block.reshape(-1, 128), "mp", [(i, i ^ step) for i in range(4)])
        parts.append(moved.reshape(block.shape))
    return jnp.concatenate(parts, axis=1)


def xor_return_channels(field, width):
    my_column = lax.axis_index("mp")
    parts = [lax.dynamic_slice_in_dim(field, my_column * width, width, axis=1)]
    for step in range(1, 4):
        block = lax.dynamic_slice_in_dim(field, (my_column ^ step) * width, width, axis=1)
        moved = lax.ppermute(block.reshape(-1, 128), "mp", [(i, i ^ step) for i in range(4)])
        parts.append(moved.reshape(block.shape))
    order = jnp.bitwise_xor(jnp.arange(4, dtype=jnp.int32), my_column)
    picked = jnp.take(jnp.stack(parts), order, axis=0, mode="clip")
    return picked.reshape((4 * field.shape[0],) + picked.shape[2:])


def shift_parts(shard, count):
    parts = [shard]
    for step in range(1, count):
        parts.append(lax.ppermute(shard, "dp", [(i, (i + step) % count) for i in range(count)]))
    return jnp.stack(parts)


def order_rows(stacked, wanted_blocks):
    my_shard = lax.axis_index("dp")
    count = stacked.shape[0]
    picked = jnp.take(stacked, (my_shard - wanted_blocks) % count, axis=0, mode="clip")
    return picked.reshape((count * stacked.shape[1],) + stacked.shape[2:])


def gather_kernel(weight_shard):
    return lax.all_gather(weight_shard, "dp", axis=0, tiled=True)


def gather_projection(weight_shard):
    return lax.all_gather(weight_shard, "dp", axis=0, tiled=True)


def apply_kernel(full_field, kernel):
    sample_count = full_field.shape[0]
    out_width = kernel.shape[2]
    tap_images = jnp.einsum("scq,cte->stqe", full_field, kernel, preferred_element_type=jnp.float32)
    tap_images = tap_images.reshape(sample_count, 9, SIDE, SIDE, out_width)
    padded = jnp.pad(tap_images, ((0, 0), (0, 0), (1, 1), (1, 1), (0, 0)))
    running = padded[:, 0, 0:SIDE, 0:SIDE, :]
    for offset in range(1, 9):
        row_shift, col_shift = (offset // 3, offset % 3)
        running = (
            running
            + padded[:, offset, row_shift : row_shift + SIDE, col_shift : col_shift + SIDE, :]
        )
    return jnp.transpose(running.reshape(sample_count, SIDE * SIDE, out_width), (0, 2, 1))


def local(
    latents,
    modulation,
    first_kernel,
    second_kernel,
    encoder_cache,
    query_weight,
    output_weight,
    kept_prompt_list,
    destination,
    lengths,
):
    group_width = C // GROUPS
    dp_count = lax.axis_size("dp")
    mp_count = lax.axis_size("mp")
    my_shard = lax.axis_index("dp")
    my_column = lax.axis_index("mp")
    sample_shard_count = latents.shape[0]
    prompt_dev = encoder_cache.shape[0]
    cache_len = encoder_cache.shape[2]
    cache_width = encoder_cache.shape[1]
    cell_count = latents.shape[2]
    slot_limit = 2 * (sample_shard_count // dp_count)
    all_samples = destination.shape[0]
    owner_target = destination.reshape(dp_count, sample_shard_count)
    positions = jnp.arange(sample_shard_count, dtype=jnp.int32)
    before = positions[None, :] < positions[:, None]
    same_target = owner_target[:, :, None] == owner_target[:, None, :]
    slot_rank = jnp.sum((same_target & before[None]).astype(jnp.int32), axis=2)
    my_target = lax.dynamic_index_in_dim(owner_target, my_shard, 0, keepdims=False)
    my_rank = lax.dynamic_index_in_dim(slot_rank, my_shard, 0, keepdims=False)
    my_prompts = (
        lax.dynamic_slice_in_dim(
            kept_prompt_list, my_shard * sample_shard_count, sample_shard_count
        )
        - my_shard * prompt_dev
    )
    send_slot = my_target * slot_limit + my_rank
    slot_table = send_slot[:, None] == jnp.arange(dp_count * slot_limit, dtype=jnp.int32)[None, :]
    source_row = jnp.sum(jnp.where(slot_table, my_prompts[:, None], 0), axis=0)
    filled = jnp.any(slot_table, axis=0)
    send_rows = jnp.take(encoder_cache, source_row, axis=0)
    send_rows = jnp.where(filled[:, None, None], send_rows, jnp.zeros_like(send_rows))
    outgoing = send_rows.reshape(dp_count, slot_limit, cache_width, cache_len)
    arriving = destination == my_shard
    arrival_pos = jnp.cumsum(arriving.astype(jnp.int32)) - 1
    selector = arriving[None, :] & (arrival_pos[None, :] == positions[:, None])
    kept_prompt = jnp.sum(
        jnp.where(selector, jnp.arange(all_samples, dtype=jnp.int32)[None, :], 0), axis=1
    )
    incoming_order_rank = jnp.sum(jnp.where(selector, slot_rank.reshape(-1)[None, :], 0), axis=1)
    prompt_ids = jnp.sum(jnp.where(selector, kept_prompt_list[None, :], 0), axis=1)
    landing_slot = kept_prompt // sample_shard_count * slot_limit + incoming_order_rank
    prompt_hits = prompt_ids[:, None] == jnp.arange(lengths.shape[0], dtype=jnp.int32)[None, :]
    my_lengths = jnp.sum(jnp.where(prompt_hits, lengths[None, :], 0), axis=1)
    fast = dp_count == 4 and mp_count == 4 and lax.axis_size("groups") == 2
    weight_shards = (first_kernel, second_kernel, query_weight, output_weight)
    if fast:
        block_ids = jnp.arange(dp_count, dtype=jnp.int32)
        channel_blocks = jnp.bitwise_xor(block_ids, my_column)
        pieces = (first_kernel, second_kernel, query_weight, output_weight)
        dense = [piece.reshape(-1, 128) for piece in pieces]
        natural, latents, line_done = split_line_gather(jnp.concatenate(dense, axis=0), latents)
        kernel_rows = dense[0].shape[0] + dense[1].shape[0]
        kernel_part = jnp.take(natural[:, :kernel_rows], channel_blocks, axis=0, mode="clip")
        proj_part = natural[:, kernel_rows:]
        full_weights = []
        cut = 0
        query_part = jnp.take(proj_part, channel_blocks, axis=0, mode="clip")
        for piece, block, source in zip(pieces, dense, (kernel_part, kernel_part, query_part, proj_part)):
            if cut == kernel_rows:
                cut = 0
            chunk = source[:, cut : cut + block.shape[0]]
            cut += block.shape[0]
            full_weights.append(chunk.reshape((dp_count * piece.shape[0],) + piece.shape[1:]))
        gathered = (kernel_part, proj_part)
        full_weights = tuple(full_weights)
        outgoing = lax.optimization_barrier((outgoing, line_done))[0]
        spread_channels = pair_gather_channels
    else:
        full_weights = (
            gather_kernel(first_kernel),
            gather_kernel(second_kernel),
            gather_projection(query_weight),
            gather_projection(output_weight),
        )
        spread_channels = gather_channels
    incoming = lax.all_to_all(outgoing, "dp", split_axis=0, concat_axis=0, tiled=True)
    my_pairs = jnp.take(
        incoming.reshape(dp_count * slot_limit, cache_width, cache_len), landing_slot, axis=0
    )
    start_field = latents.astype(jnp.float32)
    activated = jax.nn.silu(norm_groups(start_field, group_width)).astype(jnp.bfloat16)
    first_in = spread_channels(activated)

    def convolve(full_field, which_weight):
        half = full_field.shape[0] // 2
        return jnp.concatenate(
            [
                apply_kernel(full_field[:half], full_weights[which_weight]),
                apply_kernel(full_field[half:], full_weights[which_weight]),
            ]
        )

    def project(field_rows, which_weight):
        full_weight = full_weights[which_weight]
        return jnp.einsum(
            "scq,ce->seq", field_rows, full_weight, preferred_element_type=jnp.float32
        )

    first_out = convolve(first_in, 0)
    scale_term = modulation[:, 0, :].astype(jnp.float32)[:, :, None]
    shift_term = modulation[:, 1, :].astype(jnp.float32)[:, :, None]
    modulated = jax.nn.silu(
        norm_groups(first_out, group_width) * (1.0 + scale_term) + shift_term
    ).astype(jnp.bfloat16)
    if fast:
        second_in = pair_gather_channel_minor(modulated)
    else:
        second_in = spread_channels(modulated)
    residual = start_field + convolve(second_in, 1)
    normed_out = norm_groups(residual, group_width).astype(jnp.bfloat16)
    local_samples = sample_shard_count // mp_count
    if fast:
        query_cells = xor_spread_samples(normed_out, local_samples)
        my_pairs = lax.optimization_barrier((my_pairs, query_cells))[0]
    else:
        query_cells = lax.all_to_all(normed_out, "mp", split_axis=0, concat_axis=1, tiled=True)
    if fast:
        spread = xor_spread_samples(my_pairs, local_samples)
        width = my_pairs.shape[1]
        stacked = jnp.stack([spread[:, i * width : (i + 1) * width] for i in range(mp_count)])
        order = jnp.bitwise_xor(jnp.arange(mp_count, dtype=jnp.int32), my_column)
        natural = jnp.take(stacked, order, axis=0, mode="clip")
        pair_heads = jnp.transpose(natural, (1, 0, 2, 3)).reshape(
            local_samples, mp_count * width, cache_len
        )
    else:
        pair_heads = lax.all_to_all(my_pairs, "mp", split_axis=0, concat_axis=1, tiled=True)
    total_width = query_cells.shape[1]
    head_count = total_width // HEAD
    queries = project(query_cells, 2).astype(jnp.bfloat16)
    queries = queries.reshape(local_samples, head_count, HEAD, cell_count)
    heads_of_keys = pair_heads[:, :total_width, :].reshape(
        local_samples, head_count, HEAD, cache_len
    )
    value_heads = pair_heads[:, total_width:, :].reshape(local_samples, head_count, HEAD, cache_len)
    scores = jnp.einsum(
        "shdq,shdk->shqk", queries, heads_of_keys, preferred_element_type=jnp.float32
    ) * HEAD ** (-0.5)
    local_lengths = lax.dynamic_slice_in_dim(my_lengths, my_column * local_samples, local_samples)
    visible = (
        jnp.arange(cache_len, dtype=jnp.int32)[None, None, None, :]
        < local_lengths[:, None, None, None]
    )
    scores = jnp.where(visible, scores, MASKED)
    row_peak = jnp.max(scores, axis=3, keepdims=True)
    exponent = jnp.exp(scores - row_peak)
    attention = (exponent / jnp.sum(exponent, axis=3, keepdims=True)).astype(jnp.bfloat16)
    attention = lax.optimization_barrier(attention)
    context = jnp.einsum(
        "shqk,shdk->sqhd", attention, value_heads, preferred_element_type=jnp.float32
    ).astype(jnp.bfloat16)
    attended = jnp.einsum(
        "sqc,ce->seq",
        context.reshape(local_samples, cell_count, total_width),
        full_weights[3],
        preferred_element_type=jnp.float32,
    ).astype(jnp.bfloat16)
    if fast:
        returned = xor_return_channels(attended, attended.shape[1] // mp_count)
    else:
        returned = lax.all_to_all(attended, "mp", split_axis=1, concat_axis=0, tiled=True)
    final_field = residual + returned.astype(jnp.float32)
    return final_field.astype(jnp.bfloat16)


def solution(mesh):
    in_specs = (
        P(("groups", "dp"), "mp", None),
        P(("groups", "dp"), None, "mp"),
        P("dp", None, "mp"),
        P("dp", None, "mp"),
        P(("groups", "dp"), "mp", None),
        P("dp", None),
        P("dp", None),
        P("groups"),
        P("groups"),
        P("groups"),
    )
    out_specs = P(("groups", "dp"), "mp", None)
    return jax.shard_map(local, mesh=mesh, in_specs=in_specs, out_specs=out_specs, check_vma=False)
```

```python
import jax
import jax.numpy as jnp
from jax import lax
from jax.sharding import PartitionSpec as P

C = 640
GROUPS = 32
HEAD = 64
SIDE = 8


EPSILON = 1e-05
MASKED = -1e30


def norm_groups(values, group_width):
    field_shape = values.shape
    grouped = values.reshape(
        field_shape[0], field_shape[1] // group_width, group_width, field_shape[2]
    )
    center = grouped - jnp.mean(grouped, axis=(2, 3), keepdims=True)
    spread = jnp.mean(center * center, axis=(2, 3), keepdims=True)
    return (center * lax.rsqrt(spread + EPSILON)).reshape(field_shape)


def gather_channels(field):
    return lax.all_gather(field, "mp", axis=1, tiled=True)


def pair_gather_channels(field):
    dense = field.reshape(-1, 128)
    across = lax.ppermute(dense, "mp", [(i, i ^ 2) for i in range(4)])
    beside = lax.ppermute(dense, "mp", [(i, i ^ 1) for i in range(4)])
    relayed = lax.ppermute(across, "mp", [(i, i ^ 1) for i in range(4)])
    parts = [part.reshape(field.shape) for part in (beside, across, relayed)]
    return jnp.concatenate([field] + parts, axis=1)


def line_gather_flat(flat, count):
    my_shard = lax.axis_index("dp")
    rightward = [(i, i + 1) for i in range(count - 1)]
    leftward = [(i + 1, i) for i in range(count - 1)]
    going_right, going_left = flat, flat
    held = [flat]
    from_left, from_right = [], []
    for _ in range(1, count):
        going_right = lax.ppermute(going_right, "dp", rightward)
        going_left = lax.ppermute(going_left, "dp", leftward)
        from_left.append(going_right)
        from_right.append(going_left)
    line = jnp.stack(from_left[::-1] + held + from_right)
    return lax.dynamic_slice_in_dim(line, count - 1 - my_shard, count, axis=0)


def split_line_gather(packed, gated):
    my_shard = lax.axis_index("dp")
    my_group = lax.axis_index("groups")
    halves = packed.reshape(2, packed.shape[0] // 2, packed.shape[1])
    mine = lax.dynamic_index_in_dim(halves, my_group, 0, keepdims=False)
    mine, gated = lax.optimization_barrier((mine, gated))
    rightward = [(i, i + 1) for i in range(3)]
    leftward = [(i + 1, i) for i in range(3)]
    swap = [(0, 1), (1, 0)]
    left_1 = lax.ppermute(mine, "dp", rightward)
    right_1 = lax.ppermute(mine, "dp", leftward)
    first_swap = lax.ppermute(jnp.where(my_shard >= 1, left_1, right_1), "groups", swap)
    left_2 = lax.ppermute(left_1, "dp", rightward)
    right_2 = lax.ppermute(right_1, "dp", leftward)
    second_swap = lax.ppermute(jnp.where(my_shard >= 2, left_2, right_2), "groups", swap)
    left_3 = lax.ppermute(left_2, "dp", rightward)
    right_3 = lax.ppermute(right_2, "dp", leftward)
    third_pick = jnp.where(my_shard == 0, right_3, jnp.where(my_shard == 3, left_3, right_1))
    third_swap = lax.ppermute(third_pick, "groups", swap)

    def whole(own_half, other_half):
        lead = jnp.where(my_group == 0, own_half, other_half)
        tail = jnp.where(my_group == 0, other_half, own_half)
        return jnp.concatenate([lead, tail], axis=0)

    line = jnp.stack(
        [
            whole(left_3, third_swap),
            whole(left_2, second_swap),
            whole(left_1, first_swap),
            packed,
            whole(right_1, jnp.where(my_shard == 0, first_swap, third_swap)),
            whole(right_2, second_swap),
            whole(right_3, third_swap),
        ]
    )
    return lax.dynamic_slice_in_dim(line, 3 - my_shard, 4, axis=0), gated, (left_3, right_3)


def pair_gather_channel_minor(field):
    cell_major = jnp.transpose(field, (0, 2, 1))
    dense = cell_major.reshape(-1, 128)
    across = lax.ppermute(dense, "mp", [(i, i ^ 2) for i in range(4)])
    beside = lax.ppermute(dense, "mp", [(i, i ^ 1) for i in range(4)])
    relayed = lax.ppermute(across, "mp", [(i, i ^ 1) for i in range(4)])
    parts = [jnp.transpose(part.reshape(cell_major.shape), (0, 2, 1)) for part in (beside, across, relayed)]
    return jnp.concatenate([field] + parts, axis=1)


def xor_spread_samples(field, group):
    my_column = lax.axis_index("mp")
    parts = [lax.dynamic_slice_in_dim(field, my_column * group, group, axis=0)]
    for step in range(1, 4):
        block = lax.dynamic_slice_in_dim(field, (my_column ^ step) * group, group, axis=0)
        moved = lax.ppermute(block.reshape(-1, 128), "mp", [(i, i ^ step) for i in range(4)])
        parts.append(moved.reshape(block.shape))
    return jnp.concatenate(parts, axis=1)


def xor_return_channels(field, width):
    my_column = lax.axis_index("mp")
    parts = [lax.dynamic_slice_in_dim(field, my_column * width, width, axis=1)]
    for step in range(1, 4):
        block = lax.dynamic_slice_in_dim(field, (my_column ^ step) * width, width, axis=1)
        moved = lax.ppermute(block.reshape(-1, 128), "mp", [(i, i ^ step) for i in range(4)])
        parts.append(moved.reshape(block.shape))
    natural = []
    for block in range(4):
        picked = parts[block]
        for column in range(1, 4):
            picked = jnp.where(my_column == column, parts[block ^ column], picked)
        natural.append(picked)
    return jnp.concatenate(natural, axis=0)


def shift_parts(shard, count):
    parts = [shard]
    for step in range(1, count):
        parts.append(lax.ppermute(shard, "dp", [(i, (i + step) % count) for i in range(count)]))
    return jnp.stack(parts)


def order_rows(stacked, wanted_blocks):
    my_shard = lax.axis_index("dp")
    count = stacked.shape[0]
    picked = jnp.take(stacked, (my_shard - wanted_blocks) % count, axis=0, mode="clip")
    return picked.reshape((count * stacked.shape[1],) + stacked.shape[2:])


def gather_kernel(weight_shard):
    return lax.all_gather(weight_shard, "dp", axis=0, tiled=True)


def gather_projection(weight_shard):
    return lax.all_gather(weight_shard, "dp", axis=0, tiled=True)


def apply_kernel(full_field, kernel):
    sample_count = full_field.shape[0]
    out_width = kernel.shape[2]
    tap_images = jnp.einsum("scq,cte->stqe", full_field, kernel, preferred_element_type=jnp.float32)
    tap_images = tap_images.reshape(sample_count, 9, SIDE, SIDE, out_width)
    padded = jnp.pad(tap_images, ((0, 0), (0, 0), (1, 1), (1, 1), (0, 0)))
    running = padded[:, 0, 0:SIDE, 0:SIDE, :]
    for offset in range(1, 9):
        row_shift, col_shift = (offset // 3, offset % 3)
        running = (
            running
            + padded[:, offset, row_shift : row_shift + SIDE, col_shift : col_shift + SIDE, :]
        )
    return jnp.transpose(running.reshape(sample_count, SIDE * SIDE, out_width), (0, 2, 1))


def local(
    latents,
    modulation,
    first_kernel,
    second_kernel,
    encoder_cache,
    query_weight,
    output_weight,
    kept_prompt_list,
    destination,
    lengths,
):
    group_width = C // GROUPS
    dp_count = lax.axis_size("dp")
    mp_count = lax.axis_size("mp")
    my_shard = lax.axis_index("dp")
    my_column = lax.axis_index("mp")
    sample_shard_count = latents.shape[0]
    prompt_dev = encoder_cache.shape[0]
    cache_len = encoder_cache.shape[2]
    cache_width = encoder_cache.shape[1]
    cell_count = latents.shape[2]
    slot_limit = 2 * (sample_shard_count // dp_count)
    all_samples = destination.shape[0]
    owner_target = destination.reshape(dp_count, sample_shard_count)
    positions = jnp.arange(sample_shard_count, dtype=jnp.int32)
    before = positions[None, :] < positions[:, None]
    same_target = owner_target[:, :, None] == owner_target[:, None, :]
    slot_rank = jnp.sum((same_target & before[None]).astype(jnp.int32), axis=2)
    my_target = lax.dynamic_index_in_dim(owner_target, my_shard, 0, keepdims=False)
    my_rank = lax.dynamic_index_in_dim(slot_rank, my_shard, 0, keepdims=False)
    my_prompts = (
        lax.dynamic_slice_in_dim(
            kept_prompt_list, my_shard * sample_shard_count, sample_shard_count
        )
        - my_shard * prompt_dev
    )
    send_slot = my_target * slot_limit + my_rank
    slot_table = send_slot[:, None] == jnp.arange(dp_count * slot_limit, dtype=jnp.int32)[None, :]
    source_row = jnp.sum(jnp.where(slot_table, my_prompts[:, None], 0), axis=0)
    filled = jnp.any(slot_table, axis=0)
    send_rows = jnp.take(encoder_cache, source_row, axis=0)
    send_rows = jnp.where(filled[:, None, None], send_rows, jnp.zeros_like(send_rows))
    outgoing = send_rows.reshape(dp_count, slot_limit, cache_width, cache_len)
    arriving = destination == my_shard
    arrival_pos = jnp.cumsum(arriving.astype(jnp.int32)) - 1
    selector = arriving[None, :] & (arrival_pos[None, :] == positions[:, None])
    kept_prompt = jnp.sum(
        jnp.where(selector, jnp.arange(all_samples, dtype=jnp.int32)[None, :], 0), axis=1
    )
    incoming_order_rank = jnp.sum(jnp.where(selector, slot_rank.reshape(-1)[None, :], 0), axis=1)
    prompt_ids = jnp.sum(jnp.where(selector, kept_prompt_list[None, :], 0), axis=1)
    landing_slot = kept_prompt // sample_shard_count * slot_limit + incoming_order_rank
    prompt_hits = prompt_ids[:, None] == jnp.arange(lengths.shape[0], dtype=jnp.int32)[None, :]
    my_lengths = jnp.sum(jnp.where(prompt_hits, lengths[None, :], 0), axis=1)
    fast = dp_count == 4 and mp_count == 4 and lax.axis_size("groups") == 2
    weight_shards = (first_kernel, second_kernel, query_weight, output_weight)
    if fast:
        block_ids = jnp.arange(dp_count, dtype=jnp.int32)
        channel_blocks = jnp.bitwise_xor(block_ids, my_column)
        pieces = (first_kernel, second_kernel, query_weight, output_weight)
        dense = [piece.reshape(-1, 128) for piece in pieces]
        natural, latents, line_done = split_line_gather(jnp.concatenate(dense, axis=0), latents)
        kernel_rows = dense[0].shape[0] + dense[1].shape[0]
        kernel_part = jnp.take(natural[:, :kernel_rows], channel_blocks, axis=0, mode="clip")
        proj_part = natural[:, kernel_rows:]
        full_weights = []
        cut = 0
        query_part = jnp.take(proj_part, channel_blocks, axis=0, mode="clip")
        for piece, block, source in zip(pieces, dense, (kernel_part, kernel_part, query_part, proj_part)):
            if cut == kernel_rows:
                cut = 0
            chunk = source[:, cut : cut + block.shape[0]]
            cut += block.shape[0]
            full_weights.append(chunk.reshape((dp_count * piece.shape[0],) + piece.shape[1:]))
        gathered = (kernel_part, proj_part)
        full_weights = tuple(full_weights)
        outgoing = lax.optimization_barrier((outgoing, line_done))[0]
        spread_channels = pair_gather_channels
    else:
        full_weights = (
            gather_kernel(first_kernel),
            gather_kernel(second_kernel),
            gather_projection(query_weight),
            gather_projection(output_weight),
        )
        spread_channels = gather_channels
    incoming = lax.all_to_all(outgoing, "dp", split_axis=0, concat_axis=0, tiled=True)
    my_pairs = jnp.take(
        incoming.reshape(dp_count * slot_limit, cache_width, cache_len), landing_slot, axis=0
    )
    start_field = latents.astype(jnp.float32)
    activated = jax.nn.silu(norm_groups(start_field, group_width)).astype(jnp.bfloat16)
    first_in = spread_channels(activated)

    def convolve(full_field, which_weight):
        half = full_field.shape[0] // 2
        return jnp.concatenate(
            [
                apply_kernel(full_field[:half], full_weights[which_weight]),
                apply_kernel(full_field[half:], full_weights[which_weight]),
            ]
        )

    def project(field_rows, which_weight):
        full_weight = full_weights[which_weight]
        return jnp.einsum(
            "scq,ce->seq", field_rows, full_weight, preferred_element_type=jnp.float32
        )

    first_out = convolve(first_in, 0)
    scale_term = modulation[:, 0, :].astype(jnp.float32)[:, :, None]
    shift_term = modulation[:, 1, :].astype(jnp.float32)[:, :, None]
    modulated = jax.nn.silu(
        norm_groups(first_out, group_width) * (1.0 + scale_term) + shift_term
    ).astype(jnp.bfloat16)
    if fast:
        second_in = pair_gather_channel_minor(modulated)
    else:
        second_in = spread_channels(modulated)
    residual = start_field + convolve(second_in, 1)
    normed_out = norm_groups(residual, group_width).astype(jnp.bfloat16)
    local_samples = sample_shard_count // mp_count
    if fast:
        query_cells = xor_spread_samples(normed_out, local_samples)
        my_pairs = lax.optimization_barrier((my_pairs, query_cells))[0]
    else:
        query_cells = lax.all_to_all(normed_out, "mp", split_axis=0, concat_axis=1, tiled=True)
    pair_heads = lax.all_to_all(my_pairs, "mp", split_axis=0, concat_axis=1, tiled=True)
    total_width = query_cells.shape[1]
    head_count = total_width // HEAD
    queries = project(query_cells, 2).astype(jnp.bfloat16)
    queries = queries.reshape(local_samples, head_count, HEAD, cell_count)
    heads_of_keys = pair_heads[:, :total_width, :].reshape(
        local_samples, head_count, HEAD, cache_len
    )
    value_heads = pair_heads[:, total_width:, :].reshape(local_samples, head_count, HEAD, cache_len)
    scores = jnp.einsum(
        "shdq,shdk->shqk", queries, heads_of_keys, preferred_element_type=jnp.float32
    ) * HEAD ** (-0.5)
    local_lengths = lax.dynamic_slice_in_dim(my_lengths, my_column * local_samples, local_samples)
    visible = (
        jnp.arange(cache_len, dtype=jnp.int32)[None, None, None, :]
        < local_lengths[:, None, None, None]
    )
    scores = jnp.where(visible, scores, MASKED)
    row_peak = jnp.max(scores, axis=3, keepdims=True)
    exponent = jnp.exp(scores - row_peak)
    attention = (exponent / jnp.sum(exponent, axis=3, keepdims=True)).astype(jnp.bfloat16)
    attention = lax.optimization_barrier(attention)
    context = jnp.einsum(
        "shqk,shdk->sqhd", attention, value_heads, preferred_element_type=jnp.float32
    ).astype(jnp.bfloat16)
    attended = jnp.einsum(
        "sqc,ce->seq",
        context.reshape(local_samples, cell_count, total_width),
        full_weights[3],
        preferred_element_type=jnp.float32,
    ).astype(jnp.bfloat16)
    if fast:
        returned = xor_return_channels(attended, attended.shape[1] // mp_count)
    else:
        returned = lax.all_to_all(attended, "mp", split_axis=1, concat_axis=0, tiled=True)
    final_field = residual + returned.astype(jnp.float32)
    return final_field.astype(jnp.bfloat16)


def solution(mesh):
    in_specs = (
        P(("groups", "dp"), "mp", None),
        P(("groups", "dp"), None, "mp"),
        P("dp", None, "mp"),
        P("dp", None, "mp"),
        P(("groups", "dp"), "mp", None),
        P("dp", None),
        P("dp", None),
        P("groups"),
        P("groups"),
        P("groups"),
    )
    out_specs = P(("groups", "dp"), "mp", None)
    return jax.shard_map(local, mesh=mesh, in_specs=in_specs, out_specs=out_specs, check_vma=False)
```

```python
import jax
import jax.numpy as jnp
from jax import lax
from jax.sharding import PartitionSpec as P

C = 640
GROUPS = 32
HEAD = 64
SIDE = 8


EPSILON = 1e-05
MASKED = -1e30


def norm_groups(values, group_width):
    field_shape = values.shape
    grouped = values.reshape(
        field_shape[0], field_shape[1] // group_width, group_width, field_shape[2]
    )
    center = grouped - jnp.mean(grouped, axis=(2, 3), keepdims=True)
    spread = jnp.mean(center * center, axis=(2, 3), keepdims=True)
    return (center * lax.rsqrt(spread + EPSILON)).reshape(field_shape)


def gather_channels(field):
    return lax.all_gather(field, "mp", axis=1, tiled=True)


def pair_gather_channels(field):
    dense = field.reshape(-1, 128)
    across = lax.ppermute(dense, "mp", [(i, i ^ 2) for i in range(4)])
    beside = lax.ppermute(dense, "mp", [(i, i ^ 1) for i in range(4)])
    relayed = lax.ppermute(across, "mp", [(i, i ^ 1) for i in range(4)])
    parts = [part.reshape(field.shape) for part in (beside, across, relayed)]
    return jnp.concatenate([field] + parts, axis=1)


def line_gather_flat(flat, count):
    my_shard = lax.axis_index("dp")
    rightward = [(i, i + 1) for i in range(count - 1)]
    leftward = [(i + 1, i) for i in range(count - 1)]
    going_right, going_left = flat, flat
    held = [flat]
    from_left, from_right = [], []
    for _ in range(1, count):
        going_right = lax.ppermute(going_right, "dp", rightward)
        going_left = lax.ppermute(going_left, "dp", leftward)
        from_left.append(going_right)
        from_right.append(going_left)
    line = jnp.stack(from_left[::-1] + held + from_right)
    return lax.dynamic_slice_in_dim(line, count - 1 - my_shard, count, axis=0)


def split_line_gather(packed, gated):
    my_shard = lax.axis_index("dp")
    my_group = lax.axis_index("groups")
    halves = packed.reshape(2, packed.shape[0] // 2, packed.shape[1])
    mine = lax.dynamic_index_in_dim(halves, my_group, 0, keepdims=False)
    mine, gated = lax.optimization_barrier((mine, gated))
    rightward = [(i, i + 1) for i in range(3)]
    leftward = [(i + 1, i) for i in range(3)]
    swap = [(0, 1), (1, 0)]
    left_1 = lax.ppermute(mine, "dp", rightward)
    right_1 = lax.ppermute(mine, "dp", leftward)
    first_swap = lax.ppermute(jnp.where(my_shard >= 1, left_1, right_1), "groups", swap)
    left_2 = lax.ppermute(left_1, "dp", rightward)
    right_2 = lax.ppermute(right_1, "dp", leftward)
    second_swap = lax.ppermute(jnp.where(my_shard >= 2, left_2, right_2), "groups", swap)
    left_3 = lax.ppermute(left_2, "dp", rightward)
    right_3 = lax.ppermute(right_2, "dp", leftward)
    third_pick = jnp.where(my_shard == 0, right_3, jnp.where(my_shard == 3, left_3, right_1))
    third_swap = lax.ppermute(third_pick, "groups", swap)

    def whole(own_half, other_half):
        lead = jnp.where(my_group == 0, own_half, other_half)
        tail = jnp.where(my_group == 0, other_half, own_half)
        return jnp.concatenate([lead, tail], axis=0)

    line = jnp.stack(
        [
            whole(left_3, third_swap),
            whole(left_2, second_swap),
            whole(left_1, first_swap),
            packed,
            whole(right_1, jnp.where(my_shard == 0, first_swap, third_swap)),
            whole(right_2, second_swap),
            whole(right_3, third_swap),
        ]
    )
    return lax.dynamic_slice_in_dim(line, 3 - my_shard, 4, axis=0), gated, (left_3, right_3)


def pair_gather_channel_minor(field):
    cell_major = jnp.transpose(field, (0, 2, 1))
    dense = cell_major.reshape(-1, 128)
    across = lax.ppermute(dense, "mp", [(i, i ^ 2) for i in range(4)])
    beside = lax.ppermute(dense, "mp", [(i, i ^ 1) for i in range(4)])
    relayed = lax.ppermute(across, "mp", [(i, i ^ 1) for i in range(4)])
    parts = [jnp.transpose(part.reshape(cell_major.shape), (0, 2, 1)) for part in (beside, across, relayed)]
    return jnp.concatenate([field] + parts, axis=1)


def xor_spread_samples(field, group):
    my_column = lax.axis_index("mp")
    parts = [lax.dynamic_slice_in_dim(field, my_column * group, group, axis=0)]
    for step in range(1, 4):
        block = lax.dynamic_slice_in_dim(field, (my_column ^ step) * group, group, axis=0)
        moved = lax.ppermute(block.reshape(-1, 128), "mp", [(i, i ^ step) for i in range(4)])
        parts.append(moved.reshape(block.shape))
    return jnp.concatenate(parts, axis=1)


def xor_return_channels(field, width):
    my_column = lax.axis_index("mp")
    parts = [lax.dynamic_slice_in_dim(field, my_column * width, width, axis=1)]
    for step in range(1, 4):
        block = lax.dynamic_slice_in_dim(field, (my_column ^ step) * width, width, axis=1)
        moved = lax.ppermute(block.reshape(-1, 128), "mp", [(i, i ^ step) for i in range(4)])
        parts.append(moved.reshape(block.shape))
    natural = []
    for block in range(4):
        picked = parts[block]
        for column in range(1, 4):
            picked = jnp.where(my_column == column, parts[block ^ column], picked)
        natural.append(picked)
    return jnp.concatenate(natural, axis=0)


def shift_parts(shard, count):
    parts = [shard]
    for step in range(1, count):
        parts.append(lax.ppermute(shard, "dp", [(i, (i + step) % count) for i in range(count)]))
    return jnp.stack(parts)


def order_rows(stacked, wanted_blocks):
    my_shard = lax.axis_index("dp")
    count = stacked.shape[0]
    picked = jnp.take(stacked, (my_shard - wanted_blocks) % count, axis=0, mode="clip")
    return picked.reshape((count * stacked.shape[1],) + stacked.shape[2:])


def gather_kernel(weight_shard):
    return lax.all_gather(weight_shard, "dp", axis=0, tiled=True)


def gather_projection(weight_shard):
    return lax.all_gather(weight_shard, "dp", axis=0, tiled=True)


def apply_kernel(full_field, kernel):
    sample_count = full_field.shape[0]
    out_width = kernel.shape[2]
    tap_images = jnp.einsum("scq,cte->stqe", full_field, kernel, preferred_element_type=jnp.float32)
    tap_images = tap_images.reshape(sample_count, 9, SIDE, SIDE, out_width)
    padded = jnp.pad(tap_images, ((0, 0), (0, 0), (1, 1), (1, 1), (0, 0)))
    running = padded[:, 0, 0:SIDE, 0:SIDE, :]
    for offset in range(1, 9):
        row_shift, col_shift = (offset // 3, offset % 3)
        running = (
            running
            + padded[:, offset, row_shift : row_shift + SIDE, col_shift : col_shift + SIDE, :]
        )
    return jnp.transpose(running.reshape(sample_count, SIDE * SIDE, out_width), (0, 2, 1))


def local(
    latents,
    modulation,
    first_kernel,
    second_kernel,
    encoder_cache,
    query_weight,
    output_weight,
    kept_prompt_list,
    destination,
    lengths,
):
    group_width = C // GROUPS
    dp_count = lax.axis_size("dp")
    mp_count = lax.axis_size("mp")
    my_shard = lax.axis_index("dp")
    my_column = lax.axis_index("mp")
    sample_shard_count = latents.shape[0]
    prompt_dev = encoder_cache.shape[0]
    cache_len = encoder_cache.shape[2]
    cache_width = encoder_cache.shape[1]
    cell_count = latents.shape[2]
    slot_limit = 2 * (sample_shard_count // dp_count)
    all_samples = destination.shape[0]
    owner_target = destination.reshape(dp_count, sample_shard_count)
    positions = jnp.arange(sample_shard_count, dtype=jnp.int32)
    before = positions[None, :] < positions[:, None]
    same_target = owner_target[:, :, None] == owner_target[:, None, :]
    slot_rank = jnp.sum((same_target & before[None]).astype(jnp.int32), axis=2)
    my_target = lax.dynamic_index_in_dim(owner_target, my_shard, 0, keepdims=False)
    my_rank = lax.dynamic_index_in_dim(slot_rank, my_shard, 0, keepdims=False)
    my_prompts = (
        lax.dynamic_slice_in_dim(
            kept_prompt_list, my_shard * sample_shard_count, sample_shard_count
        )
        - my_shard * prompt_dev
    )
    send_slot = my_target * slot_limit + my_rank
    slot_table = send_slot[:, None] == jnp.arange(dp_count * slot_limit, dtype=jnp.int32)[None, :]
    source_row = jnp.sum(jnp.where(slot_table, my_prompts[:, None], 0), axis=0)
    filled = jnp.any(slot_table, axis=0)
    send_rows = jnp.take(encoder_cache, source_row, axis=0)
    send_rows = jnp.where(filled[:, None, None], send_rows, jnp.zeros_like(send_rows))
    outgoing = send_rows.reshape(dp_count, slot_limit, cache_width, cache_len)
    arriving = destination == my_shard
    arrival_pos = jnp.cumsum(arriving.astype(jnp.int32)) - 1
    selector = arriving[None, :] & (arrival_pos[None, :] == positions[:, None])
    kept_prompt = jnp.sum(
        jnp.where(selector, jnp.arange(all_samples, dtype=jnp.int32)[None, :], 0), axis=1
    )
    incoming_order_rank = jnp.sum(jnp.where(selector, slot_rank.reshape(-1)[None, :], 0), axis=1)
    prompt_ids = jnp.sum(jnp.where(selector, kept_prompt_list[None, :], 0), axis=1)
    landing_slot = kept_prompt // sample_shard_count * slot_limit + incoming_order_rank
    prompt_hits = prompt_ids[:, None] == jnp.arange(lengths.shape[0], dtype=jnp.int32)[None, :]
    my_lengths = jnp.sum(jnp.where(prompt_hits, lengths[None, :], 0), axis=1)
    fast = dp_count == 4 and mp_count == 4 and lax.axis_size("groups") == 2
    weight_shards = (first_kernel, second_kernel, query_weight, output_weight)
    if fast:
        block_ids = jnp.arange(dp_count, dtype=jnp.int32)
        channel_blocks = jnp.bitwise_xor(block_ids, my_column)
        pieces = (first_kernel, second_kernel, query_weight, output_weight)
        dense = [piece.reshape(-1, 128) for piece in pieces]
        natural, latents, line_done = split_line_gather(jnp.concatenate(dense, axis=0), latents)
        kernel_rows = dense[0].shape[0] + dense[1].shape[0]
        def xor_order(blocks):
            ordered = []
            for position in range(dp_count):
                picked = blocks[position]
                for column in range(1, dp_count):
                    picked = jnp.where(my_column == column, blocks[position ^ column], picked)
                ordered.append(picked)
            return jnp.stack(ordered)

        kernel_part = xor_order(natural[:, :kernel_rows])
        proj_part = natural[:, kernel_rows:]
        full_weights = []
        cut = 0
        query_part = xor_order(proj_part)
        for piece, block, source in zip(pieces, dense, (kernel_part, kernel_part, query_part, proj_part)):
            if cut == kernel_rows:
                cut = 0
            chunk = source[:, cut : cut + block.shape[0]]
            cut += block.shape[0]
            full_weights.append(chunk.reshape((dp_count * piece.shape[0],) + piece.shape[1:]))
        gathered = (kernel_part, proj_part)
        full_weights = tuple(full_weights)
        outgoing = lax.optimization_barrier((outgoing, line_done))[0]
        spread_channels = pair_gather_channels
    else:
        full_weights = (
            gather_kernel(first_kernel),
            gather_kernel(second_kernel),
            gather_projection(query_weight),
            gather_projection(output_weight),
        )
        spread_channels = gather_channels
    incoming = lax.all_to_all(outgoing, "dp", split_axis=0, concat_axis=0, tiled=True)
    my_pairs = jnp.take(
        incoming.reshape(dp_count * slot_limit, cache_width, cache_len), landing_slot, axis=0
    )
    start_field = latents.astype(jnp.float32)
    activated = jax.nn.silu(norm_groups(start_field, group_width)).astype(jnp.bfloat16)
    first_in = spread_channels(activated)

    def convolve(full_field, which_weight):
        half = full_field.shape[0] // 2
        return jnp.concatenate(
            [
                apply_kernel(full_field[:half], full_weights[which_weight]),
                apply_kernel(full_field[half:], full_weights[which_weight]),
            ]
        )

    def project(field_rows, which_weight):
        full_weight = full_weights[which_weight]
        return jnp.einsum(
            "scq,ce->seq", field_rows, full_weight, preferred_element_type=jnp.float32
        )

    first_out = convolve(first_in, 0)
    scale_term = modulation[:, 0, :].astype(jnp.float32)[:, :, None]
    shift_term = modulation[:, 1, :].astype(jnp.float32)[:, :, None]
    modulated = jax.nn.silu(
        norm_groups(first_out, group_width) * (1.0 + scale_term) + shift_term
    ).astype(jnp.bfloat16)
    if fast:
        second_in = pair_gather_channel_minor(modulated)
    else:
        second_in = spread_channels(modulated)
    residual = start_field + convolve(second_in, 1)
    normed_out = norm_groups(residual, group_width).astype(jnp.bfloat16)
    local_samples = sample_shard_count // mp_count
    if fast:
        query_cells = xor_spread_samples(normed_out, local_samples)
        my_pairs = lax.optimization_barrier((my_pairs, query_cells))[0]
    else:
        query_cells = lax.all_to_all(normed_out, "mp", split_axis=0, concat_axis=1, tiled=True)
    pair_heads = lax.all_to_all(my_pairs, "mp", split_axis=0, concat_axis=1, tiled=True)
    total_width = query_cells.shape[1]
    head_count = total_width // HEAD
    queries = project(query_cells, 2).astype(jnp.bfloat16)
    queries = queries.reshape(local_samples, head_count, HEAD, cell_count)
    heads_of_keys = pair_heads[:, :total_width, :].reshape(
        local_samples, head_count, HEAD, cache_len
    )
    value_heads = pair_heads[:, total_width:, :].reshape(local_samples, head_count, HEAD, cache_len)
    scores = jnp.einsum(
        "shdq,shdk->shqk", queries, heads_of_keys, preferred_element_type=jnp.float32
    ) * HEAD ** (-0.5)
    local_lengths = lax.dynamic_slice_in_dim(my_lengths, my_column * local_samples, local_samples)
    visible = (
        jnp.arange(cache_len, dtype=jnp.int32)[None, None, None, :]
        < local_lengths[:, None, None, None]
    )
    scores = jnp.where(visible, scores, MASKED)
    row_peak = jnp.max(scores, axis=3, keepdims=True)
    exponent = jnp.exp(scores - row_peak)
    attention = (exponent / jnp.sum(exponent, axis=3, keepdims=True)).astype(jnp.bfloat16)
    attention = lax.optimization_barrier(attention)
    context = jnp.einsum(
        "shqk,shdk->sqhd", attention, value_heads, preferred_element_type=jnp.float32
    ).astype(jnp.bfloat16)
    attended = jnp.einsum(
        "sqc,ce->seq",
        context.reshape(local_samples, cell_count, total_width),
        full_weights[3],
        preferred_element_type=jnp.float32,
    ).astype(jnp.bfloat16)
    if fast:
        returned = xor_return_channels(attended, attended.shape[1] // mp_count)
    else:
        returned = lax.all_to_all(attended, "mp", split_axis=1, concat_axis=0, tiled=True)
    final_field = residual + returned.astype(jnp.float32)
    return final_field.astype(jnp.bfloat16)


def solution(mesh):
    in_specs = (
        P(("groups", "dp"), "mp", None),
        P(("groups", "dp"), None, "mp"),
        P("dp", None, "mp"),
        P("dp", None, "mp"),
        P(("groups", "dp"), "mp", None),
        P("dp", None),
        P("dp", None),
        P("groups"),
        P("groups"),
        P("groups"),
    )
    out_specs = P(("groups", "dp"), "mp", None)
    return jax.shard_map(local, mesh=mesh, in_specs=in_specs, out_specs=out_specs, check_vma=False)
```

```python
import jax
import jax.numpy as jnp
from jax import lax
from jax.sharding import PartitionSpec as P

C = 640
GROUPS = 32
HEAD = 64
SIDE = 8


EPSILON = 1e-05
MASKED = -1e30


def norm_groups(values, group_width):
    field_shape = values.shape
    grouped = values.reshape(
        field_shape[0], field_shape[1] // group_width, group_width, field_shape[2]
    )
    center = grouped - jnp.mean(grouped, axis=(2, 3), keepdims=True)
    spread = jnp.mean(center * center, axis=(2, 3), keepdims=True)
    return (center * lax.rsqrt(spread + EPSILON)).reshape(field_shape)


def gather_channels(field):
    return lax.all_gather(field, "mp", axis=1, tiled=True)


def pair_gather_channels(field):
    dense = field.reshape(-1, 128)
    across = lax.ppermute(dense, "mp", [(i, i ^ 2) for i in range(4)])
    beside = lax.ppermute(dense, "mp", [(i, i ^ 1) for i in range(4)])
    relayed = lax.ppermute(across, "mp", [(i, i ^ 1) for i in range(4)])
    parts = [part.reshape(field.shape) for part in (beside, across, relayed)]
    return jnp.concatenate([field] + parts, axis=1)


def line_gather_flat(flat, count):
    my_shard = lax.axis_index("dp")
    rightward = [(i, i + 1) for i in range(count - 1)]
    leftward = [(i + 1, i) for i in range(count - 1)]
    going_right, going_left = flat, flat
    held = [flat]
    from_left, from_right = [], []
    for _ in range(1, count):
        going_right = lax.ppermute(going_right, "dp", rightward)
        going_left = lax.ppermute(going_left, "dp", leftward)
        from_left.append(going_right)
        from_right.append(going_left)
    line = jnp.stack(from_left[::-1] + held + from_right)
    return lax.dynamic_slice_in_dim(line, count - 1 - my_shard, count, axis=0)


def split_line_gather(packed, gated):
    my_shard = lax.axis_index("dp")
    my_group = lax.axis_index("groups")
    halves = packed.reshape(2, packed.shape[0] // 2, packed.shape[1])
    mine = lax.dynamic_index_in_dim(halves, my_group, 0, keepdims=False)
    mine, gated = lax.optimization_barrier((mine, gated))
    rightward = [(i, i + 1) for i in range(3)]
    leftward = [(i + 1, i) for i in range(3)]
    swap = [(0, 1), (1, 0)]
    left_1 = lax.ppermute(mine, "dp", rightward)
    right_1 = lax.ppermute(mine, "dp", leftward)
    first_swap = lax.ppermute(jnp.where(my_shard >= 1, left_1, right_1), "groups", swap)
    left_2 = lax.ppermute(left_1, "dp", rightward)
    right_2 = lax.ppermute(right_1, "dp", leftward)
    second_swap = lax.ppermute(jnp.where(my_shard >= 2, left_2, right_2), "groups", swap)
    left_3 = lax.ppermute(left_2, "dp", rightward)
    right_3 = lax.ppermute(right_2, "dp", leftward)
    third_pick = jnp.where(my_shard == 0, right_3, jnp.where(my_shard == 3, left_3, right_1))
    third_swap = lax.ppermute(third_pick, "groups", swap)

    other_own = lax.dynamic_index_in_dim(halves, 1 - my_group, 0, keepdims=False)
    line = [
        (left_3, third_swap),
        (left_2, second_swap),
        (left_1, first_swap),
        (mine, other_own),
        (right_1, jnp.where(my_shard == 0, first_swap, third_swap)),
        (right_2, second_swap),
        (right_3, third_swap),
    ]
    natural = []
    for block in range(4):
        own_half, other_half = line[block + 3]
        for shard in range(1, 4):
            own_half = jnp.where(my_shard == shard, line[block + 3 - shard][0], own_half)
            other_half = jnp.where(my_shard == shard, line[block + 3 - shard][1], other_half)
        lead = jnp.where(my_group == 0, own_half, other_half)
        tail = jnp.where(my_group == 0, other_half, own_half)
        natural.append(jnp.concatenate([lead, tail], axis=0))
    return jnp.stack(natural), gated, (left_3, right_3)


def pair_gather_channel_minor(field):
    cell_major = jnp.transpose(field, (0, 2, 1))
    dense = cell_major.reshape(-1, 128)
    across = lax.ppermute(dense, "mp", [(i, i ^ 2) for i in range(4)])
    beside = lax.ppermute(dense, "mp", [(i, i ^ 1) for i in range(4)])
    relayed = lax.ppermute(across, "mp", [(i, i ^ 1) for i in range(4)])
    parts = [jnp.transpose(part.reshape(cell_major.shape), (0, 2, 1)) for part in (beside, across, relayed)]
    return jnp.concatenate([field] + parts, axis=1)


def xor_spread_samples(field, group):
    my_column = lax.axis_index("mp")
    parts = [lax.dynamic_slice_in_dim(field, my_column * group, group, axis=0)]
    for step in range(1, 4):
        block = lax.dynamic_slice_in_dim(field, (my_column ^ step) * group, group, axis=0)
        moved = lax.ppermute(block.reshape(-1, 128), "mp", [(i, i ^ step) for i in range(4)])
        parts.append(moved.reshape(block.shape))
    return jnp.concatenate(parts, axis=1)


def xor_return_channels(field, width):
    my_column = lax.axis_index("mp")
    parts = [lax.dynamic_slice_in_dim(field, my_column * width, width, axis=1)]
    for step in range(1, 4):
        block = lax.dynamic_slice_in_dim(field, (my_column ^ step) * width, width, axis=1)
        moved = lax.ppermute(block.reshape(-1, 128), "mp", [(i, i ^ step) for i in range(4)])
        parts.append(moved.reshape(block.shape))
    natural = []
    for block in range(4):
        picked = parts[block]
        for column in range(1, 4):
            picked = jnp.where(my_column == column, parts[block ^ column], picked)
        natural.append(picked)
    return jnp.concatenate(natural, axis=0)


def shift_parts(shard, count):
    parts = [shard]
    for step in range(1, count):
        parts.append(lax.ppermute(shard, "dp", [(i, (i + step) % count) for i in range(count)]))
    return jnp.stack(parts)


def order_rows(stacked, wanted_blocks):
    my_shard = lax.axis_index("dp")
    count = stacked.shape[0]
    picked = jnp.take(stacked, (my_shard - wanted_blocks) % count, axis=0, mode="clip")
    return picked.reshape((count * stacked.shape[1],) + stacked.shape[2:])


def gather_kernel(weight_shard):
    return lax.all_gather(weight_shard, "dp", axis=0, tiled=True)


def gather_projection(weight_shard):
    return lax.all_gather(weight_shard, "dp", axis=0, tiled=True)


def apply_kernel(full_field, kernel):
    sample_count = full_field.shape[0]
    out_width = kernel.shape[2]
    tap_images = jnp.einsum("scq,cte->stqe", full_field, kernel, preferred_element_type=jnp.float32)
    tap_images = tap_images.reshape(sample_count, 9, SIDE, SIDE, out_width)
    padded = jnp.pad(tap_images, ((0, 0), (0, 0), (1, 1), (1, 1), (0, 0)))
    running = padded[:, 0, 0:SIDE, 0:SIDE, :]
    for offset in range(1, 9):
        row_shift, col_shift = (offset // 3, offset % 3)
        running = (
            running
            + padded[:, offset, row_shift : row_shift + SIDE, col_shift : col_shift + SIDE, :]
        )
    return jnp.transpose(running.reshape(sample_count, SIDE * SIDE, out_width), (0, 2, 1))


def local(
    latents,
    modulation,
    first_kernel,
    second_kernel,
    encoder_cache,
    query_weight,
    output_weight,
    kept_prompt_list,
    destination,
    lengths,
):
    group_width = C // GROUPS
    dp_count = lax.axis_size("dp")
    mp_count = lax.axis_size("mp")
    my_shard = lax.axis_index("dp")
    my_column = lax.axis_index("mp")
    sample_shard_count = latents.shape[0]
    prompt_dev = encoder_cache.shape[0]
    cache_len = encoder_cache.shape[2]
    cache_width = encoder_cache.shape[1]
    cell_count = latents.shape[2]
    slot_limit = 2 * (sample_shard_count // dp_count)
    all_samples = destination.shape[0]
    owner_target = destination.reshape(dp_count, sample_shard_count)
    positions = jnp.arange(sample_shard_count, dtype=jnp.int32)
    before = positions[None, :] < positions[:, None]
    same_target = owner_target[:, :, None] == owner_target[:, None, :]
    slot_rank = jnp.sum((same_target & before[None]).astype(jnp.int32), axis=2)
    my_target = lax.dynamic_index_in_dim(owner_target, my_shard, 0, keepdims=False)
    my_rank = lax.dynamic_index_in_dim(slot_rank, my_shard, 0, keepdims=False)
    my_prompts = (
        lax.dynamic_slice_in_dim(
            kept_prompt_list, my_shard * sample_shard_count, sample_shard_count
        )
        - my_shard * prompt_dev
    )
    send_slot = my_target * slot_limit + my_rank
    slot_table = send_slot[:, None] == jnp.arange(dp_count * slot_limit, dtype=jnp.int32)[None, :]
    source_row = jnp.sum(jnp.where(slot_table, my_prompts[:, None], 0), axis=0)
    filled = jnp.any(slot_table, axis=0)
    send_rows = jnp.take(encoder_cache, source_row, axis=0)
    send_rows = jnp.where(filled[:, None, None], send_rows, jnp.zeros_like(send_rows))
    outgoing = send_rows.reshape(dp_count, slot_limit, cache_width, cache_len)
    arriving = destination == my_shard
    arrival_pos = jnp.cumsum(arriving.astype(jnp.int32)) - 1
    selector = arriving[None, :] & (arrival_pos[None, :] == positions[:, None])
    kept_prompt = jnp.sum(
        jnp.where(selector, jnp.arange(all_samples, dtype=jnp.int32)[None, :], 0), axis=1
    )
    incoming_order_rank = jnp.sum(jnp.where(selector, slot_rank.reshape(-1)[None, :], 0), axis=1)
    prompt_ids = jnp.sum(jnp.where(selector, kept_prompt_list[None, :], 0), axis=1)
    landing_slot = kept_prompt // sample_shard_count * slot_limit + incoming_order_rank
    prompt_hits = prompt_ids[:, None] == jnp.arange(lengths.shape[0], dtype=jnp.int32)[None, :]
    my_lengths = jnp.sum(jnp.where(prompt_hits, lengths[None, :], 0), axis=1)
    fast = dp_count == 4 and mp_count == 4 and lax.axis_size("groups") == 2
    weight_shards = (first_kernel, second_kernel, query_weight, output_weight)
    if fast:
        block_ids = jnp.arange(dp_count, dtype=jnp.int32)
        channel_blocks = jnp.bitwise_xor(block_ids, my_column)
        pieces = (first_kernel, second_kernel, query_weight, output_weight)
        dense = [piece.reshape(-1, 128) for piece in pieces]
        natural, latents, line_done = split_line_gather(jnp.concatenate(dense, axis=0), latents)
        kernel_rows = dense[0].shape[0] + dense[1].shape[0]
        def xor_order(blocks):
            ordered = []
            for position in range(dp_count):
                picked = blocks[position]
                for column in range(1, dp_count):
                    picked = jnp.where(my_column == column, blocks[position ^ column], picked)
                ordered.append(picked)
            return jnp.stack(ordered)

        kernel_part = xor_order(natural[:, :kernel_rows])
        proj_part = natural[:, kernel_rows:]
        full_weights = []
        cut = 0
        query_part = xor_order(proj_part)
        for piece, block, source in zip(pieces, dense, (kernel_part, kernel_part, query_part, proj_part)):
            if cut == kernel_rows:
                cut = 0
            chunk = source[:, cut : cut + block.shape[0]]
            cut += block.shape[0]
            full_weights.append(chunk.reshape((dp_count * piece.shape[0],) + piece.shape[1:]))
        gathered = (kernel_part, proj_part)
        full_weights = tuple(full_weights)
        outgoing = lax.optimization_barrier((outgoing, line_done))[0]
        spread_channels = pair_gather_channels
    else:
        full_weights = (
            gather_kernel(first_kernel),
            gather_kernel(second_kernel),
            gather_projection(query_weight),
            gather_projection(output_weight),
        )
        spread_channels = gather_channels
    incoming = lax.all_to_all(outgoing, "dp", split_axis=0, concat_axis=0, tiled=True)
    my_pairs = jnp.take(
        incoming.reshape(dp_count * slot_limit, cache_width, cache_len), landing_slot, axis=0
    )
    start_field = latents.astype(jnp.float32)
    activated = jax.nn.silu(norm_groups(start_field, group_width)).astype(jnp.bfloat16)
    first_in = spread_channels(activated)

    def convolve(full_field, which_weight):
        half = full_field.shape[0] // 2
        return jnp.concatenate(
            [
                apply_kernel(full_field[:half], full_weights[which_weight]),
                apply_kernel(full_field[half:], full_weights[which_weight]),
            ]
        )

    def project(field_rows, which_weight):
        full_weight = full_weights[which_weight]
        return jnp.einsum(
            "scq,ce->seq", field_rows, full_weight, preferred_element_type=jnp.float32
        )

    first_out = convolve(first_in, 0)
    scale_term = modulation[:, 0, :].astype(jnp.float32)[:, :, None]
    shift_term = modulation[:, 1, :].astype(jnp.float32)[:, :, None]
    modulated = jax.nn.silu(
        norm_groups(first_out, group_width) * (1.0 + scale_term) + shift_term
    ).astype(jnp.bfloat16)
    if fast:
        second_in = pair_gather_channel_minor(modulated)
    else:
        second_in = spread_channels(modulated)
    residual = start_field + convolve(second_in, 1)
    normed_out = norm_groups(residual, group_width).astype(jnp.bfloat16)
    local_samples = sample_shard_count // mp_count
    if fast:
        query_cells = xor_spread_samples(normed_out, local_samples)
        my_pairs = lax.optimization_barrier((my_pairs, query_cells))[0]
    else:
        query_cells = lax.all_to_all(normed_out, "mp", split_axis=0, concat_axis=1, tiled=True)
    pair_heads = lax.all_to_all(my_pairs, "mp", split_axis=0, concat_axis=1, tiled=True)
    total_width = query_cells.shape[1]
    head_count = total_width // HEAD
    queries = project(query_cells, 2).astype(jnp.bfloat16)
    queries = queries.reshape(local_samples, head_count, HEAD, cell_count)
    heads_of_keys = pair_heads[:, :total_width, :].reshape(
        local_samples, head_count, HEAD, cache_len
    )
    value_heads = pair_heads[:, total_width:, :].reshape(local_samples, head_count, HEAD, cache_len)
    scores = jnp.einsum(
        "shdq,shdk->shqk", queries, heads_of_keys, preferred_element_type=jnp.float32
    ) * HEAD ** (-0.5)
    local_lengths = lax.dynamic_slice_in_dim(my_lengths, my_column * local_samples, local_samples)
    visible = (
        jnp.arange(cache_len, dtype=jnp.int32)[None, None, None, :]
        < local_lengths[:, None, None, None]
    )
    scores = jnp.where(visible, scores, MASKED)
    row_peak = jnp.max(scores, axis=3, keepdims=True)
    exponent = jnp.exp(scores - row_peak)
    attention = (exponent / jnp.sum(exponent, axis=3, keepdims=True)).astype(jnp.bfloat16)
    attention = lax.optimization_barrier(attention)
    context = jnp.einsum(
        "shqk,shdk->sqhd", attention, value_heads, preferred_element_type=jnp.float32
    ).astype(jnp.bfloat16)
    attended = jnp.einsum(
        "sqc,ce->seq",
        context.reshape(local_samples, cell_count, total_width),
        full_weights[3],
        preferred_element_type=jnp.float32,
    ).astype(jnp.bfloat16)
    if fast:
        returned = xor_return_channels(attended, attended.shape[1] // mp_count)
    else:
        returned = lax.all_to_all(attended, "mp", split_axis=1, concat_axis=0, tiled=True)
    final_field = residual + returned.astype(jnp.float32)
    return final_field.astype(jnp.bfloat16)


def solution(mesh):
    in_specs = (
        P(("groups", "dp"), "mp", None),
        P(("groups", "dp"), None, "mp"),
        P("dp", None, "mp"),
        P("dp", None, "mp"),
        P(("groups", "dp"), "mp", None),
        P("dp", None),
        P("dp", None),
        P("groups"),
        P("groups"),
        P("groups"),
    )
    out_specs = P(("groups", "dp"), "mp", None)
    return jax.shard_map(local, mesh=mesh, in_specs=in_specs, out_specs=out_specs, check_vma=False)
```

```python
import jax
import jax.numpy as jnp
from jax import lax
from jax.sharding import PartitionSpec as P

C = 640
GROUPS = 32
HEAD = 64
SIDE = 8


EPSILON = 1e-05
MASKED = -1e30


def norm_groups(values, group_width):
    field_shape = values.shape
    grouped = values.reshape(
        field_shape[0], field_shape[1] // group_width, group_width, field_shape[2]
    )
    center = grouped - jnp.mean(grouped, axis=(2, 3), keepdims=True)
    spread = jnp.mean(center * center, axis=(2, 3), keepdims=True)
    return (center * lax.rsqrt(spread + EPSILON)).reshape(field_shape)


def gather_channels(field):
    return lax.all_gather(field, "mp", axis=1, tiled=True)


def pair_gather_channels(field):
    dense = field.reshape(-1, 128)
    across = lax.ppermute(dense, "mp", [(i, i ^ 2) for i in range(4)])
    beside = lax.ppermute(dense, "mp", [(i, i ^ 1) for i in range(4)])
    relayed = lax.ppermute(across, "mp", [(i, i ^ 1) for i in range(4)])
    parts = [part.reshape(field.shape) for part in (beside, across, relayed)]
    return jnp.concatenate([field] + parts, axis=1)


def line_gather_flat(flat, count):
    my_shard = lax.axis_index("dp")
    rightward = [(i, i + 1) for i in range(count - 1)]
    leftward = [(i + 1, i) for i in range(count - 1)]
    going_right, going_left = flat, flat
    held = [flat]
    from_left, from_right = [], []
    for _ in range(1, count):
        going_right = lax.ppermute(going_right, "dp", rightward)
        going_left = lax.ppermute(going_left, "dp", leftward)
        from_left.append(going_right)
        from_right.append(going_left)
    line = jnp.stack(from_left[::-1] + held + from_right)
    return lax.dynamic_slice_in_dim(line, count - 1 - my_shard, count, axis=0)


def split_line_gather(packed, gated):
    my_shard = lax.axis_index("dp")
    my_group = lax.axis_index("groups")
    halves = packed.reshape(2, packed.shape[0] // 2, packed.shape[1])
    mine = lax.dynamic_index_in_dim(halves, my_group, 0, keepdims=False)
    mine, gated = lax.optimization_barrier((mine, gated))
    rightward = [(i, i + 1) for i in range(3)]
    leftward = [(i + 1, i) for i in range(3)]
    swap = [(0, 1), (1, 0)]
    left_1 = lax.ppermute(mine, "dp", rightward)
    right_1 = lax.ppermute(mine, "dp", leftward)
    first_swap = lax.ppermute(jnp.where(my_shard >= 1, left_1, right_1), "groups", swap)
    left_2 = lax.ppermute(left_1, "dp", rightward)
    right_2 = lax.ppermute(right_1, "dp", leftward)
    second_swap = lax.ppermute(jnp.where(my_shard >= 2, left_2, right_2), "groups", swap)
    left_3 = lax.ppermute(left_2, "dp", rightward)
    right_3 = lax.ppermute(right_2, "dp", leftward)
    third_pick = jnp.where(my_shard == 0, right_3, jnp.where(my_shard == 3, left_3, right_1))
    third_swap = lax.ppermute(third_pick, "groups", swap)

    other_own = lax.dynamic_index_in_dim(halves, 1 - my_group, 0, keepdims=False)
    line = [
        (left_3, third_swap),
        (left_2, second_swap),
        (left_1, first_swap),
        (mine, other_own),
        (right_1, jnp.where(my_shard == 0, first_swap, third_swap)),
        (right_2, second_swap),
        (right_3, third_swap),
    ]
    natural = []
    for block in range(4):
        own_half, other_half = line[block + 3]
        for shard in range(1, 4):
            own_half = jnp.where(my_shard == shard, line[block + 3 - shard][0], own_half)
            other_half = jnp.where(my_shard == shard, line[block + 3 - shard][1], other_half)
        lead = jnp.where(my_group == 0, own_half, other_half)
        tail = jnp.where(my_group == 0, other_half, own_half)
        natural.append(jnp.concatenate([lead, tail], axis=0))
    return jnp.stack(natural), gated, (left_3, right_3)


def pair_gather_channel_minor(field):
    cell_major = jnp.transpose(field, (0, 2, 1))
    dense = cell_major.reshape(-1, 128)
    across = lax.ppermute(dense, "mp", [(i, i ^ 2) for i in range(4)])
    beside = lax.ppermute(dense, "mp", [(i, i ^ 1) for i in range(4)])
    relayed = lax.ppermute(across, "mp", [(i, i ^ 1) for i in range(4)])
    parts = [jnp.transpose(part.reshape(cell_major.shape), (0, 2, 1)) for part in (beside, across, relayed)]
    return jnp.concatenate([field] + parts, axis=1)


def xor_spread_samples(field, group):
    my_column = lax.axis_index("mp")
    parts = [lax.dynamic_slice_in_dim(field, my_column * group, group, axis=0)]
    for step in range(1, 4):
        block = lax.dynamic_slice_in_dim(field, (my_column ^ step) * group, group, axis=0)
        moved = lax.ppermute(block.reshape(-1, 128), "mp", [(i, i ^ step) for i in range(4)])
        parts.append(moved.reshape(block.shape))
    return jnp.concatenate(parts, axis=1)


def xor_return_channels(field, width):
    my_column = lax.axis_index("mp")
    parts = [lax.dynamic_slice_in_dim(field, my_column * width, width, axis=1)]
    for step in range(1, 4):
        block = lax.dynamic_slice_in_dim(field, (my_column ^ step) * width, width, axis=1)
        moved = lax.ppermute(block.reshape(-1, 128), "mp", [(i, i ^ step) for i in range(4)])
        parts.append(moved.reshape(block.shape))
    natural = []
    for block in range(4):
        picked = parts[block]
        for column in range(1, 4):
            picked = jnp.where(my_column == column, parts[block ^ column], picked)
        natural.append(picked)
    return jnp.concatenate(natural, axis=0)


def shift_parts(shard, count):
    parts = [shard]
    for step in range(1, count):
        parts.append(lax.ppermute(shard, "dp", [(i, (i + step) % count) for i in range(count)]))
    return jnp.stack(parts)


def order_rows(stacked, wanted_blocks):
    my_shard = lax.axis_index("dp")
    count = stacked.shape[0]
    picked = jnp.take(stacked, (my_shard - wanted_blocks) % count, axis=0, mode="clip")
    return picked.reshape((count * stacked.shape[1],) + stacked.shape[2:])


def gather_kernel(weight_shard):
    return lax.all_gather(weight_shard, "dp", axis=0, tiled=True)


def gather_projection(weight_shard):
    return lax.all_gather(weight_shard, "dp", axis=0, tiled=True)


def apply_kernel(full_field, kernel):
    sample_count = full_field.shape[0]
    out_width = kernel.shape[2]
    tap_images = jnp.einsum("scq,cte->stqe", full_field, kernel, preferred_element_type=jnp.float32)
    tap_images = tap_images.reshape(sample_count, 9, SIDE, SIDE, out_width)
    padded = jnp.pad(tap_images, ((0, 0), (0, 0), (1, 1), (1, 1), (0, 0)))
    running = padded[:, 0, 0:SIDE, 0:SIDE, :]
    for offset in range(1, 9):
        row_shift, col_shift = (offset // 3, offset % 3)
        running = (
            running
            + padded[:, offset, row_shift : row_shift + SIDE, col_shift : col_shift + SIDE, :]
        )
    return jnp.transpose(running.reshape(sample_count, SIDE * SIDE, out_width), (0, 2, 1))


def local(
    latents,
    modulation,
    first_kernel,
    second_kernel,
    encoder_cache,
    query_weight,
    output_weight,
    kept_prompt_list,
    destination,
    lengths,
):
    group_width = C // GROUPS
    dp_count = lax.axis_size("dp")
    mp_count = lax.axis_size("mp")
    my_shard = lax.axis_index("dp")
    my_column = lax.axis_index("mp")
    sample_shard_count = latents.shape[0]
    prompt_dev = encoder_cache.shape[0]
    cache_len = encoder_cache.shape[2]
    cache_width = encoder_cache.shape[1]
    cell_count = latents.shape[2]
    slot_limit = 2 * (sample_shard_count // dp_count)
    all_samples = destination.shape[0]
    owner_target = destination.reshape(dp_count, sample_shard_count)
    positions = jnp.arange(sample_shard_count, dtype=jnp.int32)
    before = positions[None, :] < positions[:, None]
    same_target = owner_target[:, :, None] == owner_target[:, None, :]
    slot_rank = jnp.sum((same_target & before[None]).astype(jnp.int32), axis=2)
    my_target = lax.dynamic_index_in_dim(owner_target, my_shard, 0, keepdims=False)
    my_rank = lax.dynamic_index_in_dim(slot_rank, my_shard, 0, keepdims=False)
    my_prompts = (
        lax.dynamic_slice_in_dim(
            kept_prompt_list, my_shard * sample_shard_count, sample_shard_count
        )
        - my_shard * prompt_dev
    )
    send_slot = my_target * slot_limit + my_rank
    slot_table = send_slot[:, None] == jnp.arange(dp_count * slot_limit, dtype=jnp.int32)[None, :]
    source_row = jnp.sum(jnp.where(slot_table, my_prompts[:, None], 0), axis=0)
    filled = jnp.any(slot_table, axis=0)
    send_rows = jnp.take(encoder_cache, source_row, axis=0)
    send_rows = jnp.where(filled[:, None, None], send_rows, jnp.zeros_like(send_rows))
    outgoing = send_rows.reshape(dp_count, slot_limit, cache_width, cache_len)
    arriving = destination == my_shard
    arrival_pos = jnp.cumsum(arriving.astype(jnp.int32)) - 1
    selector = arriving[None, :] & (arrival_pos[None, :] == positions[:, None])
    kept_prompt = jnp.sum(
        jnp.where(selector, jnp.arange(all_samples, dtype=jnp.int32)[None, :], 0), axis=1
    )
    incoming_order_rank = jnp.sum(jnp.where(selector, slot_rank.reshape(-1)[None, :], 0), axis=1)
    prompt_ids = jnp.sum(jnp.where(selector, kept_prompt_list[None, :], 0), axis=1)
    landing_slot = kept_prompt // sample_shard_count * slot_limit + incoming_order_rank
    prompt_hits = prompt_ids[:, None] == jnp.arange(lengths.shape[0], dtype=jnp.int32)[None, :]
    my_lengths = jnp.sum(jnp.where(prompt_hits, lengths[None, :], 0), axis=1)
    fast = dp_count == 4 and mp_count == 4 and lax.axis_size("groups") == 2
    weight_shards = (first_kernel, second_kernel, query_weight, output_weight)
    if fast:
        block_ids = jnp.arange(dp_count, dtype=jnp.int32)
        channel_blocks = jnp.bitwise_xor(block_ids, my_column)
        pieces = (first_kernel, second_kernel, query_weight, output_weight)
        dense = [piece.reshape(-1, 128) for piece in pieces]
        natural, latents, line_done = split_line_gather(jnp.concatenate(dense, axis=0), latents)
        kernel_rows = dense[0].shape[0] + dense[1].shape[0]
        def xor_order(blocks):
            ordered = []
            for position in range(dp_count):
                picked = blocks[position]
                for column in range(1, dp_count):
                    picked = jnp.where(my_column == column, blocks[position ^ column], picked)
                ordered.append(picked)
            return jnp.stack(ordered)

        kernel_part = xor_order(natural[:, :kernel_rows])
        proj_part = natural[:, kernel_rows:]
        full_weights = []
        cut = 0
        query_part = xor_order(proj_part)
        for piece, block, source in zip(pieces, dense, (kernel_part, kernel_part, query_part, proj_part)):
            if cut == kernel_rows:
                cut = 0
            chunk = source[:, cut : cut + block.shape[0]]
            cut += block.shape[0]
            full_weights.append(chunk.reshape((dp_count * piece.shape[0],) + piece.shape[1:]))
        gathered = (kernel_part, proj_part)
        full_weights = tuple(full_weights)
        outgoing = lax.optimization_barrier((outgoing, line_done))[0]
        spread_channels = pair_gather_channels
    else:
        full_weights = (
            gather_kernel(first_kernel),
            gather_kernel(second_kernel),
            gather_projection(query_weight),
            gather_projection(output_weight),
        )
        spread_channels = gather_channels
    incoming = lax.all_to_all(outgoing, "dp", split_axis=0, concat_axis=0, tiled=True)
    my_pairs = jnp.take(
        incoming.reshape(dp_count * slot_limit, cache_width, cache_len), landing_slot, axis=0
    )
    start_field = latents.astype(jnp.float32)
    activated = jax.nn.silu(norm_groups(start_field, group_width)).astype(jnp.bfloat16)
    first_in = spread_channels(activated)

    def convolve(full_field, which_weight):
        half = full_field.shape[0] // 2
        return jnp.concatenate(
            [
                apply_kernel(full_field[:half], full_weights[which_weight]),
                apply_kernel(full_field[half:], full_weights[which_weight]),
            ]
        )

    def project(field_rows, which_weight):
        full_weight = full_weights[which_weight]
        return jnp.einsum(
            "scq,ce->seq", field_rows, full_weight, preferred_element_type=jnp.float32
        )

    first_out = convolve(first_in, 0)
    scale_term = modulation[:, 0, :].astype(jnp.float32)[:, :, None]
    shift_term = modulation[:, 1, :].astype(jnp.float32)[:, :, None]
    modulated = jax.nn.silu(
        norm_groups(first_out, group_width) * (1.0 + scale_term) + shift_term
    ).astype(jnp.bfloat16)
    if fast:
        second_in = pair_gather_channel_minor(modulated)
    else:
        second_in = spread_channels(modulated)
    residual = start_field + convolve(second_in, 1)
    normed_out = norm_groups(residual, group_width).astype(jnp.bfloat16)
    local_samples = sample_shard_count // mp_count
    if fast:
        query_cells = xor_spread_samples(normed_out, local_samples)
    else:
        query_cells = lax.all_to_all(normed_out, "mp", split_axis=0, concat_axis=1, tiled=True)
    pair_heads = lax.all_to_all(my_pairs, "mp", split_axis=0, concat_axis=1, tiled=True)
    total_width = query_cells.shape[1]
    head_count = total_width // HEAD
    queries = project(query_cells, 2).astype(jnp.bfloat16)
    queries = queries.reshape(local_samples, head_count, HEAD, cell_count)
    heads_of_keys = pair_heads[:, :total_width, :].reshape(
        local_samples, head_count, HEAD, cache_len
    )
    value_heads = pair_heads[:, total_width:, :].reshape(local_samples, head_count, HEAD, cache_len)
    scores = jnp.einsum(
        "shdq,shdk->shqk", queries, heads_of_keys, preferred_element_type=jnp.float32
    ) * HEAD ** (-0.5)
    local_lengths = lax.dynamic_slice_in_dim(my_lengths, my_column * local_samples, local_samples)
    visible = (
        jnp.arange(cache_len, dtype=jnp.int32)[None, None, None, :]
        < local_lengths[:, None, None, None]
    )
    scores = jnp.where(visible, scores, MASKED)
    row_peak = jnp.max(scores, axis=3, keepdims=True)
    exponent = jnp.exp(scores - row_peak)
    attention = (exponent / jnp.sum(exponent, axis=3, keepdims=True)).astype(jnp.bfloat16)
    attention = lax.optimization_barrier(attention)
    context = jnp.einsum(
        "shqk,shdk->sqhd", attention, value_heads, preferred_element_type=jnp.float32
    ).astype(jnp.bfloat16)
    attended = jnp.einsum(
        "sqc,ce->seq",
        context.reshape(local_samples, cell_count, total_width),
        full_weights[3],
        preferred_element_type=jnp.float32,
    ).astype(jnp.bfloat16)
    if fast:
        returned = xor_return_channels(attended, attended.shape[1] // mp_count)
    else:
        returned = lax.all_to_all(attended, "mp", split_axis=1, concat_axis=0, tiled=True)
    final_field = residual + returned.astype(jnp.float32)
    return final_field.astype(jnp.bfloat16)


def solution(mesh):
    in_specs = (
        P(("groups", "dp"), "mp", None),
        P(("groups", "dp"), None, "mp"),
        P("dp", None, "mp"),
        P("dp", None, "mp"),
        P(("groups", "dp"), "mp", None),
        P("dp", None),
        P("dp", None),
        P("groups"),
        P("groups"),
        P("groups"),
    )
    out_specs = P(("groups", "dp"), "mp", None)
    return jax.shard_map(local, mesh=mesh, in_specs=in_specs, out_specs=out_specs, check_vma=False)
```

```python
import jax
import jax.numpy as jnp
from jax import lax
from jax.sharding import PartitionSpec as P

C = 640
GROUPS = 32
HEAD = 64
SIDE = 8


EPSILON = 1e-05
MASKED = -1e30


def norm_groups(values, group_width):
    field_shape = values.shape
    grouped = values.reshape(
        field_shape[0], field_shape[1] // group_width, group_width, field_shape[2]
    )
    center = grouped - jnp.mean(grouped, axis=(2, 3), keepdims=True)
    spread = jnp.mean(center * center, axis=(2, 3), keepdims=True)
    return (center * lax.rsqrt(spread + EPSILON)).reshape(field_shape)


def gather_channels(field):
    return lax.all_gather(field, "mp", axis=1, tiled=True)


def pair_gather_channels(field):
    dense = field.reshape(-1, 128)
    across = lax.ppermute(dense, "mp", [(i, i ^ 2) for i in range(4)])
    beside = lax.ppermute(dense, "mp", [(i, i ^ 1) for i in range(4)])
    relayed = lax.ppermute(across, "mp", [(i, i ^ 1) for i in range(4)])
    parts = [part.reshape(field.shape) for part in (beside, across, relayed)]
    return jnp.concatenate([field] + parts, axis=1)


def line_gather_flat(flat, count):
    my_shard = lax.axis_index("dp")
    rightward = [(i, i + 1) for i in range(count - 1)]
    leftward = [(i + 1, i) for i in range(count - 1)]
    going_right, going_left = flat, flat
    held = [flat]
    from_left, from_right = [], []
    for _ in range(1, count):
        going_right = lax.ppermute(going_right, "dp", rightward)
        going_left = lax.ppermute(going_left, "dp", leftward)
        from_left.append(going_right)
        from_right.append(going_left)
    line = jnp.stack(from_left[::-1] + held + from_right)
    return lax.dynamic_slice_in_dim(line, count - 1 - my_shard, count, axis=0)


def split_line_gather(packed, gated):
    my_shard = lax.axis_index("dp")
    my_group = lax.axis_index("groups")
    halves = packed.reshape(2, packed.shape[0] // 2, packed.shape[1])
    mine = lax.dynamic_index_in_dim(halves, my_group, 0, keepdims=False)
    mine, gated = lax.optimization_barrier((mine, gated))
    rightward = [(i, i + 1) for i in range(3)]
    leftward = [(i + 1, i) for i in range(3)]
    swap = [(0, 1), (1, 0)]
    left_1 = lax.ppermute(mine, "dp", rightward)
    right_1 = lax.ppermute(mine, "dp", leftward)
    first_swap = lax.ppermute(jnp.where(my_shard >= 1, left_1, right_1), "groups", swap)
    left_2 = lax.ppermute(left_1, "dp", rightward)
    right_2 = lax.ppermute(right_1, "dp", leftward)
    second_swap = lax.ppermute(jnp.where(my_shard >= 2, left_2, right_2), "groups", swap)
    left_3 = lax.ppermute(left_2, "dp", rightward)
    right_3 = lax.ppermute(right_2, "dp", leftward)
    third_pick = jnp.where(my_shard == 0, right_3, jnp.where(my_shard == 3, left_3, right_1))
    third_swap = lax.ppermute(third_pick, "groups", swap)

    other_own = lax.dynamic_index_in_dim(halves, 1 - my_group, 0, keepdims=False)
    line = [
        (left_3, third_swap),
        (left_2, second_swap),
        (left_1, first_swap),
        (mine, other_own),
        (right_1, jnp.where(my_shard == 0, first_swap, third_swap)),
        (right_2, second_swap),
        (right_3, third_swap),
    ]
    natural = []
    for block in range(4):
        own_half, other_half = line[block + 3]
        for shard in range(1, 4):
            own_half = jnp.where(my_shard == shard, line[block + 3 - shard][0], own_half)
            other_half = jnp.where(my_shard == shard, line[block + 3 - shard][1], other_half)
        lead = jnp.where(my_group == 0, own_half, other_half)
        tail = jnp.where(my_group == 0, other_half, own_half)
        natural.append(jnp.concatenate([lead, tail], axis=0))
    return jnp.stack(natural), gated, (left_3, right_3)


def pair_gather_channel_minor(field):
    cell_major = jnp.transpose(field, (0, 2, 1))
    dense = cell_major.reshape(-1, 128)
    across = lax.ppermute(dense, "mp", [(i, i ^ 2) for i in range(4)])
    beside = lax.ppermute(dense, "mp", [(i, i ^ 1) for i in range(4)])
    relayed = lax.ppermute(across, "mp", [(i, i ^ 1) for i in range(4)])
    parts = [jnp.transpose(part.reshape(cell_major.shape), (0, 2, 1)) for part in (beside, across, relayed)]
    return jnp.concatenate([field] + parts, axis=1)


def xor_spread_samples(field, group):
    my_column = lax.axis_index("mp")
    parts = [lax.dynamic_slice_in_dim(field, my_column * group, group, axis=0)]
    for step in range(1, 4):
        block = lax.dynamic_slice_in_dim(field, (my_column ^ step) * group, group, axis=0)
        moved = lax.ppermute(block.reshape(-1, 128), "mp", [(i, i ^ step) for i in range(4)])
        parts.append(moved.reshape(block.shape))
    return jnp.concatenate(parts, axis=1)


def xor_return_channels(field, width):
    my_column = lax.axis_index("mp")
    parts = [lax.dynamic_slice_in_dim(field, my_column * width, width, axis=1)]
    for step in range(1, 4):
        block = lax.dynamic_slice_in_dim(field, (my_column ^ step) * width, width, axis=1)
        moved = lax.ppermute(block.reshape(-1, 128), "mp", [(i, i ^ step) for i in range(4)])
        parts.append(moved.reshape(block.shape))
    natural = []
    for block in range(4):
        picked = parts[block]
        for column in range(1, 4):
            picked = jnp.where(my_column == column, parts[block ^ column], picked)
        natural.append(picked)
    return jnp.concatenate(natural, axis=0)


def shift_parts(shard, count):
    parts = [shard]
    for step in range(1, count):
        parts.append(lax.ppermute(shard, "dp", [(i, (i + step) % count) for i in range(count)]))
    return jnp.stack(parts)


def order_rows(stacked, wanted_blocks):
    my_shard = lax.axis_index("dp")
    count = stacked.shape[0]
    picked = jnp.take(stacked, (my_shard - wanted_blocks) % count, axis=0, mode="clip")
    return picked.reshape((count * stacked.shape[1],) + stacked.shape[2:])


def gather_kernel(weight_shard):
    return lax.all_gather(weight_shard, "dp", axis=0, tiled=True)


def gather_projection(weight_shard):
    return lax.all_gather(weight_shard, "dp", axis=0, tiled=True)


def apply_kernel(full_field, kernel):
    sample_count = full_field.shape[0]
    out_width = kernel.shape[2]
    tap_images = jnp.einsum("scq,cte->stqe", full_field, kernel, preferred_element_type=jnp.float32)
    tap_images = tap_images.reshape(sample_count, 9, SIDE, SIDE, out_width)
    padded = jnp.pad(tap_images, ((0, 0), (0, 0), (1, 1), (1, 1), (0, 0)))
    running = padded[:, 0, 0:SIDE, 0:SIDE, :]
    for offset in range(1, 9):
        row_shift, col_shift = (offset // 3, offset % 3)
        running = (
            running
            + padded[:, offset, row_shift : row_shift + SIDE, col_shift : col_shift + SIDE, :]
        )
    return jnp.transpose(running.reshape(sample_count, SIDE * SIDE, out_width), (0, 2, 1))


def local(
    latents,
    modulation,
    first_kernel,
    second_kernel,
    encoder_cache,
    query_weight,
    output_weight,
    kept_prompt_list,
    destination,
    lengths,
):
    group_width = C // GROUPS
    dp_count = lax.axis_size("dp")
    mp_count = lax.axis_size("mp")
    my_shard = lax.axis_index("dp")
    my_column = lax.axis_index("mp")
    sample_shard_count = latents.shape[0]
    prompt_dev = encoder_cache.shape[0]
    cache_len = encoder_cache.shape[2]
    cache_width = encoder_cache.shape[1]
    cell_count = latents.shape[2]
    slot_limit = 2 * (sample_shard_count // dp_count)
    all_samples = destination.shape[0]
    owner_target = destination.reshape(dp_count, sample_shard_count)
    positions = jnp.arange(sample_shard_count, dtype=jnp.int32)
    before = positions[None, :] < positions[:, None]
    same_target = owner_target[:, :, None] == owner_target[:, None, :]
    slot_rank = jnp.sum((same_target & before[None]).astype(jnp.int32), axis=2)
    my_target = lax.dynamic_index_in_dim(owner_target, my_shard, 0, keepdims=False)
    my_rank = lax.dynamic_index_in_dim(slot_rank, my_shard, 0, keepdims=False)
    my_prompts = (
        lax.dynamic_slice_in_dim(
            kept_prompt_list, my_shard * sample_shard_count, sample_shard_count
        )
        - my_shard * prompt_dev
    )
    send_slot = my_target * slot_limit + my_rank
    slot_table = send_slot[:, None] == jnp.arange(dp_count * slot_limit, dtype=jnp.int32)[None, :]
    source_row = jnp.sum(jnp.where(slot_table, my_prompts[:, None], 0), axis=0)
    filled = jnp.any(slot_table, axis=0)
    send_rows = jnp.take(encoder_cache, source_row, axis=0)
    send_rows = jnp.where(filled[:, None, None], send_rows, jnp.zeros_like(send_rows))
    outgoing = send_rows.reshape(dp_count, slot_limit, cache_width, cache_len)
    arriving = destination == my_shard
    arrival_pos = jnp.cumsum(arriving.astype(jnp.int32)) - 1
    selector = arriving[None, :] & (arrival_pos[None, :] == positions[:, None])
    kept_prompt = jnp.sum(
        jnp.where(selector, jnp.arange(all_samples, dtype=jnp.int32)[None, :], 0), axis=1
    )
    incoming_order_rank = jnp.sum(jnp.where(selector, slot_rank.reshape(-1)[None, :], 0), axis=1)
    prompt_ids = jnp.sum(jnp.where(selector, kept_prompt_list[None, :], 0), axis=1)
    landing_slot = kept_prompt // sample_shard_count * slot_limit + incoming_order_rank
    prompt_hits = prompt_ids[:, None] == jnp.arange(lengths.shape[0], dtype=jnp.int32)[None, :]
    my_lengths = jnp.sum(jnp.where(prompt_hits, lengths[None, :], 0), axis=1)
    fast = dp_count == 4 and mp_count == 4 and lax.axis_size("groups") == 2
    weight_shards = (first_kernel, second_kernel, query_weight, output_weight)
    if fast:
        block_ids = jnp.arange(dp_count, dtype=jnp.int32)
        channel_blocks = jnp.bitwise_xor(block_ids, my_column)
        pieces = (first_kernel, second_kernel, query_weight, output_weight)
        dense = [piece.reshape(-1, 128) for piece in pieces]
        natural, latents, line_done = split_line_gather(jnp.concatenate(dense, axis=0), latents)
        kernel_rows = dense[0].shape[0] + dense[1].shape[0]
        def xor_order(blocks):
            ordered = []
            for position in range(dp_count):
                picked = blocks[position]
                for column in range(1, dp_count):
                    picked = jnp.where(my_column == column, blocks[position ^ column], picked)
                ordered.append(picked)
            return jnp.stack(ordered)

        kernel_part = xor_order(natural[:, :kernel_rows])
        proj_part = natural[:, kernel_rows:]
        full_weights = []
        cut = 0
        query_part = xor_order(proj_part)
        for piece, block, source in zip(pieces, dense, (kernel_part, kernel_part, query_part, proj_part)):
            if cut == kernel_rows:
                cut = 0
            chunk = source[:, cut : cut + block.shape[0]]
            cut += block.shape[0]
            full_weights.append(chunk.reshape((dp_count * piece.shape[0],) + piece.shape[1:]))
        gathered = (kernel_part, proj_part)
        full_weights = tuple(full_weights)
        outgoing = lax.optimization_barrier((outgoing, line_done))[0]
        spread_channels = pair_gather_channels
    else:
        full_weights = (
            gather_kernel(first_kernel),
            gather_kernel(second_kernel),
            gather_projection(query_weight),
            gather_projection(output_weight),
        )
        spread_channels = gather_channels
    incoming = lax.all_to_all(outgoing, "dp", split_axis=0, concat_axis=0, tiled=True)
    my_pairs = jnp.take(
        incoming.reshape(dp_count * slot_limit, cache_width, cache_len), landing_slot, axis=0
    )
    start_field = latents.astype(jnp.float32)
    activated = jax.nn.silu(norm_groups(start_field, group_width)).astype(jnp.bfloat16)
    first_in = spread_channels(activated)

    def convolve(full_field, which_weight):
        kernel = full_weights[which_weight]
        half = kernel.shape[2] // 2
        return jnp.concatenate(
            [
                apply_kernel(full_field, kernel[:, :, :half]),
                apply_kernel(full_field, kernel[:, :, half:]),
            ],
            axis=1,
        )

    def project(field_rows, which_weight):
        full_weight = full_weights[which_weight]
        return jnp.einsum(
            "scq,ce->seq", field_rows, full_weight, preferred_element_type=jnp.float32
        )

    first_out = convolve(first_in, 0)
    scale_term = modulation[:, 0, :].astype(jnp.float32)[:, :, None]
    shift_term = modulation[:, 1, :].astype(jnp.float32)[:, :, None]
    modulated = jax.nn.silu(
        norm_groups(first_out, group_width) * (1.0 + scale_term) + shift_term
    ).astype(jnp.bfloat16)
    if fast:
        second_in = pair_gather_channel_minor(modulated)
    else:
        second_in = spread_channels(modulated)
    residual = start_field + convolve(second_in, 1)
    normed_out = norm_groups(residual, group_width).astype(jnp.bfloat16)
    local_samples = sample_shard_count // mp_count
    if fast:
        query_cells = xor_spread_samples(normed_out, local_samples)
        my_pairs = lax.optimization_barrier((my_pairs, query_cells))[0]
    else:
        query_cells = lax.all_to_all(normed_out, "mp", split_axis=0, concat_axis=1, tiled=True)
    pair_heads = lax.all_to_all(my_pairs, "mp", split_axis=0, concat_axis=1, tiled=True)
    total_width = query_cells.shape[1]
    head_count = total_width // HEAD
    queries = project(query_cells, 2).astype(jnp.bfloat16)
    queries = queries.reshape(local_samples, head_count, HEAD, cell_count)
    heads_of_keys = pair_heads[:, :total_width, :].reshape(
        local_samples, head_count, HEAD, cache_len
    )
    value_heads = pair_heads[:, total_width:, :].reshape(local_samples, head_count, HEAD, cache_len)
    scores = jnp.einsum(
        "shdq,shdk->shqk", queries, heads_of_keys, preferred_element_type=jnp.float32
    ) * HEAD ** (-0.5)
    local_lengths = lax.dynamic_slice_in_dim(my_lengths, my_column * local_samples, local_samples)
    visible = (
        jnp.arange(cache_len, dtype=jnp.int32)[None, None, None, :]
        < local_lengths[:, None, None, None]
    )
    scores = jnp.where(visible, scores, MASKED)
    row_peak = jnp.max(scores, axis=3, keepdims=True)
    exponent = jnp.exp(scores - row_peak)
    attention = (exponent / jnp.sum(exponent, axis=3, keepdims=True)).astype(jnp.bfloat16)
    attention = lax.optimization_barrier(attention)
    context = jnp.einsum(
        "shqk,shdk->sqhd", attention, value_heads, preferred_element_type=jnp.float32
    ).astype(jnp.bfloat16)
    attended = jnp.einsum(
        "sqc,ce->seq",
        context.reshape(local_samples, cell_count, total_width),
        full_weights[3],
        preferred_element_type=jnp.float32,
    ).astype(jnp.bfloat16)
    if fast:
        returned = xor_return_channels(attended, attended.shape[1] // mp_count)
    else:
        returned = lax.all_to_all(attended, "mp", split_axis=1, concat_axis=0, tiled=True)
    final_field = residual + returned.astype(jnp.float32)
    return final_field.astype(jnp.bfloat16)


def solution(mesh):
    in_specs = (
        P(("groups", "dp"), "mp", None),
        P(("groups", "dp"), None, "mp"),
        P("dp", None, "mp"),
        P("dp", None, "mp"),
        P(("groups", "dp"), "mp", None),
        P("dp", None),
        P("dp", None),
        P("groups"),
        P("groups"),
        P("groups"),
    )
    out_specs = P(("groups", "dp"), "mp", None)
    return jax.shard_map(local, mesh=mesh, in_specs=in_specs, out_specs=out_specs, check_vma=False)
```
